512 devices in a mesh: blk: 32 (over y, z_hi), kv: 16 (over z_lo, x, core).
Axes of the slice: x: 4, y: 8, z: 8 (z_hi: 4, z_lo: 2; z = z_hi * 2 + z_lo), core: 2. Of those that a mesh axis runs over, the one named last changes fastest.
Arguments:
- cache_entries: bfloat16 [65536, 8, 256], P(('kv', 'blk'))
- recompute_input: bfloat16 [4096, 4096], P('kv', 'blk'), may hold values from -6 to 6
- norm_gain: bfloat16 [4096], replicated, may hold values from 0.099609375 to 1.8984375
- w_query: bfloat16 [4096, 4096], P(None, 'blk'), may hold values from -0.25 to 0.25
- w_keyval: bfloat16 [4096, 2048], P('blk'), may hold values from -0.09375 to 0.09375
- w_out: bfloat16 [4096, 4096], P('blk'), may hold values from -0.09375 to 0.09375
- rotate_offsets: int32 [64], replicated, may hold values from 0 to 65535
- span_order: int32 [64], replicated, may hold values from 0 to 63, as said below
- tenant_of_span: int32 [64], replicated, may hold values from 0 to 3, never falling along the last dimension, each value on 1 to 32 neighbouring positions
- recompute_pos: int32 [4096], replicated, may hold values from 0 to 4095, as said below
- recompute_count: int32 [16], replicated, may hold values from 1 to 256, as said below
Outputs:
- attention_out: bfloat16 [4096, 4096], P('kv', 'blk')
The draws below stay inside these ranges and needn't reach their ends.
Inputs may be any that keep to these rules, and one draw needn't show every extreme that they name: `span_order`: each aligned block of 4 entries is a permutation of the block slots of that same block. `tenant_of_span`: tenants never fall along the block slots; there are 4 tenants, one of exactly 32 blocks. `recompute_pos`: the 256 entries of each shard are distinct. `recompute_count`: at least one shard has all 256 slots live.
All inputs are finite; a program needn't handle non-finite values.
Results may differ from the reference program's by a relative error of at most 0.035.
Values may be sent and summed in bfloat16 or wider, within the bound.
No kernel may reach another device: no remote copies, remote signals or barrier semaphores. Data moves between devices by JAX's collectives and lax.ppermute only.
A program may use at most 64 MiB of HBM per device.

```python
import math
import jax
import jax.numpy as jnp
import numpy as np
from jax import lax

D = 4096
QH = 32
KVH = 8
HEAD_DIM = 128
WINDOW = 4096
SPAN = 1024
SPANS_DEV = 4
CAP = 256
SHARD_LEN = 4096
SPANS = 64
CTX = 65536
SLOTS = 4096
N_BLK = 32
N_KV = 16


def draw_cache_entries(key, part):
    first_key = jax.random.fold_in(key, 0)
    base = jax.random.normal(first_key, (CTX, KVH, 2 * HEAD_DIM), jnp.float32)
    return base.astype(jnp.bfloat16)


def draw_span_order(key, part):
    blocks = SPANS // SPANS_DEV
    block_keys = jax.random.split(key, blocks)
    perms = jax.vmap(lambda one_key: jax.random.permutation(one_key, SPANS_DEV))(block_keys)
    starts = jnp.arange(blocks, dtype=jnp.int32)[:, None] * SPANS_DEV
    return (perms.astype(jnp.int32) + starts).reshape(-1).astype(jnp.int32)


def draw_recompute_pos(key, part):
    blocks = SPANS // SPANS_DEV
    block_keys = jax.random.split(key, blocks)

    def one_block(one_key):
        perm = jax.random.permutation(one_key, SHARD_LEN)[:CAP].astype(jnp.int32)
        return (perm + (SHARD_LEN - 1 - perm[0])) % SHARD_LEN
    return jax.vmap(one_block)(block_keys).reshape(-1).astype(jnp.int32)


def draw_recompute_count(key, part):
    blocks = SPANS // SPANS_DEV
    first_key, second_key = jax.random.split(key, 2)
    draws = jax.random.randint(first_key, (blocks,), 0, CAP)
    counts = 1 + draws * draws // CAP
    full = jax.random.randint(second_key, (), 0, blocks)
    return jnp.where(jnp.arange(blocks) == full, CAP, counts).astype(jnp.int32)


def place_ends(array, rng, least, largest):
    extent = array.shape
    spot = [jax.random.randint(jax.random.fold_in(rng, axis), (), 0, extent[axis]) for axis in range(len(extent))]
    array = array.at[tuple(spot)].set(least)
    longest = extent.index(max(extent))
    spot[longest] = (spot[longest] + 1) % extent[longest]
    return array.at[tuple(spot)].set(largest)


def level_of(key, shape, cuts, smallest, largest):
    def one(dim, parts):
        steps = jax.random.uniform(jax.random.fold_in(jax.random.fold_in(key, 6), dim), (parts,), jnp.float32, smallest / len(cuts), largest / len(cuts))
        return jnp.repeat(jnp.exp(steps), shape[dim] // parts).reshape((-1,) + (1,) * (len(shape) - dim - 1))

    factor_of = one(*cuts[0])
    for cut in cuts[1:]:
        factor_of = factor_of * one(*cut)
    return factor_of


def length_profile(count, total, most, slope):
    loads = [(1 << 20) // math.isqrt(standing ** slope) + 1 for standing in range(2, count + 1)]
    rest, given = total - most - (count - 1), [1] * (count - 1)
    while rest > 0:
        movable = [i for i in range(count - 1) if given[i] < most]
        mass, remaining = sum([loads[i] for i in movable]), rest
        for i in movable:
            addition = min(most - given[i], max(1, remaining * loads[i] // mass), rest)
            given[i] = given[i] + addition
            rest = rest - addition
    return np.array([most] + given)


def uneven(rng, number_of, total, bound, skew):
    if number_of == 2:
        one = jax.random.randint(rng, (), max(1, total - bound), min(bound, total - 1) + 1)
        return jnp.stack([one, total - one])
    lengths = jnp.asarray(length_profile(number_of, total, bound, skew), jnp.int32)
    pairs = (number_of - 1) // 2
    giver, sink = lengths[1:1 + 2 * pairs:2], lengths[2:2 + 2 * pairs:2]
    slack = jnp.minimum(giver - 1, bound - sink)
    passed = jax.random.randint(jax.random.fold_in(rng, 1), (pairs,), 0, 1 << 20) % (slack + 1)
    lengths = lengths.at[1:1 + 2 * pairs:2].set(giver - passed).at[2:2 + 2 * pairs:2].set(sink + passed)
    return lengths[jax.random.permutation(jax.random.fold_in(rng, 2), number_of)]


def normal_values(key, shape, spread, reach, cuts=(), kind=jnp.bfloat16):
    drawn = jax.random.normal(key, shape, jnp.float32) * spread
    if len(cuts) > 0:
        drawn = level_of(key, shape, cuts, -0.22, 0.18) * drawn
    return jnp.clip(drawn, min=-reach, max=reach).astype(kind)


def setup_inputs(seed: int = 0) -> dict:
    seeds = jax.random.split(jax.random.key(seed), 12)
    cache_entries = draw_cache_entries(jax.random.fold_in(seeds[11], 71), 0)
    recompute_input = normal_values(seeds[1], (SLOTS, D), 1.0, 6.0, ((0, 16), (1, 32)))
    norm_gain = jnp.clip(1.0 + 0.18 * jax.random.normal(seeds[2], (D,), jnp.float32), 0.099609375, 1.8984375).astype(jnp.bfloat16)
    w_query = normal_values(seeds[3], (D, QH * HEAD_DIM), (D // 9) ** -0.5, 0.25, ((1, 32),))
    w_keyval = normal_values(seeds[4], (D, KVH * 2 * HEAD_DIM), D ** -0.5, 0.09375, ((0, 32),))
    w_out = normal_values(seeds[5], (QH * HEAD_DIM, D), (QH * HEAD_DIM) ** -0.5, 0.09375, ((0, 32),))
    rotate_offsets = place_ends(jax.random.randint(seeds[6], (SPANS,), 0, CTX), jax.random.fold_in(seeds[6], 1), 0, CTX - 1).astype(jnp.int32)
    span_order = draw_span_order(jax.random.fold_in(seeds[11], 71), 0)
    tenant_of_span = jnp.searchsorted(jnp.cumsum(uneven(seeds[8], 4, SPANS, SPANS // 2, 1)), jnp.arange(SPANS), side="right").astype(jnp.int32)
    recompute_pos = draw_recompute_pos(jax.random.fold_in(seeds[11], 71), 0)
    recompute_count = draw_recompute_count(jax.random.fold_in(seeds[11], 71), 0)
    return {"cache_entries": cache_entries, "recompute_input": recompute_input, "norm_gain": norm_gain, "w_query": w_query, "w_keyval": w_keyval, "w_out": w_out, "rotate_offsets": rotate_offsets, "span_order": span_order, "tenant_of_span": tenant_of_span, "recompute_pos": recompute_pos, "recompute_count": recompute_count}


NEG_FILL = -1e+30
ROPE_BASE = 10000.0
NORM_EPS = 1e-05

def rotate_half(values, positions):
    half = values.shape[-1] // 2
    inverse = ROPE_BASE ** (-(jnp.arange(half, dtype=jnp.float32) * 2.0 / values.shape[-1]))
    angles = positions.astype(jnp.float32)[:, None] * inverse[None, :]
    shape = (positions.shape[0],) + (1,) * (values.ndim - 2) + (half,)
    cosine = jnp.cos(angles).reshape(shape)
    sine = jnp.sin(angles).reshape(shape)
    first = values[..., :half]
    second = values[..., half:]
    return jnp.concatenate([first * cosine - second * sine, second * cosine + first * sine], axis=-1)

def tenant_lookup(positions, tenant_of_span):
    span_ids = positions // SPAN
    table_index = jnp.arange(tenant_of_span.shape[0], dtype=jnp.int32)
    match = span_ids[:, None] == table_index[None, :]
    return lax.optimization_barrier(jnp.sum(jnp.where(match, tenant_of_span[None, :], 0), axis=1))

def attend_part(queries, query_pos, query_tenant, keys, values, key_pos, key_tenant):
    scale = 1.0 / math.sqrt(keys.shape[-1])
    scores = jnp.einsum('cgh,sh->gcs', queries.astype(jnp.float32), keys.astype(jnp.float32), precision=lax.Precision.HIGHEST) * scale
    gap = query_pos[:, None] - key_pos[None, :]
    allowed = (query_tenant[:, None] == key_tenant[None, :]) & (gap >= 0) & (gap < WINDOW) & (key_pos[None, :] >= 0)
    masked = jnp.where(allowed[None], scores, NEG_FILL)
    row_max = lax.optimization_barrier(jnp.max(masked, axis=2))
    weights = jnp.where(allowed[None], jnp.exp(masked - row_max[..., None]), 0.0)
    totals = lax.optimization_barrier(jnp.sum(weights, axis=2))
    rounded = weights.astype(jnp.bfloat16).astype(jnp.float32)
    summed = jnp.einsum('gcs,sh->gch', rounded, values.astype(jnp.float32), precision=lax.Precision.HIGHEST)
    return (row_max, totals, summed)

def combine_parts(first, second):
    top = jnp.maximum(first[0], second[0])
    scale_one = jnp.exp(first[0] - top)
    scale_two = jnp.exp(second[0] - top)
    totals = first[1] * scale_one + second[1] * scale_two
    summed = first[2] * scale_one[..., None] + second[2] * scale_two[..., None]
    return summed / totals[..., None]

def reference(cache_entries, recompute_input, norm_gain, w_query, w_keyval, w_out, rotate_offsets, span_order, tenant_of_span, recompute_pos, recompute_count):
    shifts = jnp.repeat(rotate_offsets, SPAN, total_repeat_length=CTX)
    turned = rotate_half(cache_entries[..., :HEAD_DIM].astype(jnp.float32), shifts).astype(jnp.bfloat16)
    rotated = jnp.concatenate([turned, cache_entries[..., HEAD_DIM:]], axis=-1)
    joined = jnp.take(rotated.reshape(SPANS, SPAN, KVH, 2 * HEAD_DIM), span_order, axis=0).reshape(CTX, KVH, 2 * HEAD_DIM)
    wide = recompute_input.astype(jnp.float32)
    inv_rms = lax.rsqrt(lax.optimization_barrier(jnp.sum(wide * wide, axis=1)) / D + NORM_EPS)
    scaled = (wide * norm_gain.astype(jnp.float32)[None, :]).astype(jnp.bfloat16)
    query_proj = jnp.dot(scaled, w_query, preferred_element_type=jnp.float32) * inv_rms[:, None]
    pair_proj = jnp.dot(scaled, w_keyval, preferred_element_type=jnp.float32) * inv_rms[:, None]
    shard_of_slot = jnp.arange(SLOTS, dtype=jnp.int32) // CAP
    slot_pos = (shard_of_slot * SHARD_LEN + recompute_pos).astype(jnp.int32)
    live = jnp.arange(SLOTS, dtype=jnp.int32) % CAP < recompute_count[shard_of_slot]
    queries = rotate_half(query_proj.reshape(SLOTS, QH, HEAD_DIM), slot_pos).astype(jnp.bfloat16)
    pair_heads = pair_proj.reshape(SLOTS, KVH, 2 * HEAD_DIM)
    fresh_keys = rotate_half(pair_heads[..., :HEAD_DIM], slot_pos).astype(jnp.bfloat16)
    fresh_values = pair_heads[..., HEAD_DIM:].astype(jnp.bfloat16)
    place = jnp.where(live, slot_pos, CTX).astype(jnp.int32)
    merged = joined.at[place].set(jnp.concatenate([fresh_keys, fresh_values], axis=-1), mode='drop')
    group = QH // KVH
    padded = jnp.concatenate([jnp.zeros((SHARD_LEN, KVH, 2 * HEAD_DIM), jnp.bfloat16), merged], axis=0)
    out_groups = w_out.astype(jnp.float32).reshape(N_BLK, QH // N_BLK, HEAD_DIM, D)

    def one_shard(index):
        query_block = lax.dynamic_slice_in_dim(queries, index * CAP, CAP, 0)
        query_at = lax.dynamic_slice_in_dim(slot_pos, index * CAP, CAP, 0)
        query_ten = tenant_lookup(query_at, tenant_of_span)
        own_rows = lax.dynamic_slice_in_dim(padded, (index + 1) * SHARD_LEN, SHARD_LEN, 0)
        prior_rows = lax.dynamic_slice_in_dim(padded, index * SHARD_LEN, SHARD_LEN, 0)
        own_at = (index * SHARD_LEN + jnp.arange(SHARD_LEN, dtype=jnp.int32)).astype(jnp.int32)
        prior_at = own_at - SHARD_LEN
        own_ten = tenant_lookup(own_at, tenant_of_span)
        prior_ten = tenant_lookup(prior_at, tenant_of_span)
        grouped = query_block.reshape(CAP, KVH, group, HEAD_DIM).transpose(1, 0, 2, 3)

        def one_group(pack):
            query_group, own_pair, prior_pair = pack
            first = attend_part(query_group, query_at, query_ten, own_pair[:, :HEAD_DIM], own_pair[:, HEAD_DIM:], own_at, own_ten)
            second = attend_part(query_group, query_at, query_ten, prior_pair[:, :HEAD_DIM], prior_pair[:, HEAD_DIM:], prior_at, prior_ten)
            return combine_parts(first, second)
        mixed = lax.map(one_group, (grouped, own_rows.transpose(1, 0, 2), prior_rows.transpose(1, 0, 2)))
        attended = mixed.reshape(QH, CAP, HEAD_DIM).astype(jnp.bfloat16)
        head_groups = attended.astype(jnp.float32).reshape(N_BLK, QH // N_BLK, CAP, HEAD_DIM)
        terms = jnp.einsum('bgch,bghd->bcd', head_groups, out_groups, precision=lax.Precision.HIGHEST).astype(jnp.bfloat16)
        terms = lax.optimization_barrier(terms)
        total = lax.optimization_barrier(jnp.sum(terms.astype(jnp.float32), axis=0))
        live_here = jnp.arange(CAP, dtype=jnp.int32) < recompute_count[index]
        return jnp.where(live_here[:, None], total, 0.0).astype(jnp.bfloat16)
    return lax.map(one_shard, jnp.arange(N_KV, dtype=jnp.int32)).reshape(SLOTS, D)
```

```python
import math

import jax
import jax.numpy as jnp
import numpy as np
from jax import lax
from jax.sharding import PartitionSpec as P

QH = 32
KVH = 8
HEAD_DIM = 128
WINDOW = 4096
SPAN = 1024


NEG_FILL = -1e30
ROPE_BASE = 10000.0
NORM_EPS = 1e-05


def shifted(shard, axis, by):
    devices = lax.axis_size(axis)
    pairs = [(i, i + by) for i in range(devices) if 0 <= i + by < devices]
    return lax.ppermute(shard, axis, pairs)


def group_gather(piece, axis, size):
    devices = lax.axis_size(axis)
    place = lax.axis_index(axis) % size
    pieces = [piece]
    for step in range(1, size):
        pairs = [(i, i - i % size + (i % size + step) % size) for i in range(devices)]
        pieces.append(lax.ppermute(piece, axis, pairs))
    stacked = jnp.stack(pieces)
    order = (place - jnp.arange(size, dtype=jnp.int32)) % size
    picked = jnp.take(stacked, order, axis=0)
    return jnp.concatenate([picked[c] for c in range(size)], axis=-1)


def rotate_half(values, positions):
    half = values.shape[-1] // 2
    inverse = ROPE_BASE ** (-(jnp.arange(half, dtype=jnp.float32) * 2.0 / values.shape[-1]))
    angles = positions.astype(jnp.float32)[:, None] * inverse[None, :]
    shape = (positions.shape[0],) + (1,) * (values.ndim - 2) + (half,)
    cosine = jnp.cos(angles).reshape(shape)
    sine = jnp.sin(angles).reshape(shape)
    first = values[..., :half]
    second = values[..., half:]
    return jnp.concatenate(
        [first * cosine - second * sine, second * cosine + first * sine], axis=-1
    )


def tenant_lookup(positions, tenant_of_span):
    span_ids = positions // SPAN
    table_index = jnp.arange(tenant_of_span.shape[0], dtype=jnp.int32)
    match = span_ids[:, None] == table_index[None, :]
    return jnp.sum(jnp.where(match, tenant_of_span[None, :], 0), axis=1)


def attend_part(queries, query_pos, query_tenant, keys, values, key_pos, key_tenant):
    scale = 1.0 / math.sqrt(keys.shape[-1])
    scores = jnp.einsum("cgh,sh->gcs", queries, keys, preferred_element_type=jnp.float32) * scale
    gap = query_pos[:, None] - key_pos[None, :]
    allowed = (
        (query_tenant[:, None] == key_tenant[None, :])
        & (gap >= 0)
        & (gap < WINDOW)
        & (key_pos[None, :] >= 0)
    )
    masked = jnp.where(allowed[None], scores, NEG_FILL)
    row_max = jnp.max(masked, axis=2)
    weights = jnp.where(allowed[None], jnp.exp(masked - row_max[..., None]), 0.0)
    totals = jnp.sum(weights, axis=2)
    summed = jnp.einsum(
        "gcs,sh->gch", weights.astype(jnp.bfloat16), values, preferred_element_type=jnp.float32
    )
    return (row_max, totals, summed)


def combine_parts(first, second):
    top = jnp.maximum(first[0], second[0])
    scale_one = jnp.exp(first[0] - top)
    scale_two = jnp.exp(second[0] - top)
    totals = first[1] * scale_one + second[1] * scale_two
    summed = first[2] * scale_one[..., None] + second[2] * scale_two[..., None]
    return summed / totals[..., None]


def local(
    cache_entries,
    recompute_input,
    norm_gain,
    w_query,
    w_keyval,
    w_out,
    rotate_offsets,
    span_order,
    tenant_of_span,
    recompute_pos,
    recompute_count,
):
    blk_count = lax.axis_size("blk")
    kv_index = lax.axis_index("kv")
    blk_index = lax.axis_index("blk")
    block_rows = cache_entries.shape[0]
    shard_len = block_rows * blk_count
    slots = recompute_input.shape[0]
    own_cols = recompute_input.shape[1]
    width = norm_gain.shape[0]
    local_heads = w_query.shape[1] // HEAD_DIM
    spans_here = shard_len // SPAN
    own_group = blk_index * local_heads // (QH // KVH)
    targets = np.arange(blk_count) * local_heads // (QH // KVH)
    spread = jnp.broadcast_to(recompute_input[:, None, :], (slots, blk_count, own_cols))
    wide = (
        lax.all_to_all(spread, "blk", 1, 1, tiled=True).reshape(slots, width).astype(jnp.float32)
    )
    gains = norm_gain.astype(jnp.float32)
    scaled = (wide * gains[None, :]).astype(jnp.bfloat16)
    query_acc = jnp.dot(scaled, w_query, preferred_element_type=jnp.float32)
    square_acc = jnp.sum(wide * wide, axis=1)
    pair_cols = w_keyval.shape[1] // blk_count
    group_size = 2 * HEAD_DIM // pair_cols
    kv_cols = lax.all_to_all(
        w_keyval.reshape(own_cols, blk_count, pair_cols), "blk", 1, 0, tiled=True
    ).reshape(width, pair_cols)
    inv_rms = lax.rsqrt(square_acc / width + NORM_EPS)
    pair_piece = jnp.dot(scaled, kv_cols, preferred_element_type=jnp.float32) * inv_rms[:, None]
    own_pair = group_gather(pair_piece, "blk", group_size)
    own_pos = lax.dynamic_slice_in_dim(recompute_pos, kv_index * slots, slots, 0)
    own_count = lax.dynamic_index_in_dim(recompute_count, kv_index, 0, keepdims=False)
    live = jnp.arange(slots, dtype=jnp.int32) < own_count
    query_pos = kv_index * shard_len + own_pos
    fresh_keys = rotate_half(own_pair[:, :HEAD_DIM], query_pos).astype(jnp.bfloat16)
    fresh_values = own_pair[:, HEAD_DIM:].astype(jnp.bfloat16)
    queries = rotate_half(
        (query_acc * inv_rms[:, None]).reshape(slots, local_heads, HEAD_DIM), query_pos
    ).astype(jnp.bfloat16)
    arrived = lax.all_to_all(
        jnp.take(cache_entries, targets, axis=1), "blk", split_axis=1, concat_axis=0, tiled=True
    )
    stored = arrived.reshape(shard_len, 2 * HEAD_DIM)
    offsets_here = lax.dynamic_slice_in_dim(rotate_offsets, kv_index * spans_here, spans_here, 0)
    row_shifts = jnp.repeat(offsets_here, SPAN, total_repeat_length=shard_len)
    turned_rows = rotate_half(stored[:, :HEAD_DIM].astype(jnp.float32), row_shifts).astype(
        jnp.bfloat16
    )
    stored = jnp.concatenate([turned_rows, stored[:, HEAD_DIM:]], axis=-1)
    local_order = (
        lax.dynamic_slice_in_dim(span_order, kv_index * spans_here, spans_here, 0)
        - kv_index * spans_here
    )
    ordered = jnp.take(stored.reshape(spans_here, SPAN, 2 * HEAD_DIM), local_order, axis=0).reshape(
        shard_len, 2 * HEAD_DIM
    )
    place = jnp.where(live, own_pos, shard_len)
    merged = ordered.at[place].set(jnp.concatenate([fresh_keys, fresh_values], axis=1), mode="drop")
    key_pos = kv_index * shard_len + jnp.arange(shard_len, dtype=jnp.int32)
    key_tenant = tenant_lookup(key_pos, tenant_of_span)
    query_tenant = tenant_lookup(query_pos, tenant_of_span)
    own_part = attend_part(
        queries,
        query_pos,
        query_tenant,
        merged[:, :HEAD_DIM],
        merged[:, HEAD_DIM:],
        key_pos,
        key_tenant,
    )
    prior = shifted(merged, "kv", 1)
    prior_pos = key_pos - shard_len
    prior_part = attend_part(
        queries,
        query_pos,
        query_tenant,
        prior[:, :HEAD_DIM],
        prior[:, HEAD_DIM:],
        prior_pos,
        tenant_lookup(prior_pos, tenant_of_span),
    )
    heads_out = combine_parts(own_part, prior_part).astype(jnp.bfloat16)
    out_rows = w_out.reshape(local_heads, HEAD_DIM, width)
    term = jnp.einsum("gch,ghd->cd", heads_out, out_rows, preferred_element_type=jnp.float32)
    term_blocks = term.astype(jnp.bfloat16).reshape(slots, blk_count, own_cols)
    arrived_terms = lax.all_to_all(term_blocks, "blk", 1, 1, tiled=True)
    summed_out = jnp.sum(arrived_terms.astype(jnp.float32), axis=1)
    return jnp.where(live[:, None], summed_out, 0.0).astype(jnp.bfloat16)


def solution(mesh):
    placed = (
        P(("kv", "blk"), None, None),
        P("kv", "blk"),
        P(),
        P(None, "blk"),
        P("blk", None),
        P("blk", None),
        P(),
        P(),
        P(),
        P(),
        P(),
    )
    return jax.shard_map(
        local, mesh=mesh, in_specs=placed, out_specs=P("kv", "blk"), check_vma=False
    )
```

```python
import math

import jax
import jax.numpy as jnp
import numpy as np
from jax import lax
from jax.sharding import PartitionSpec as P

QH = 32
KVH = 8
HEAD_DIM = 128
WINDOW = 4096
SPAN = 1024


NEG_FILL = -1e30
ROPE_BASE = 10000.0
NORM_EPS = 1e-05


def shifted(shard, axis, by):
    devices = lax.axis_size(axis)
    pairs = [(i, i + by) for i in range(devices) if 0 <= i + by < devices]
    return lax.ppermute(shard, axis, pairs)


def rotate_half(values, positions):
    half = values.shape[-1] // 2
    inverse = ROPE_BASE ** (-(jnp.arange(half, dtype=jnp.float32) * 2.0 / values.shape[-1]))
    angles = positions.astype(jnp.float32)[:, None] * inverse[None, :]
    shape = (positions.shape[0],) + (1,) * (values.ndim - 2) + (half,)
    cosine = jnp.cos(angles).reshape(shape)
    sine = jnp.sin(angles).reshape(shape)
    first = values[..., :half]
    second = values[..., half:]
    return jnp.concatenate(
        [first * cosine - second * sine, second * cosine + first * sine], axis=-1
    )


def tenant_lookup(positions, tenant_of_span):
    span_ids = positions // SPAN
    table_index = jnp.arange(tenant_of_span.shape[0], dtype=jnp.int32)
    match = span_ids[:, None] == table_index[None, :]
    return jnp.sum(jnp.where(match, tenant_of_span[None, :], 0), axis=1)


def attend_part(queries, query_pos, query_tenant, keys, values, key_pos, key_tenant):
    scale = 1.0 / math.sqrt(keys.shape[-1])
    scores = jnp.einsum("cgh,sh->gcs", queries, keys, preferred_element_type=jnp.float32) * scale
    gap = query_pos[:, None] - key_pos[None, :]
    allowed = (
        (query_tenant[:, None] == key_tenant[None, :])
        & (gap >= 0)
        & (gap < WINDOW)
        & (key_pos[None, :] >= 0)
    )
    masked = jnp.where(allowed[None], scores, NEG_FILL)
    row_max = jnp.max(masked, axis=2)
    weights = jnp.where(allowed[None], jnp.exp(masked - row_max[..., None]), 0.0)
    totals = jnp.sum(weights, axis=2)
    summed = jnp.einsum(
        "gcs,sh->gch", weights.astype(jnp.bfloat16), values, preferred_element_type=jnp.float32
    )
    return (row_max, totals, summed)


def combine_parts(first, second):
    top = jnp.maximum(first[0], second[0])
    scale_one = jnp.exp(first[0] - top)
    scale_two = jnp.exp(second[0] - top)
    totals = first[1] * scale_one + second[1] * scale_two
    summed = first[2] * scale_one[..., None] + second[2] * scale_two[..., None]
    return summed / totals[..., None]


def group_gather(piece, axis, size):
    devices = lax.axis_size(axis)
    place = lax.axis_index(axis) % size
    pieces = [piece]
    for step in range(1, size):
        pairs = [(i, i - i % size + (i % size + step) % size) for i in range(devices)]
        pieces.append(lax.ppermute(piece, axis, pairs))
    stacked = jnp.stack(pieces)
    order = (place - jnp.arange(size, dtype=jnp.int32)) % size
    return jnp.take(stacked, order, axis=0)


def group_exchange(parts, axis, size):
    devices = lax.axis_size(axis)
    place = lax.axis_index(axis) % size
    mine = [lax.dynamic_index_in_dim(parts, place, 0, keepdims=False)]
    for step in range(1, size):
        pairs = [(i, i - i % size + (i % size + step) % size) for i in range(devices)]
        outgoing = lax.dynamic_index_in_dim(parts, (place + step) % size, 0, keepdims=False)
        mine.append(lax.ppermute(outgoing, axis, pairs))
    return jnp.stack(mine)


def joined_slot(span_order, shard, spans_here, block):
    local_order = lax.dynamic_slice_in_dim(span_order, shard * spans_here, spans_here, 0)
    local_order = local_order - shard * spans_here
    return jnp.sum(jnp.where(local_order == block, jnp.arange(spans_here, dtype=jnp.int32), 0))


def local(
    cache_entries,
    recompute_input,
    norm_gain,
    w_query,
    w_keyval,
    w_out,
    rotate_offsets,
    span_order,
    tenant_of_span,
    recompute_pos,
    recompute_count,
):
    blk_count = lax.axis_size("blk")
    kv_index = lax.axis_index("kv")
    blk_index = lax.axis_index("blk")
    block_rows = cache_entries.shape[0]
    shard_len = block_rows * blk_count
    slots = recompute_input.shape[0]
    own_cols = recompute_input.shape[1]
    width = norm_gain.shape[0]
    spans_here = shard_len // SPAN
    group_size = QH // KVH
    chunks_per_span = SPAN // block_rows
    pair_cols = w_keyval.shape[1] // blk_count
    member = blk_index % group_size
    group = blk_index // group_size

    x_part = jnp.broadcast_to(
        recompute_input.reshape(1, slots * own_cols), (blk_count, slots * own_cols)
    )
    w_part = (
        w_keyval.reshape(own_cols, blk_count, pair_cols)
        .transpose(1, 0, 2)
        .reshape(blk_count, own_cols * pair_cols)
    )
    arrived = lax.all_to_all(
        jnp.concatenate([x_part, w_part], axis=1), "blk", 0, 0, tiled=True
    )
    wide = (
        arrived[:, : slots * own_cols]
        .reshape(blk_count, slots, own_cols)
        .transpose(1, 0, 2)
        .reshape(slots, width)
        .astype(jnp.float32)
    )
    kv_cols = arrived[:, slots * own_cols :].reshape(width, pair_cols)

    pieces = []
    for step in range(chunks_per_span):
        chosen = (blk_index % chunks_per_span + step) % KVH
        pairs = [
            (k, ((k % chunks_per_span + step) % KVH) * group_size + k // chunks_per_span)
            for k in range(blk_count)
        ]
        outgoing = lax.dynamic_index_in_dim(cache_entries, chosen, 1, keepdims=False)
        pieces.append(lax.ppermute(outgoing, "blk", pairs))
    stacked = jnp.stack(pieces)
    order = (group - jnp.arange(chunks_per_span, dtype=jnp.int32)) % KVH
    stored = jnp.take(stacked, order, axis=0).reshape(SPAN, 2 * HEAD_DIM)

    gains = norm_gain.astype(jnp.float32)
    scaled = (wide * gains[None, :]).astype(jnp.bfloat16)
    square_acc = jnp.sum(wide * wide, axis=1)
    inv_rms = lax.rsqrt(square_acc / width + NORM_EPS)
    query_acc = jnp.dot(scaled, w_query, preferred_element_type=jnp.float32) * inv_rms[:, None]
    pair_piece = jnp.dot(scaled, kv_cols, preferred_element_type=jnp.float32) * inv_rms[:, None]
    shared = group_gather(jnp.concatenate([query_acc, pair_piece], axis=1), "blk", group_size)
    group_pair = shared[:, :, HEAD_DIM:].transpose(1, 0, 2).reshape(slots, group_size * pair_cols)

    own_pos = lax.dynamic_slice_in_dim(recompute_pos, kv_index * slots, slots, 0)
    own_count = lax.dynamic_index_in_dim(recompute_count, kv_index, 0, keepdims=False)
    live = jnp.arange(slots, dtype=jnp.int32) < own_count
    query_pos = kv_index * shard_len + own_pos
    fresh_keys = rotate_half(group_pair[:, :HEAD_DIM], query_pos).astype(jnp.bfloat16)
    fresh_values = group_pair[:, HEAD_DIM:].astype(jnp.bfloat16)
    queries = rotate_half(shared[:, :, :HEAD_DIM].transpose(1, 0, 2), query_pos).astype(
        jnp.bfloat16
    )

    offset = lax.dynamic_index_in_dim(
        rotate_offsets, kv_index * spans_here + member, 0, keepdims=False
    )
    row_shifts = jnp.full((SPAN,), offset, dtype=jnp.int32)
    turned_rows = rotate_half(stored[:, :HEAD_DIM].astype(jnp.float32), row_shifts).astype(
        jnp.bfloat16
    )
    stored = jnp.concatenate([turned_rows, stored[:, HEAD_DIM:]], axis=-1)
    own_slot = joined_slot(span_order, kv_index, spans_here, member)
    place = jnp.where(live & (own_pos // SPAN == own_slot), own_pos % SPAN, SPAN)
    merged = stored.at[place].set(jnp.concatenate([fresh_keys, fresh_values], axis=1), mode="drop")
    key_pos = kv_index * shard_len + own_slot * SPAN + jnp.arange(SPAN, dtype=jnp.int32)
    query_tenant = tenant_lookup(query_pos, tenant_of_span)
    own_part = attend_part(
        queries,
        query_pos,
        query_tenant,
        merged[:, :HEAD_DIM],
        merged[:, HEAD_DIM:],
        key_pos,
        tenant_lookup(key_pos, tenant_of_span),
    )
    prior = shifted(merged, "kv", 1)
    prior_slot = joined_slot(span_order, jnp.maximum(kv_index - 1, 0), spans_here, member)
    prior_pos = (
        (kv_index - 1) * shard_len + prior_slot * SPAN + jnp.arange(SPAN, dtype=jnp.int32)
    )
    prior_part = attend_part(
        queries,
        query_pos,
        query_tenant,
        prior[:, :HEAD_DIM],
        prior[:, HEAD_DIM:],
        prior_pos,
        tenant_lookup(prior_pos, tenant_of_span),
    )
    top = jnp.maximum(own_part[0], prior_part[0])
    scale_own = jnp.exp(own_part[0] - top)
    scale_prior = jnp.exp(prior_part[0] - top)
    totals = own_part[1] * scale_own + prior_part[1] * scale_prior
    summed = own_part[2] * scale_own[..., None] + prior_part[2] * scale_prior[..., None]
    packed = jnp.concatenate([summed, top[..., None], totals[..., None]], axis=-1)
    gathered = group_exchange(packed, "blk", group_size)
    part_max = gathered[:, :, HEAD_DIM]
    best = jnp.max(part_max, axis=0)
    weight = jnp.exp(part_max - best[None])
    total = jnp.sum(gathered[:, :, HEAD_DIM + 1] * weight, axis=0)
    heads_sum = jnp.sum(gathered[:, :, :HEAD_DIM] * weight[..., None], axis=0)
    heads_out = (heads_sum / total[:, None]).astype(jnp.bfloat16)
    term = jnp.dot(heads_out, w_out, preferred_element_type=jnp.float32)
    term_blocks = term.astype(jnp.bfloat16).reshape(slots, blk_count, own_cols)
    arrived_terms = lax.all_to_all(term_blocks, "blk", 1, 1, tiled=True)
    summed_out = jnp.sum(arrived_terms.astype(jnp.float32), axis=1)
    return jnp.where(live[:, None], summed_out, 0.0).astype(jnp.bfloat16)


def solution(mesh):
    placed = (
        P(("kv", "blk"), None, None),
        P("kv", "blk"),
        P(),
        P(None, "blk"),
        P("blk", None),
        P("blk", None),
        P(),
        P(),
        P(),
        P(),
        P(),
    )
    return jax.shard_map(
        local, mesh=mesh, in_specs=placed, out_specs=P("kv", "blk"), check_vma=False
    )
```

```python
import math

import jax
import jax.numpy as jnp
import numpy as np
from jax import lax
from jax.sharding import PartitionSpec as P

QH = 32
KVH = 8
HEAD_DIM = 128
WINDOW = 4096
SPAN = 1024


NEG_FILL = -1e30
ROPE_BASE = 10000.0
NORM_EPS = 1e-05


def shifted(shard, axis, by):
    devices = lax.axis_size(axis)
    pairs = [(i, i + by) for i in range(devices) if 0 <= i + by < devices]
    return lax.ppermute(shard, axis, pairs)


def rotate_half(values, positions):
    half = values.shape[-1] // 2
    inverse = ROPE_BASE ** (-(jnp.arange(half, dtype=jnp.float32) * 2.0 / values.shape[-1]))
    angles = positions.astype(jnp.float32)[:, None] * inverse[None, :]
    shape = (positions.shape[0],) + (1,) * (values.ndim - 2) + (half,)
    cosine = jnp.cos(angles).reshape(shape)
    sine = jnp.sin(angles).reshape(shape)
    first = values[..., :half]
    second = values[..., half:]
    return jnp.concatenate(
        [first * cosine - second * sine, second * cosine + first * sine], axis=-1
    )


def tenant_lookup(positions, tenant_of_span):
    span_ids = positions // SPAN
    table_index = jnp.arange(tenant_of_span.shape[0], dtype=jnp.int32)
    match = span_ids[:, None] == table_index[None, :]
    return jnp.sum(jnp.where(match, tenant_of_span[None, :], 0), axis=1)


def attend_part(queries, query_pos, query_tenant, keys, values, key_pos, key_tenant):
    scale = 1.0 / math.sqrt(keys.shape[-1])
    scores = jnp.einsum("cgh,sh->gcs", queries, keys, preferred_element_type=jnp.float32) * scale
    gap = query_pos[:, None] - key_pos[None, :]
    allowed = (
        (query_tenant[:, None] == key_tenant[None, :])
        & (gap >= 0)
        & (gap < WINDOW)
        & (key_pos[None, :] >= 0)
    )
    masked = jnp.where(allowed[None], scores, NEG_FILL)
    row_max = jnp.max(masked, axis=2)
    weights = jnp.where(allowed[None], jnp.exp(masked - row_max[..., None]), 0.0)
    totals = jnp.sum(weights, axis=2)
    summed = jnp.einsum(
        "gcs,sh->gch", weights.astype(jnp.bfloat16), values, preferred_element_type=jnp.float32
    )
    return (row_max, totals, summed)


def combine_parts(first, second):
    top = jnp.maximum(first[0], second[0])
    scale_one = jnp.exp(first[0] - top)
    scale_two = jnp.exp(second[0] - top)
    totals = first[1] * scale_one + second[1] * scale_two
    summed = first[2] * scale_one[..., None] + second[2] * scale_two[..., None]
    return summed / totals[..., None]


def group_gather(piece, axis, size):
    devices = lax.axis_size(axis)
    place = lax.axis_index(axis) % size
    pieces = [piece]
    for step in range(1, size):
        pairs = [(i, i - i % size + (i % size + step) % size) for i in range(devices)]
        pieces.append(lax.ppermute(piece, axis, pairs))
    stacked = jnp.stack(pieces)
    order = (place - jnp.arange(size, dtype=jnp.int32)) % size
    return jnp.take(stacked, order, axis=0)


def group_exchange(parts, axis, size):
    devices = lax.axis_size(axis)
    place = lax.axis_index(axis) % size
    mine = [lax.dynamic_index_in_dim(parts, place, 0, keepdims=False)]
    for step in range(1, size):
        pairs = [(i, i - i % size + (i % size + step) % size) for i in range(devices)]
        outgoing = lax.dynamic_index_in_dim(parts, (place + step) % size, 0, keepdims=False)
        mine.append(lax.ppermute(outgoing, axis, pairs))
    return jnp.stack(mine)


def joined_rows(span_order, shard, spans_here, stored_rows):
    local_order = lax.dynamic_slice_in_dim(span_order, shard * spans_here, spans_here, 0)
    local_order = local_order - shard * spans_here
    blocks = jnp.arange(spans_here, dtype=jnp.int32)
    inverse = jnp.sum(
        jnp.where(local_order[None, :] == blocks[:, None], blocks[None, :], 0), axis=1
    )
    slot = jnp.take(inverse, stored_rows // SPAN)
    return shard * spans_here * SPAN + slot * SPAN + stored_rows % SPAN


def local(
    cache_entries,
    recompute_input,
    norm_gain,
    w_query,
    w_keyval,
    w_out,
    rotate_offsets,
    span_order,
    tenant_of_span,
    recompute_pos,
    recompute_count,
):
    blk_count = lax.axis_size("blk")
    kv_index = lax.axis_index("kv")
    blk_index = lax.axis_index("blk")
    block_rows = cache_entries.shape[0]
    shard_len = block_rows * blk_count
    slots = recompute_input.shape[0]
    own_cols = recompute_input.shape[1]
    width = norm_gain.shape[0]
    spans_here = shard_len // SPAN
    group_size = QH // KVH
    pair_cols = w_keyval.shape[1] // blk_count
    member = blk_index % group_size
    group = blk_index // group_size

    rows_each = block_rows // group_size
    x_part = jnp.broadcast_to(recompute_input[None], (blk_count, slots, own_cols))
    w_part = (
        w_keyval.reshape(own_cols, blk_count, pair_cols)
        .transpose(1, 0, 2)
        .reshape(blk_count, own_cols * pair_cols // HEAD_DIM, HEAD_DIM)
    )
    c_part = (
        cache_entries.reshape(group_size, rows_each, KVH, 2 * HEAD_DIM)
        .transpose(2, 0, 1, 3)
        .reshape(blk_count, rows_each * 2, HEAD_DIM)
    )
    arrived = lax.all_to_all(
        jnp.concatenate([x_part, w_part, c_part], axis=1), "blk", 0, 0, tiled=True
    )
    w_rows = own_cols * pair_cols // HEAD_DIM
    wide = arrived[:, :slots].astype(jnp.float32)
    kv_cols = arrived[:, slots : slots + w_rows].reshape(blk_count, own_cols, pair_cols)
    stored = arrived[:, slots + w_rows :].reshape(blk_count * rows_each, 2 * HEAD_DIM)

    gains = norm_gain.astype(jnp.float32).reshape(blk_count, 1, own_cols)
    scaled = (wide * gains).astype(jnp.bfloat16)
    square_acc = jnp.sum(wide * wide, axis=(0, 2))
    inv_rms = lax.rsqrt(square_acc / width + NORM_EPS)
    query_acc = jnp.einsum(
        "ksc,kcd->sd",
        scaled,
        w_query.reshape(blk_count, own_cols, HEAD_DIM),
        preferred_element_type=jnp.float32,
    ) * inv_rms[:, None]
    pair_piece = jnp.einsum(
        "ksc,kcd->sd", scaled, kv_cols, preferred_element_type=jnp.float32
    ) * inv_rms[:, None]
    shared = group_gather(jnp.concatenate([query_acc, pair_piece], axis=1), "blk", group_size)
    group_pair = shared[:, :, HEAD_DIM:].transpose(1, 0, 2).reshape(slots, group_size * pair_cols)

    own_pos = lax.dynamic_slice_in_dim(recompute_pos, kv_index * slots, slots, 0)
    own_count = lax.dynamic_index_in_dim(recompute_count, kv_index, 0, keepdims=False)
    live = jnp.arange(slots, dtype=jnp.int32) < own_count
    query_pos = kv_index * shard_len + own_pos
    fresh_keys = rotate_half(group_pair[:, :HEAD_DIM], query_pos).astype(jnp.bfloat16)
    fresh_values = group_pair[:, HEAD_DIM:].astype(jnp.bfloat16)
    queries = rotate_half(shared[:, :, :HEAD_DIM].transpose(1, 0, 2), query_pos).astype(
        jnp.bfloat16
    )

    local_rows = jnp.arange(blk_count * rows_each, dtype=jnp.int32)
    stored_rows = (local_rows // rows_each) * block_rows + member * rows_each + local_rows % rows_each
    key_pos = joined_rows(span_order, kv_index, spans_here, stored_rows)
    offsets = lax.dynamic_slice_in_dim(rotate_offsets, kv_index * spans_here, spans_here, 0)
    row_shifts = jnp.take(offsets, stored_rows // SPAN)
    turned_rows = rotate_half(stored[:, :HEAD_DIM].astype(jnp.float32), row_shifts).astype(
        jnp.bfloat16
    )
    stored = jnp.concatenate([turned_rows, stored[:, HEAD_DIM:]], axis=-1)
    local_order = lax.dynamic_slice_in_dim(span_order, kv_index * spans_here, spans_here, 0)
    slot_rows = (jnp.take(local_order, own_pos // SPAN) - kv_index * spans_here) * SPAN + own_pos % SPAN
    mine = live & ((slot_rows % block_rows) // rows_each == member)
    place = jnp.where(
        mine, (slot_rows // block_rows) * rows_each + slot_rows % rows_each, blk_count * rows_each
    )
    merged = stored.at[place].set(jnp.concatenate([fresh_keys, fresh_values], axis=1), mode="drop")
    query_tenant = tenant_lookup(query_pos, tenant_of_span)
    own_part = attend_part(
        queries,
        query_pos,
        query_tenant,
        merged[:, :HEAD_DIM],
        merged[:, HEAD_DIM:],
        key_pos,
        tenant_lookup(key_pos, tenant_of_span),
    )
    prior = shifted(merged, "kv", 1)
    prior_pos = joined_rows(span_order, jnp.maximum(kv_index - 1, 0), spans_here, stored_rows)
    prior_pos = jnp.where(kv_index > 0, prior_pos, -1)
    prior_part = attend_part(
        queries,
        query_pos,
        query_tenant,
        prior[:, :HEAD_DIM],
        prior[:, HEAD_DIM:],
        prior_pos,
        tenant_lookup(prior_pos, tenant_of_span),
    )
    top = jnp.maximum(own_part[0], prior_part[0])
    scale_own = jnp.exp(own_part[0] - top)
    scale_prior = jnp.exp(prior_part[0] - top)
    totals = own_part[1] * scale_own + prior_part[1] * scale_prior
    summed = own_part[2] * scale_own[..., None] + prior_part[2] * scale_prior[..., None]
    packed = jnp.concatenate([summed, top[..., None], totals[..., None]], axis=-1)
    gathered = group_exchange(packed, "blk", group_size)
    part_max = gathered[:, :, HEAD_DIM]
    best = jnp.max(part_max, axis=0)
    weight = jnp.exp(part_max - best[None])
    total = jnp.sum(gathered[:, :, HEAD_DIM + 1] * weight, axis=0)
    heads_sum = jnp.sum(gathered[:, :, :HEAD_DIM] * weight[..., None], axis=0)
    heads_out = (heads_sum / total[:, None]).astype(jnp.bfloat16)
    term = jnp.dot(heads_out, w_out, preferred_element_type=jnp.float32)
    term_blocks = term.astype(jnp.bfloat16).reshape(slots, blk_count, own_cols)
    arrived_terms = lax.all_to_all(term_blocks, "blk", 1, 1, tiled=True)
    summed_out = jnp.sum(arrived_terms.astype(jnp.float32), axis=1)
    return jnp.where(live[:, None], summed_out, 0.0).astype(jnp.bfloat16)


def solution(mesh):
    placed = (
        P(("kv", "blk"), None, None),
        P("kv", "blk"),
        P(),
        P(None, "blk"),
        P("blk", None),
        P("blk", None),
        P(),
        P(),
        P(),
        P(),
        P(),
    )
    return jax.shard_map(
        local, mesh=mesh, in_specs=placed, out_specs=P("kv", "blk"), check_vma=False
    )
```

```python
import math

import jax
import jax.numpy as jnp
import numpy as np
from jax import lax
from jax.sharding import PartitionSpec as P

QH = 32
KVH = 8
HEAD_DIM = 128
WINDOW = 4096
SPAN = 1024


NEG_FILL = -1e30
ROPE_BASE = 10000.0
NORM_EPS = 1e-05


def shifted(shard, axis, by):
    devices = lax.axis_size(axis)
    pairs = [(i, i + by) for i in range(devices) if 0 <= i + by < devices]
    return lax.ppermute(shard, axis, pairs)


def rotate_half(values, positions):
    half = values.shape[-1] // 2
    inverse = ROPE_BASE ** (-(jnp.arange(half, dtype=jnp.float32) * 2.0 / values.shape[-1]))
    angles = positions.astype(jnp.float32)[:, None] * inverse[None, :]
    shape = (positions.shape[0],) + (1,) * (values.ndim - 2) + (half,)
    cosine = jnp.cos(angles).reshape(shape)
    sine = jnp.sin(angles).reshape(shape)
    first = values[..., :half]
    second = values[..., half:]
    return jnp.concatenate(
        [first * cosine - second * sine, second * cosine + first * sine], axis=-1
    )


def tenant_lookup(positions, tenant_of_span):
    span_ids = positions // SPAN
    table_index = jnp.arange(tenant_of_span.shape[0], dtype=jnp.int32)
    match = span_ids[:, None] == table_index[None, :]
    return jnp.sum(jnp.where(match, tenant_of_span[None, :], 0), axis=1)


def attend_part(queries, query_pos, query_tenant, keys, values, key_pos, key_tenant):
    scale = 1.0 / math.sqrt(keys.shape[-1])
    scores = jnp.einsum("cgh,sh->gcs", queries, keys, preferred_element_type=jnp.float32) * scale
    gap = query_pos[:, None] - key_pos[None, :]
    allowed = (
        (query_tenant[:, None] == key_tenant[None, :])
        & (gap >= 0)
        & (gap < WINDOW)
        & (key_pos[None, :] >= 0)
    )
    masked = jnp.where(allowed[None], scores, NEG_FILL)
    row_max = jnp.max(masked, axis=2)
    weights = jnp.where(allowed[None], jnp.exp(masked - row_max[..., None]), 0.0)
    totals = jnp.sum(weights, axis=2)
    summed = jnp.einsum(
        "gcs,sh->gch", weights.astype(jnp.bfloat16), values, preferred_element_type=jnp.float32
    )
    return (row_max, totals, summed)


def combine_parts(first, second):
    top = jnp.maximum(first[0], second[0])
    scale_one = jnp.exp(first[0] - top)
    scale_two = jnp.exp(second[0] - top)
    totals = first[1] * scale_one + second[1] * scale_two
    summed = first[2] * scale_one[..., None] + second[2] * scale_two[..., None]
    return summed / totals[..., None]


def group_gather(piece, axis, size):
    devices = lax.axis_size(axis)
    place = lax.axis_index(axis) % size
    pieces = [piece]
    for step in range(1, size):
        pairs = [(i, i - i % size + (i % size + step) % size) for i in range(devices)]
        pieces.append(lax.ppermute(piece, axis, pairs))
    stacked = jnp.stack(pieces)
    order = (place - jnp.arange(size, dtype=jnp.int32)) % size
    return jnp.take(stacked, order, axis=0)


def group_exchange(parts, axis, size):
    devices = lax.axis_size(axis)
    place = lax.axis_index(axis) % size
    mine = [lax.dynamic_index_in_dim(parts, place, 0, keepdims=False)]
    for step in range(1, size):
        pairs = [(i, i - i % size + (i % size + step) % size) for i in range(devices)]
        outgoing = lax.dynamic_index_in_dim(parts, (place + step) % size, 0, keepdims=False)
        mine.append(lax.ppermute(outgoing, axis, pairs))
    return jnp.stack(mine)


def joined_rows(span_order, shard, spans_here, stored_rows):
    local_order = lax.dynamic_slice_in_dim(span_order, shard * spans_here, spans_here, 0)
    local_order = local_order - shard * spans_here
    blocks = jnp.arange(spans_here, dtype=jnp.int32)
    inverse = jnp.sum(
        jnp.where(local_order[None, :] == blocks[:, None], blocks[None, :], 0), axis=1
    )
    slot = jnp.take(inverse, stored_rows // SPAN)
    return shard * spans_here * SPAN + slot * SPAN + stored_rows % SPAN


def local(
    cache_entries,
    recompute_input,
    norm_gain,
    w_query,
    w_keyval,
    w_out,
    rotate_offsets,
    span_order,
    tenant_of_span,
    recompute_pos,
    recompute_count,
):
    blk_count = lax.axis_size("blk")
    kv_index = lax.axis_index("kv")
    blk_index = lax.axis_index("blk")
    block_rows = cache_entries.shape[0]
    shard_len = block_rows * blk_count
    slots = recompute_input.shape[0]
    own_cols = recompute_input.shape[1]
    width = norm_gain.shape[0]
    spans_here = shard_len // SPAN
    group_size = QH // KVH
    pair_cols = w_keyval.shape[1] // blk_count
    member = blk_index % group_size
    group = blk_index // group_size

    rows_each = block_rows // group_size
    x_part = jnp.broadcast_to(recompute_input[None], (blk_count, slots, own_cols))
    w_part = (
        w_keyval.reshape(own_cols, blk_count, pair_cols)
        .transpose(1, 0, 2)
        .reshape(blk_count, own_cols * pair_cols // HEAD_DIM, HEAD_DIM)
    )
    c_part = (
        cache_entries.reshape(group_size, rows_each, KVH, 2 * HEAD_DIM)
        .transpose(2, 0, 1, 3)
        .reshape(blk_count, rows_each * 2, HEAD_DIM)
    )
    arrived = lax.all_to_all(jnp.concatenate([x_part, w_part], axis=1), "blk", 0, 0, tiled=True)
    wide = arrived[:, :slots].astype(jnp.float32)
    kv_cols = arrived[:, slots:].reshape(blk_count, own_cols, pair_cols)
    arrived, c_part = lax.optimization_barrier((arrived, c_part))
    stored = lax.all_to_all(c_part, "blk", 0, 0, tiled=True).reshape(
        blk_count * rows_each, 2 * HEAD_DIM
    )

    gains = norm_gain.astype(jnp.float32).reshape(blk_count, 1, own_cols)
    scaled = (wide * gains).astype(jnp.bfloat16)
    square_acc = jnp.sum(wide * wide, axis=(0, 2))
    inv_rms = lax.rsqrt(square_acc / width + NORM_EPS)
    query_acc = jnp.einsum(
        "ksc,kcd->sd",
        scaled,
        w_query.reshape(blk_count, own_cols, HEAD_DIM),
        preferred_element_type=jnp.float32,
    ) * inv_rms[:, None]
    pair_piece = jnp.einsum(
        "ksc,kcd->sd", scaled, kv_cols, preferred_element_type=jnp.float32
    ) * inv_rms[:, None]
    shared = group_gather(jnp.concatenate([query_acc, pair_piece], axis=1), "blk", group_size)
    group_pair = shared[:, :, HEAD_DIM:].transpose(1, 0, 2).reshape(slots, group_size * pair_cols)

    own_pos = lax.dynamic_slice_in_dim(recompute_pos, kv_index * slots, slots, 0)
    own_count = lax.dynamic_index_in_dim(recompute_count, kv_index, 0, keepdims=False)
    live = jnp.arange(slots, dtype=jnp.int32) < own_count
    query_pos = kv_index * shard_len + own_pos
    fresh_keys = rotate_half(group_pair[:, :HEAD_DIM], query_pos).astype(jnp.bfloat16)
    fresh_values = group_pair[:, HEAD_DIM:].astype(jnp.bfloat16)
    queries = rotate_half(shared[:, :, :HEAD_DIM].transpose(1, 0, 2), query_pos).astype(
        jnp.bfloat16
    )

    local_rows = jnp.arange(blk_count * rows_each, dtype=jnp.int32)
    stored_rows = (local_rows // rows_each) * block_rows + member * rows_each + local_rows % rows_each
    key_pos = joined_rows(span_order, kv_index, spans_here, stored_rows)
    offsets = lax.dynamic_slice_in_dim(rotate_offsets, kv_index * spans_here, spans_here, 0)
    row_shifts = jnp.take(offsets, stored_rows // SPAN)
    turned_rows = rotate_half(stored[:, :HEAD_DIM].astype(jnp.float32), row_shifts).astype(
        jnp.bfloat16
    )
    stored = jnp.concatenate([turned_rows, stored[:, HEAD_DIM:]], axis=-1)
    local_order = lax.dynamic_slice_in_dim(span_order, kv_index * spans_here, spans_here, 0)
    slot_rows = (jnp.take(local_order, own_pos // SPAN) - kv_index * spans_here) * SPAN + own_pos % SPAN
    mine = live & ((slot_rows % block_rows) // rows_each == member)
    place = jnp.where(
        mine, (slot_rows // block_rows) * rows_each + slot_rows % rows_each, blk_count * rows_each
    )
    merged = stored.at[place].set(jnp.concatenate([fresh_keys, fresh_values], axis=1), mode="drop")
    query_tenant = tenant_lookup(query_pos, tenant_of_span)
    own_part = attend_part(
        queries,
        query_pos,
        query_tenant,
        merged[:, :HEAD_DIM],
        merged[:, HEAD_DIM:],
        key_pos,
        tenant_lookup(key_pos, tenant_of_span),
    )
    prior = shifted(merged, "kv", 1)
    prior_pos = joined_rows(span_order, jnp.maximum(kv_index - 1, 0), spans_here, stored_rows)
    prior_pos = jnp.where(kv_index > 0, prior_pos, -1)
    prior_part = attend_part(
        queries,
        query_pos,
        query_tenant,
        prior[:, :HEAD_DIM],
        prior[:, HEAD_DIM:],
        prior_pos,
        tenant_lookup(prior_pos, tenant_of_span),
    )
    top = jnp.maximum(own_part[0], prior_part[0])
    scale_own = jnp.exp(own_part[0] - top)
    scale_prior = jnp.exp(prior_part[0] - top)
    totals = own_part[1] * scale_own + prior_part[1] * scale_prior
    summed = own_part[2] * scale_own[..., None] + prior_part[2] * scale_prior[..., None]
    packed = jnp.concatenate([summed, top[..., None], totals[..., None]], axis=-1)
    gathered = group_exchange(packed, "blk", group_size)
    part_max = gathered[:, :, HEAD_DIM]
    best = jnp.max(part_max, axis=0)
    weight = jnp.exp(part_max - best[None])
    total = jnp.sum(gathered[:, :, HEAD_DIM + 1] * weight, axis=0)
    heads_sum = jnp.sum(gathered[:, :, :HEAD_DIM] * weight[..., None], axis=0)
    heads_out = (heads_sum / total[:, None]).astype(jnp.bfloat16)
    term = jnp.dot(heads_out, w_out, preferred_element_type=jnp.float32)
    term_blocks = term.astype(jnp.bfloat16).reshape(slots, blk_count, own_cols)
    arrived_terms = lax.all_to_all(term_blocks, "blk", 1, 1, tiled=True)
    summed_out = jnp.sum(arrived_terms.astype(jnp.float32), axis=1)
    return jnp.where(live[:, None], summed_out, 0.0).astype(jnp.bfloat16)


def solution(mesh):
    placed = (
        P(("kv", "blk"), None, None),
        P("kv", "blk"),
        P(),
        P(None, "blk"),
        P("blk", None),
        P("blk", None),
        P(),
        P(),
        P(),
        P(),
        P(),
    )
    return jax.shard_map(
        local, mesh=mesh, in_specs=placed, out_specs=P("kv", "blk"), check_vma=False
    )
```

```python
import math

import jax
import jax.numpy as jnp
import numpy as np
from jax import lax
from jax.sharding import PartitionSpec as P

QH = 32
KVH = 8
HEAD_DIM = 128
WINDOW = 4096
SPAN = 1024


NEG_FILL = -1e30
RING_FAST = 4
ROPE_BASE = 10000.0
NORM_EPS = 1e-05


def shifted(shard, axis, by):
    devices = lax.axis_size(axis)
    pairs = [(i, i + by) for i in range(devices) if 0 <= i + by < devices]
    return lax.ppermute(shard, axis, pairs)


def rotate_half(values, positions):
    half = values.shape[-1] // 2
    inverse = ROPE_BASE ** (-(jnp.arange(half, dtype=jnp.float32) * 2.0 / values.shape[-1]))
    angles = positions.astype(jnp.float32)[:, None] * inverse[None, :]
    shape = (positions.shape[0],) + (1,) * (values.ndim - 2) + (half,)
    cosine = jnp.cos(angles).reshape(shape)
    sine = jnp.sin(angles).reshape(shape)
    first = values[..., :half]
    second = values[..., half:]
    return jnp.concatenate(
        [first * cosine - second * sine, second * cosine + first * sine], axis=-1
    )


def tenant_lookup(positions, tenant_of_span):
    span_ids = positions // SPAN
    table_index = jnp.arange(tenant_of_span.shape[0], dtype=jnp.int32)
    match = span_ids[:, None] == table_index[None, :]
    return jnp.sum(jnp.where(match, tenant_of_span[None, :], 0), axis=1)


def attend_part(queries, query_pos, query_tenant, keys, values, key_pos, key_tenant):
    scale = 1.0 / math.sqrt(keys.shape[-1])
    scores = jnp.einsum("cgh,sh->gcs", queries, keys, preferred_element_type=jnp.float32) * scale
    gap = query_pos[:, None] - key_pos[None, :]
    allowed = (
        (query_tenant[:, None] == key_tenant[None, :])
        & (gap >= 0)
        & (gap < WINDOW)
        & (key_pos[None, :] >= 0)
    )
    masked = jnp.where(allowed[None], scores, NEG_FILL)
    row_max = jnp.max(masked, axis=2)
    weights = jnp.where(allowed[None], jnp.exp(masked - row_max[..., None]), 0.0)
    totals = jnp.sum(weights, axis=2)
    summed = jnp.einsum(
        "gcs,sh->gch", weights.astype(jnp.bfloat16), values, preferred_element_type=jnp.float32
    )
    return (row_max, totals, summed)


def combine_parts(first, second):
    top = jnp.maximum(first[0], second[0])
    scale_one = jnp.exp(first[0] - top)
    scale_two = jnp.exp(second[0] - top)
    totals = first[1] * scale_one + second[1] * scale_two
    summed = first[2] * scale_one[..., None] + second[2] * scale_two[..., None]
    return summed / totals[..., None]


def ring_pairs(devices, size, stride, shift):
    pairs = []
    for i in range(devices):
        coord = (i // stride) % size
        pairs.append((i, i + ((coord + shift) % size - coord) * stride))
    return pairs


def ring_gather(piece, axis, size, stride):
    devices = lax.axis_size(axis)
    coord = (lax.axis_index(axis) // stride) % size
    by_offset = {0: piece}
    forward = piece
    backward = piece
    for step in range(1, size // 2 + 1):
        forward = lax.ppermute(forward, axis, ring_pairs(devices, size, stride, 1))
        by_offset[(-step) % size] = forward
        if step < size - step:
            backward = lax.ppermute(backward, axis, ring_pairs(devices, size, stride, -1))
            by_offset[step] = backward
    stacked = jnp.stack([by_offset[o] for o in range(size)])
    return jnp.take(stacked, (jnp.arange(size, dtype=jnp.int32) - coord) % size, axis=0)


def group_gather(piece, axis, size):
    devices = lax.axis_size(axis)
    place = lax.axis_index(axis) % size
    pieces = [piece]
    for step in range(1, size):
        pairs = [(i, i - i % size + (i % size + step) % size) for i in range(devices)]
        pieces.append(lax.ppermute(piece, axis, pairs))
    stacked = jnp.stack(pieces)
    order = (place - jnp.arange(size, dtype=jnp.int32)) % size
    return jnp.take(stacked, order, axis=0)


def group_exchange(parts, axis, size):
    devices = lax.axis_size(axis)
    place = lax.axis_index(axis) % size
    mine = [lax.dynamic_index_in_dim(parts, place, 0, keepdims=False)]
    for step in range(1, size):
        pairs = [(i, i - i % size + (i % size + step) % size) for i in range(devices)]
        outgoing = lax.dynamic_index_in_dim(parts, (place + step) % size, 0, keepdims=False)
        mine.append(lax.ppermute(outgoing, axis, pairs))
    return jnp.stack(mine)


def joined_rows(span_order, shard, spans_here, stored_rows):
    local_order = lax.dynamic_slice_in_dim(span_order, shard * spans_here, spans_here, 0)
    local_order = local_order - shard * spans_here
    blocks = jnp.arange(spans_here, dtype=jnp.int32)
    inverse = jnp.sum(
        jnp.where(local_order[None, :] == blocks[:, None], blocks[None, :], 0), axis=1
    )
    slot = jnp.take(inverse, stored_rows // SPAN)
    return shard * spans_here * SPAN + slot * SPAN + stored_rows % SPAN


def local(
    cache_entries,
    recompute_input,
    norm_gain,
    w_query,
    w_keyval,
    w_out,
    rotate_offsets,
    span_order,
    tenant_of_span,
    recompute_pos,
    recompute_count,
):
    blk_count = lax.axis_size("blk")
    kv_index = lax.axis_index("kv")
    blk_index = lax.axis_index("blk")
    block_rows = cache_entries.shape[0]
    shard_len = block_rows * blk_count
    slots = recompute_input.shape[0]
    own_cols = recompute_input.shape[1]
    width = norm_gain.shape[0]
    spans_here = shard_len // SPAN
    group_size = QH // KVH
    pair_cols = w_keyval.shape[1] // blk_count
    member = blk_index % group_size
    group = blk_index // group_size

    rows_each = block_rows // group_size
    w_part = (
        w_keyval.reshape(own_cols, blk_count, pair_cols)
        .transpose(1, 0, 2)
        .reshape(blk_count, own_cols * pair_cols // HEAD_DIM, HEAD_DIM)
    )
    c_part = (
        cache_entries.reshape(group_size, rows_each, KVH, 2 * HEAD_DIM)
        .transpose(2, 0, 1, 3)
        .reshape(blk_count, rows_each * 2, HEAD_DIM)
    )
    w_rows = w_part.shape[1]
    near = ring_gather(recompute_input, "blk", RING_FAST, 1)
    wide = ring_gather(near, "blk", blk_count // RING_FAST, RING_FAST)
    wide = wide.reshape(blk_count, slots, own_cols).astype(jnp.float32)
    moved = lax.all_to_all(jnp.concatenate([w_part, c_part], axis=1), "blk", 0, 0, tiled=True)
    kv_cols = moved[:, :w_rows].reshape(blk_count, own_cols, pair_cols)
    stored = moved[:, w_rows:].reshape(blk_count * rows_each, 2 * HEAD_DIM)

    gains = norm_gain.astype(jnp.float32).reshape(blk_count, 1, own_cols)
    scaled = (wide * gains).astype(jnp.bfloat16)
    square_acc = jnp.sum(wide * wide, axis=(0, 2))
    inv_rms = lax.rsqrt(square_acc / width + NORM_EPS)
    query_acc = jnp.einsum(
        "ksc,kcd->sd",
        scaled,
        w_query.reshape(blk_count, own_cols, HEAD_DIM),
        preferred_element_type=jnp.float32,
    ) * inv_rms[:, None]
    pair_piece = jnp.einsum(
        "ksc,kcd->sd", scaled, kv_cols, preferred_element_type=jnp.float32
    ) * inv_rms[:, None]
    shared = group_gather(jnp.concatenate([query_acc, pair_piece], axis=1), "blk", group_size)
    group_pair = shared[:, :, HEAD_DIM:].transpose(1, 0, 2).reshape(slots, group_size * pair_cols)

    own_pos = lax.dynamic_slice_in_dim(recompute_pos, kv_index * slots, slots, 0)
    own_count = lax.dynamic_index_in_dim(recompute_count, kv_index, 0, keepdims=False)
    live = jnp.arange(slots, dtype=jnp.int32) < own_count
    query_pos = kv_index * shard_len + own_pos
    fresh_keys = rotate_half(group_pair[:, :HEAD_DIM], query_pos).astype(jnp.bfloat16)
    fresh_values = group_pair[:, HEAD_DIM:].astype(jnp.bfloat16)
    queries = rotate_half(shared[:, :, :HEAD_DIM].transpose(1, 0, 2), query_pos).astype(
        jnp.bfloat16
    )

    local_rows = jnp.arange(blk_count * rows_each, dtype=jnp.int32)
    stored_rows = (local_rows // rows_each) * block_rows + member * rows_each + local_rows % rows_each
    key_pos = joined_rows(span_order, kv_index, spans_here, stored_rows)
    offsets = lax.dynamic_slice_in_dim(rotate_offsets, kv_index * spans_here, spans_here, 0)
    row_shifts = jnp.take(offsets, stored_rows // SPAN)
    turned_rows = rotate_half(stored[:, :HEAD_DIM].astype(jnp.float32), row_shifts).astype(
        jnp.bfloat16
    )
    stored = jnp.concatenate([turned_rows, stored[:, HEAD_DIM:]], axis=-1)
    local_order = lax.dynamic_slice_in_dim(span_order, kv_index * spans_here, spans_here, 0)
    slot_rows = (jnp.take(local_order, own_pos // SPAN) - kv_index * spans_here) * SPAN + own_pos % SPAN
    mine = live & ((slot_rows % block_rows) // rows_each == member)
    place = jnp.where(
        mine, (slot_rows // block_rows) * rows_each + slot_rows % rows_each, blk_count * rows_each
    )
    merged = stored.at[place].set(jnp.concatenate([fresh_keys, fresh_values], axis=1), mode="drop")
    query_tenant = tenant_lookup(query_pos, tenant_of_span)
    own_part = attend_part(
        queries,
        query_pos,
        query_tenant,
        merged[:, :HEAD_DIM],
        merged[:, HEAD_DIM:],
        key_pos,
        tenant_lookup(key_pos, tenant_of_span),
    )
    prior = shifted(merged, "kv", 1)
    prior_pos = joined_rows(span_order, jnp.maximum(kv_index - 1, 0), spans_here, stored_rows)
    prior_pos = jnp.where(kv_index > 0, prior_pos, -1)
    prior_part = attend_part(
        queries,
        query_pos,
        query_tenant,
        prior[:, :HEAD_DIM],
        prior[:, HEAD_DIM:],
        prior_pos,
        tenant_lookup(prior_pos, tenant_of_span),
    )
    top = jnp.maximum(own_part[0], prior_part[0])
    scale_own = jnp.exp(own_part[0] - top)
    scale_prior = jnp.exp(prior_part[0] - top)
    totals = own_part[1] * scale_own + prior_part[1] * scale_prior
    summed = own_part[2] * scale_own[..., None] + prior_part[2] * scale_prior[..., None]
    packed = jnp.concatenate([summed, top[..., None], totals[..., None]], axis=-1)
    gathered = group_exchange(packed, "blk", group_size)
    part_max = gathered[:, :, HEAD_DIM]
    best = jnp.max(part_max, axis=0)
    weight = jnp.exp(part_max - best[None])
    total = jnp.sum(gathered[:, :, HEAD_DIM + 1] * weight, axis=0)
    heads_sum = jnp.sum(gathered[:, :, :HEAD_DIM] * weight[..., None], axis=0)
    heads_out = (heads_sum / total[:, None]).astype(jnp.bfloat16)
    term = jnp.dot(heads_out, w_out, preferred_element_type=jnp.float32)
    term_blocks = term.astype(jnp.bfloat16).reshape(slots, blk_count, own_cols)
    arrived_terms = lax.all_to_all(term_blocks, "blk", 1, 1, tiled=True)
    summed_out = jnp.sum(arrived_terms.astype(jnp.float32), axis=1)
    return jnp.where(live[:, None], summed_out, 0.0).astype(jnp.bfloat16)


def solution(mesh):
    placed = (
        P(("kv", "blk"), None, None),
        P("kv", "blk"),
        P(),
        P(None, "blk"),
        P("blk", None),
        P("blk", None),
        P(),
        P(),
        P(),
        P(),
        P(),
    )
    return jax.shard_map(
        local, mesh=mesh, in_specs=placed, out_specs=P("kv", "blk"), check_vma=False
    )
```

```python
import math

import jax
import jax.numpy as jnp
import numpy as np
from jax import lax
from jax.sharding import PartitionSpec as P

QH = 32
KVH = 8
HEAD_DIM = 128
WINDOW = 4096
SPAN = 1024


NEG_FILL = -1e30
ROPE_BASE = 10000.0
NORM_EPS = 1e-05


def shifted(shard, axis, by):
    devices = lax.axis_size(axis)
    pairs = [(i, i + by) for i in range(devices) if 0 <= i + by < devices]
    return lax.ppermute(shard, axis, pairs)


def rotate_half(values, positions):
    half = values.shape[-1] // 2
    inverse = ROPE_BASE ** (-(jnp.arange(half, dtype=jnp.float32) * 2.0 / values.shape[-1]))
    angles = positions.astype(jnp.float32)[:, None] * inverse[None, :]
    shape = (positions.shape[0],) + (1,) * (values.ndim - 2) + (half,)
    cosine = jnp.cos(angles).reshape(shape)
    sine = jnp.sin(angles).reshape(shape)
    first = values[..., :half]
    second = values[..., half:]
    return jnp.concatenate(
        [first * cosine - second * sine, second * cosine + first * sine], axis=-1
    )


def tenant_lookup(positions, tenant_of_span):
    span_ids = positions // SPAN
    table_index = jnp.arange(tenant_of_span.shape[0], dtype=jnp.int32)
    match = span_ids[:, None] == table_index[None, :]
    return jnp.sum(jnp.where(match, tenant_of_span[None, :], 0), axis=1)


def attend_part(queries, query_pos, query_tenant, keys, values, key_pos, key_tenant):
    scale = 1.0 / math.sqrt(keys.shape[-1])
    scores = jnp.einsum("cgh,sh->gcs", queries, keys, preferred_element_type=jnp.float32) * scale
    gap = query_pos[:, None] - key_pos[None, :]
    allowed = (
        (query_tenant[:, None] == key_tenant[None, :])
        & (gap >= 0)
        & (gap < WINDOW)
        & (key_pos[None, :] >= 0)
    )
    masked = jnp.where(allowed[None], scores, NEG_FILL)
    row_max = jnp.max(masked, axis=2)
    weights = jnp.where(allowed[None], jnp.exp(masked - row_max[..., None]), 0.0)
    totals = jnp.sum(weights, axis=2)
    summed = jnp.einsum(
        "gcs,sh->gch", weights.astype(jnp.bfloat16), values, preferred_element_type=jnp.float32
    )
    return (row_max, totals, summed)


def combine_parts(first, second):
    top = jnp.maximum(first[0], second[0])
    scale_one = jnp.exp(first[0] - top)
    scale_two = jnp.exp(second[0] - top)
    totals = first[1] * scale_one + second[1] * scale_two
    summed = first[2] * scale_one[..., None] + second[2] * scale_two[..., None]
    return summed / totals[..., None]


def member_groups(devices, size):
    return [list(range(start, start + size)) for start in range(0, devices, size)]


def group_gather(piece, axis, size):
    spread = jnp.broadcast_to(piece[None], (size,) + piece.shape)
    groups = member_groups(lax.axis_size(axis), size)
    return lax.all_to_all(spread, axis, 0, 0, axis_index_groups=groups, tiled=True)


def group_exchange(parts, axis, size):
    groups = member_groups(lax.axis_size(axis), size)
    return lax.all_to_all(parts, axis, 0, 0, axis_index_groups=groups, tiled=True)


def joined_rows(span_order, shard, spans_here, stored_rows):
    local_order = lax.dynamic_slice_in_dim(span_order, shard * spans_here, spans_here, 0)
    local_order = local_order - shard * spans_here
    blocks = jnp.arange(spans_here, dtype=jnp.int32)
    inverse = jnp.sum(
        jnp.where(local_order[None, :] == blocks[:, None], blocks[None, :], 0), axis=1
    )
    slot = jnp.take(inverse, stored_rows // SPAN)
    return shard * spans_here * SPAN + slot * SPAN + stored_rows % SPAN


def local(
    cache_entries,
    recompute_input,
    norm_gain,
    w_query,
    w_keyval,
    w_out,
    rotate_offsets,
    span_order,
    tenant_of_span,
    recompute_pos,
    recompute_count,
):
    blk_count = lax.axis_size("blk")
    kv_index = lax.axis_index("kv")
    blk_index = lax.axis_index("blk")
    block_rows = cache_entries.shape[0]
    shard_len = block_rows * blk_count
    slots = recompute_input.shape[0]
    own_cols = recompute_input.shape[1]
    width = norm_gain.shape[0]
    spans_here = shard_len // SPAN
    group_size = QH // KVH
    pair_cols = w_keyval.shape[1] // blk_count
    member = blk_index % group_size
    group = blk_index // group_size

    rows_each = block_rows // group_size
    x_part = jnp.broadcast_to(recompute_input[None], (blk_count, slots, own_cols))
    w_part = (
        w_keyval.reshape(own_cols, blk_count, pair_cols)
        .transpose(1, 0, 2)
        .reshape(blk_count, own_cols * pair_cols // HEAD_DIM, HEAD_DIM)
    )
    c_part = (
        cache_entries.reshape(group_size, rows_each, KVH, 2 * HEAD_DIM)
        .transpose(2, 0, 1, 3)
        .reshape(blk_count, rows_each * 2, HEAD_DIM)
    )
    arrived = lax.all_to_all(jnp.concatenate([x_part, w_part], axis=1), "blk", 0, 0, tiled=True)
    wide = arrived[:, :slots].astype(jnp.float32)
    kv_cols = arrived[:, slots:].reshape(blk_count, own_cols, pair_cols)
    arrived, c_part = lax.optimization_barrier((arrived, c_part))
    stored = lax.all_to_all(c_part, "blk", 0, 0, tiled=True).reshape(
        blk_count * rows_each, 2 * HEAD_DIM
    )

    gains = norm_gain.astype(jnp.float32).reshape(blk_count, 1, own_cols)
    scaled = (wide * gains).astype(jnp.bfloat16)
    square_acc = jnp.sum(wide * wide, axis=(0, 2))
    inv_rms = lax.rsqrt(square_acc / width + NORM_EPS)
    query_acc = jnp.einsum(
        "ksc,kcd->sd",
        scaled,
        w_query.reshape(blk_count, own_cols, HEAD_DIM),
        preferred_element_type=jnp.float32,
    ) * inv_rms[:, None]
    pair_piece = jnp.einsum(
        "ksc,kcd->sd", scaled, kv_cols, preferred_element_type=jnp.float32
    ) * inv_rms[:, None]
    shared = group_gather(jnp.concatenate([query_acc, pair_piece], axis=1), "blk", group_size)
    group_pair = shared[:, :, HEAD_DIM:].transpose(1, 0, 2).reshape(slots, group_size * pair_cols)

    own_pos = lax.dynamic_slice_in_dim(recompute_pos, kv_index * slots, slots, 0)
    own_count = lax.dynamic_index_in_dim(recompute_count, kv_index, 0, keepdims=False)
    live = jnp.arange(slots, dtype=jnp.int32) < own_count
    query_pos = kv_index * shard_len + own_pos
    fresh_keys = rotate_half(group_pair[:, :HEAD_DIM], query_pos).astype(jnp.bfloat16)
    fresh_values = group_pair[:, HEAD_DIM:].astype(jnp.bfloat16)
    queries = rotate_half(shared[:, :, :HEAD_DIM].transpose(1, 0, 2), query_pos).astype(
        jnp.bfloat16
    )

    local_rows = jnp.arange(blk_count * rows_each, dtype=jnp.int32)
    stored_rows = (local_rows // rows_each) * block_rows + member * rows_each + local_rows % rows_each
    key_pos = joined_rows(span_order, kv_index, spans_here, stored_rows)
    offsets = lax.dynamic_slice_in_dim(rotate_offsets, kv_index * spans_here, spans_here, 0)
    row_shifts = jnp.take(offsets, stored_rows // SPAN)
    turned_rows = rotate_half(stored[:, :HEAD_DIM].astype(jnp.float32), row_shifts).astype(
        jnp.bfloat16
    )
    stored = jnp.concatenate([turned_rows, stored[:, HEAD_DIM:]], axis=-1)
    local_order = lax.dynamic_slice_in_dim(span_order, kv_index * spans_here, spans_here, 0)
    slot_rows = (jnp.take(local_order, own_pos // SPAN) - kv_index * spans_here) * SPAN + own_pos % SPAN
    mine = live & ((slot_rows % block_rows) // rows_each == member)
    place = jnp.where(
        mine, (slot_rows // block_rows) * rows_each + slot_rows % rows_each, blk_count * rows_each
    )
    merged = stored.at[place].set(jnp.concatenate([fresh_keys, fresh_values], axis=1), mode="drop")
    query_tenant = tenant_lookup(query_pos, tenant_of_span)
    own_part = attend_part(
        queries,
        query_pos,
        query_tenant,
        merged[:, :HEAD_DIM],
        merged[:, HEAD_DIM:],
        key_pos,
        tenant_lookup(key_pos, tenant_of_span),
    )
    prior = shifted(merged, "kv", 1)
    prior_pos = joined_rows(span_order, jnp.maximum(kv_index - 1, 0), spans_here, stored_rows)
    prior_pos = jnp.where(kv_index > 0, prior_pos, -1)
    prior_part = attend_part(
        queries,
        query_pos,
        query_tenant,
        prior[:, :HEAD_DIM],
        prior[:, HEAD_DIM:],
        prior_pos,
        tenant_lookup(prior_pos, tenant_of_span),
    )
    top = jnp.maximum(own_part[0], prior_part[0])
    scale_own = jnp.exp(own_part[0] - top)
    scale_prior = jnp.exp(prior_part[0] - top)
    totals = own_part[1] * scale_own + prior_part[1] * scale_prior
    summed = own_part[2] * scale_own[..., None] + prior_part[2] * scale_prior[..., None]
    packed = jnp.concatenate([summed, top[..., None], totals[..., None]], axis=-1)
    gathered = group_exchange(packed, "blk", group_size)
    part_max = gathered[:, :, HEAD_DIM]
    best = jnp.max(part_max, axis=0)
    weight = jnp.exp(part_max - best[None])
    total = jnp.sum(gathered[:, :, HEAD_DIM + 1] * weight, axis=0)
    heads_sum = jnp.sum(gathered[:, :, :HEAD_DIM] * weight[..., None], axis=0)
    heads_out = (heads_sum / total[:, None]).astype(jnp.bfloat16)
    term = jnp.dot(heads_out, w_out, preferred_element_type=jnp.float32)
    term_blocks = term.astype(jnp.bfloat16).reshape(slots, blk_count, own_cols)
    arrived_terms = lax.all_to_all(term_blocks, "blk", 1, 1, tiled=True)
    summed_out = jnp.sum(arrived_terms.astype(jnp.float32), axis=1)
    return jnp.where(live[:, None], summed_out, 0.0).astype(jnp.bfloat16)


def solution(mesh):
    placed = (
        P(("kv", "blk"), None, None),
        P("kv", "blk"),
        P(),
        P(None, "blk"),
        P("blk", None),
        P("blk", None),
        P(),
        P(),
        P(),
        P(),
        P(),
    )
    return jax.shard_map(
        local, mesh=mesh, in_specs=placed, out_specs=P("kv", "blk"), check_vma=False
    )
```

```python
import math

import jax
import jax.numpy as jnp
import numpy as np
from jax import lax
from jax.sharding import PartitionSpec as P

QH = 32
KVH = 8
HEAD_DIM = 128
WINDOW = 4096
SPAN = 1024


NEG_FILL = -1e30
ROPE_BASE = 10000.0
NORM_EPS = 1e-05


def shifted(shard, axis, by):
    devices = lax.axis_size(axis)
    pairs = [(i, i + by) for i in range(devices) if 0 <= i + by < devices]
    return lax.ppermute(shard, axis, pairs)


def rotate_half(values, positions):
    half = values.shape[-1] // 2
    inverse = ROPE_BASE ** (-(jnp.arange(half, dtype=jnp.float32) * 2.0 / values.shape[-1]))
    angles = positions.astype(jnp.float32)[:, None] * inverse[None, :]
    shape = (positions.shape[0],) + (1,) * (values.ndim - 2) + (half,)
    cosine = jnp.cos(angles).reshape(shape)
    sine = jnp.sin(angles).reshape(shape)
    first = values[..., :half]
    second = values[..., half:]
    return jnp.concatenate(
        [first * cosine - second * sine, second * cosine + first * sine], axis=-1
    )


def tenant_lookup(positions, tenant_of_span):
    span_ids = positions // SPAN
    table_index = jnp.arange(tenant_of_span.shape[0], dtype=jnp.int32)
    match = span_ids[:, None] == table_index[None, :]
    return jnp.sum(jnp.where(match, tenant_of_span[None, :], 0), axis=1)


def attend_part(queries, query_pos, query_tenant, keys, values, key_pos, key_tenant):
    scale = 1.0 / math.sqrt(keys.shape[-1])
    scores = jnp.einsum("cgh,sh->gcs", queries, keys, preferred_element_type=jnp.float32) * scale
    gap = query_pos[:, None] - key_pos[None, :]
    allowed = (
        (query_tenant[:, None] == key_tenant[None, :])
        & (gap >= 0)
        & (gap < WINDOW)
        & (key_pos[None, :] >= 0)
    )
    masked = jnp.where(allowed[None], scores, NEG_FILL)
    row_max = jnp.max(masked, axis=2)
    weights = jnp.where(allowed[None], jnp.exp(masked - row_max[..., None]), 0.0)
    totals = jnp.sum(weights, axis=2)
    summed = jnp.einsum(
        "gcs,sh->gch", weights.astype(jnp.bfloat16), values, preferred_element_type=jnp.float32
    )
    return (row_max, totals, summed)


def combine_parts(first, second):
    top = jnp.maximum(first[0], second[0])
    scale_one = jnp.exp(first[0] - top)
    scale_two = jnp.exp(second[0] - top)
    totals = first[1] * scale_one + second[1] * scale_two
    summed = first[2] * scale_one[..., None] + second[2] * scale_two[..., None]
    return summed / totals[..., None]


def member_groups(devices, size):
    return [list(range(start, start + size)) for start in range(0, devices, size)]


def group_gather(piece, axis, size):
    spread = jnp.broadcast_to(piece[None], (size,) + piece.shape)
    groups = member_groups(lax.axis_size(axis), size)
    return lax.all_to_all(spread, axis, 0, 0, axis_index_groups=groups, tiled=True)


def group_exchange(parts, axis, size):
    groups = member_groups(lax.axis_size(axis), size)
    return lax.all_to_all(parts, axis, 0, 0, axis_index_groups=groups, tiled=True)


def joined_rows(span_order, shard, spans_here, stored_rows):
    local_order = lax.dynamic_slice_in_dim(span_order, shard * spans_here, spans_here, 0)
    local_order = local_order - shard * spans_here
    blocks = jnp.arange(spans_here, dtype=jnp.int32)
    inverse = jnp.sum(
        jnp.where(local_order[None, :] == blocks[:, None], blocks[None, :], 0), axis=1
    )
    slot = jnp.take(inverse, stored_rows // SPAN)
    return shard * spans_here * SPAN + slot * SPAN + stored_rows % SPAN


def local(
    cache_entries,
    recompute_input,
    norm_gain,
    w_query,
    w_keyval,
    w_out,
    rotate_offsets,
    span_order,
    tenant_of_span,
    recompute_pos,
    recompute_count,
):
    blk_count = lax.axis_size("blk")
    kv_index = lax.axis_index("kv")
    blk_index = lax.axis_index("blk")
    block_rows = cache_entries.shape[0]
    shard_len = block_rows * blk_count
    slots = recompute_input.shape[0]
    own_cols = recompute_input.shape[1]
    width = norm_gain.shape[0]
    spans_here = shard_len // SPAN
    group_size = QH // KVH
    pair_cols = w_keyval.shape[1] // blk_count
    member = blk_index % group_size
    group = blk_index // group_size

    rows_each = block_rows // group_size
    x_part = jnp.broadcast_to(recompute_input[None], (blk_count, slots, own_cols))
    w_part = (
        w_keyval.reshape(own_cols, blk_count, pair_cols)
        .transpose(1, 0, 2)
        .reshape(blk_count, own_cols * pair_cols // HEAD_DIM, HEAD_DIM)
    )
    c_part = (
        cache_entries.reshape(group_size, rows_each, KVH, 2 * HEAD_DIM)
        .transpose(2, 0, 1, 3)
        .reshape(blk_count, rows_each * 2, HEAD_DIM)
    )
    arrived = lax.all_to_all(x_part, "blk", 0, 0, tiled=True)
    wide = arrived.astype(jnp.float32)
    arrived, w_part, c_part = lax.optimization_barrier((arrived, w_part, c_part))
    w_rows = w_part.shape[1]
    moved = lax.all_to_all(jnp.concatenate([w_part, c_part], axis=1), "blk", 0, 0, tiled=True)
    kv_cols = moved[:, :w_rows].reshape(blk_count, own_cols, pair_cols)
    stored = moved[:, w_rows:].reshape(blk_count * rows_each, 2 * HEAD_DIM)

    gains = norm_gain.astype(jnp.float32).reshape(blk_count, 1, own_cols)
    scaled = (wide * gains).astype(jnp.bfloat16)
    square_acc = jnp.sum(wide * wide, axis=(0, 2))
    inv_rms = lax.rsqrt(square_acc / width + NORM_EPS)
    query_acc = jnp.einsum(
        "ksc,kcd->sd",
        scaled,
        w_query.reshape(blk_count, own_cols, HEAD_DIM),
        preferred_element_type=jnp.float32,
    ) * inv_rms[:, None]
    pair_piece = jnp.einsum(
        "ksc,kcd->sd", scaled, kv_cols, preferred_element_type=jnp.float32
    ) * inv_rms[:, None]
    shared = group_gather(jnp.concatenate([query_acc, pair_piece], axis=1), "blk", group_size)
    group_pair = shared[:, :, HEAD_DIM:].transpose(1, 0, 2).reshape(slots, group_size * pair_cols)

    own_pos = lax.dynamic_slice_in_dim(recompute_pos, kv_index * slots, slots, 0)
    own_count = lax.dynamic_index_in_dim(recompute_count, kv_index, 0, keepdims=False)
    live = jnp.arange(slots, dtype=jnp.int32) < own_count
    query_pos = kv_index * shard_len + own_pos
    fresh_keys = rotate_half(group_pair[:, :HEAD_DIM], query_pos).astype(jnp.bfloat16)
    fresh_values = group_pair[:, HEAD_DIM:].astype(jnp.bfloat16)
    queries = rotate_half(shared[:, :, :HEAD_DIM].transpose(1, 0, 2), query_pos).astype(
        jnp.bfloat16
    )

    local_rows = jnp.arange(blk_count * rows_each, dtype=jnp.int32)
    stored_rows = (local_rows // rows_each) * block_rows + member * rows_each + local_rows % rows_each
    key_pos = joined_rows(span_order, kv_index, spans_here, stored_rows)
    offsets = lax.dynamic_slice_in_dim(rotate_offsets, kv_index * spans_here, spans_here, 0)
    row_shifts = jnp.take(offsets, stored_rows // SPAN)
    turned_rows = rotate_half(stored[:, :HEAD_DIM].astype(jnp.float32), row_shifts).astype(
        jnp.bfloat16
    )
    stored = jnp.concatenate([turned_rows, stored[:, HEAD_DIM:]], axis=-1)
    local_order = lax.dynamic_slice_in_dim(span_order, kv_index * spans_here, spans_here, 0)
    slot_rows = (jnp.take(local_order, own_pos // SPAN) - kv_index * spans_here) * SPAN + own_pos % SPAN
    mine = live & ((slot_rows % block_rows) // rows_each == member)
    place = jnp.where(
        mine, (slot_rows // block_rows) * rows_each + slot_rows % rows_each, blk_count * rows_each
    )
    merged = stored.at[place].set(jnp.concatenate([fresh_keys, fresh_values], axis=1), mode="drop")
    query_tenant = tenant_lookup(query_pos, tenant_of_span)
    own_part = attend_part(
        queries,
        query_pos,
        query_tenant,
        merged[:, :HEAD_DIM],
        merged[:, HEAD_DIM:],
        key_pos,
        tenant_lookup(key_pos, tenant_of_span),
    )
    prior = shifted(merged, "kv", 1)
    prior_pos = joined_rows(span_order, jnp.maximum(kv_index - 1, 0), spans_here, stored_rows)
    prior_pos = jnp.where(kv_index > 0, prior_pos, -1)
    prior_part = attend_part(
        queries,
        query_pos,
        query_tenant,
        prior[:, :HEAD_DIM],
        prior[:, HEAD_DIM:],
        prior_pos,
        tenant_lookup(prior_pos, tenant_of_span),
    )
    top = jnp.maximum(own_part[0], prior_part[0])
    scale_own = jnp.exp(own_part[0] - top)
    scale_prior = jnp.exp(prior_part[0] - top)
    totals = own_part[1] * scale_own + prior_part[1] * scale_prior
    summed = own_part[2] * scale_own[..., None] + prior_part[2] * scale_prior[..., None]
    packed = jnp.concatenate([summed, top[..., None], totals[..., None]], axis=-1)
    gathered = group_exchange(packed, "blk", group_size)
    part_max = gathered[:, :, HEAD_DIM]
    best = jnp.max(part_max, axis=0)
    weight = jnp.exp(part_max - best[None])
    total = jnp.sum(gathered[:, :, HEAD_DIM + 1] * weight, axis=0)
    heads_sum = jnp.sum(gathered[:, :, :HEAD_DIM] * weight[..., None], axis=0)
    heads_out = (heads_sum / total[:, None]).astype(jnp.bfloat16)
    term = jnp.einsum(
        "ch,hkd->kcd",
        heads_out,
        w_out.reshape(HEAD_DIM, blk_count, own_cols),
        preferred_element_type=jnp.float32,
    )
    arrived_terms = lax.all_to_all(term.astype(jnp.bfloat16), "blk", 0, 0, tiled=True)
    summed_out = jnp.sum(arrived_terms.astype(jnp.float32), axis=0)
    return jnp.where(live[:, None], summed_out, 0.0).astype(jnp.bfloat16)


def solution(mesh):
    placed = (
        P(("kv", "blk"), None, None),
        P("kv", "blk"),
        P(),
        P(None, "blk"),
        P("blk", None),
        P("blk", None),
        P(),
        P(),
        P(),
        P(),
        P(),
    )
    return jax.shard_map(
        local, mesh=mesh, in_specs=placed, out_specs=P("kv", "blk"), check_vma=False
    )
```

```python
import math

import jax
import jax.numpy as jnp
import numpy as np
from jax import lax
from jax.sharding import PartitionSpec as P

QH = 32
KVH = 8
HEAD_DIM = 128
WINDOW = 4096
SPAN = 1024


NEG_FILL = -1e30
ROPE_BASE = 10000.0
NORM_EPS = 1e-05


def shifted(shard, axis, by):
    devices = lax.axis_size(axis)
    pairs = [(i, i + by) for i in range(devices) if 0 <= i + by < devices]
    return lax.ppermute(shard, axis, pairs)


def rotate_half(values, positions):
    half = values.shape[-1] // 2
    inverse = ROPE_BASE ** (-(jnp.arange(half, dtype=jnp.float32) * 2.0 / values.shape[-1]))
    angles = positions.astype(jnp.float32)[:, None] * inverse[None, :]
    shape = (positions.shape[0],) + (1,) * (values.ndim - 2) + (half,)
    cosine = jnp.cos(angles).reshape(shape)
    sine = jnp.sin(angles).reshape(shape)
    first = values[..., :half]
    second = values[..., half:]
    return jnp.concatenate(
        [first * cosine - second * sine, second * cosine + first * sine], axis=-1
    )


def tenant_lookup(positions, tenant_of_span):
    span_ids = positions // SPAN
    table_index = jnp.arange(tenant_of_span.shape[0], dtype=jnp.int32)
    match = span_ids[:, None] == table_index[None, :]
    return jnp.sum(jnp.where(match, tenant_of_span[None, :], 0), axis=1)


def attend_part(queries, query_pos, query_tenant, keys, values, key_pos, key_tenant):
    scale = 1.0 / math.sqrt(keys.shape[-1])
    scores = jnp.einsum("cgh,sh->gcs", queries, keys, preferred_element_type=jnp.float32) * scale
    gap = query_pos[:, None] - key_pos[None, :]
    allowed = (
        (query_tenant[:, None] == key_tenant[None, :])
        & (gap >= 0)
        & (gap < WINDOW)
        & (key_pos[None, :] >= 0)
    )
    masked = jnp.where(allowed[None], scores, NEG_FILL)
    row_max = jnp.max(masked, axis=2)
    weights = jnp.where(allowed[None], jnp.exp(masked - row_max[..., None]), 0.0)
    totals = jnp.sum(weights, axis=2)
    summed = jnp.einsum(
        "gcs,sh->gch", weights.astype(jnp.bfloat16), values, preferred_element_type=jnp.float32
    )
    return (row_max, totals, summed)


def combine_parts(first, second):
    top = jnp.maximum(first[0], second[0])
    scale_one = jnp.exp(first[0] - top)
    scale_two = jnp.exp(second[0] - top)
    totals = first[1] * scale_one + second[1] * scale_two
    summed = first[2] * scale_one[..., None] + second[2] * scale_two[..., None]
    return summed / totals[..., None]


def split_wide(values):
    high = values.astype(jnp.bfloat16)
    low = (values - high.astype(jnp.float32)).astype(jnp.bfloat16)
    return high, low


def member_groups(devices, size):
    return [list(range(start, start + size)) for start in range(0, devices, size)]


def group_gather(piece, axis, size):
    spread = jnp.broadcast_to(piece[None], (size,) + piece.shape)
    groups = member_groups(lax.axis_size(axis), size)
    return lax.all_to_all(spread, axis, 0, 0, axis_index_groups=groups, tiled=True)


def group_exchange(parts, axis, size):
    groups = member_groups(lax.axis_size(axis), size)
    return lax.all_to_all(parts, axis, 0, 0, axis_index_groups=groups, tiled=True)


def joined_rows(span_order, shard, spans_here, stored_rows):
    local_order = lax.dynamic_slice_in_dim(span_order, shard * spans_here, spans_here, 0)
    local_order = local_order - shard * spans_here
    blocks = jnp.arange(spans_here, dtype=jnp.int32)
    inverse = jnp.sum(
        jnp.where(local_order[None, :] == blocks[:, None], blocks[None, :], 0), axis=1
    )
    slot = jnp.take(inverse, stored_rows // SPAN)
    return shard * spans_here * SPAN + slot * SPAN + stored_rows % SPAN


def local(
    cache_entries,
    recompute_input,
    norm_gain,
    w_query,
    w_keyval,
    w_out,
    rotate_offsets,
    span_order,
    tenant_of_span,
    recompute_pos,
    recompute_count,
):
    blk_count = lax.axis_size("blk")
    kv_index = lax.axis_index("kv")
    blk_index = lax.axis_index("blk")
    block_rows = cache_entries.shape[0]
    shard_len = block_rows * blk_count
    slots = recompute_input.shape[0]
    own_cols = recompute_input.shape[1]
    width = norm_gain.shape[0]
    spans_here = shard_len // SPAN
    group_size = QH // KVH
    pair_cols = w_keyval.shape[1] // blk_count
    member = blk_index % group_size
    group = blk_index // group_size

    rows_each = block_rows // group_size
    x_part = jnp.broadcast_to(recompute_input[None], (blk_count, slots, own_cols))
    quarter = pair_cols // 2
    key_members = HEAD_DIM // pair_cols
    groups_w = w_keyval.reshape(own_cols, KVH, 2 * HEAD_DIM)
    sorted_w = []
    for m in range(key_members):
        sorted_w.append(groups_w[:, :, m * quarter : (m + 1) * quarter])
        second = HEAD_DIM // 2 + m * quarter
        sorted_w.append(groups_w[:, :, second : second + quarter])
    sorted_w.append(groups_w[:, :, HEAD_DIM:])
    w_part = (
        jnp.concatenate(sorted_w, axis=2)
        .reshape(own_cols, blk_count, pair_cols)
        .transpose(1, 0, 2)
        .reshape(blk_count, own_cols * pair_cols // HEAD_DIM, HEAD_DIM)
    )
    c_part = (
        cache_entries.reshape(group_size, rows_each, KVH, 2 * HEAD_DIM)
        .transpose(2, 0, 1, 3)
        .reshape(blk_count, rows_each * 2, HEAD_DIM)
    )
    arrived = lax.all_to_all(x_part, "blk", 0, 0, tiled=True)
    wide = arrived.astype(jnp.float32)
    arrived, w_part, c_part = lax.optimization_barrier((arrived, w_part, c_part))
    w_rows = w_part.shape[1]
    moved = lax.all_to_all(jnp.concatenate([w_part, c_part], axis=1), "blk", 0, 0, tiled=True)
    kv_cols = moved[:, :w_rows].reshape(blk_count, own_cols, pair_cols)
    stored = moved[:, w_rows:].reshape(blk_count * rows_each, 2 * HEAD_DIM)

    gains = norm_gain.astype(jnp.float32).reshape(blk_count, 1, own_cols)
    scaled = (wide * gains).astype(jnp.bfloat16)
    square_acc = jnp.sum(wide * wide, axis=(0, 2))
    inv_rms = lax.rsqrt(square_acc / width + NORM_EPS)
    query_acc = jnp.einsum(
        "ksc,kcd->sd",
        scaled,
        w_query.reshape(blk_count, own_cols, HEAD_DIM),
        preferred_element_type=jnp.float32,
    ) * inv_rms[:, None]
    pair_piece = jnp.einsum(
        "ksc,kcd->sd", scaled, kv_cols, preferred_element_type=jnp.float32
    ) * inv_rms[:, None]
    own_pos = lax.dynamic_slice_in_dim(recompute_pos, kv_index * slots, slots, 0)
    own_count = lax.dynamic_index_in_dim(recompute_count, kv_index, 0, keepdims=False)
    live = jnp.arange(slots, dtype=jnp.int32) < own_count
    query_pos = kv_index * shard_len + own_pos
    own_query = rotate_half(query_acc.reshape(slots, 1, HEAD_DIM), query_pos)
    own_query = own_query.astype(jnp.bfloat16).reshape(slots, HEAD_DIM)
    inverse = ROPE_BASE ** (
        -(jnp.arange(HEAD_DIM // 2, dtype=jnp.float32) * 2.0 / HEAD_DIM)
    )
    freq = lax.dynamic_slice_in_dim(inverse, (member % key_members) * quarter, quarter, 0)
    angles = query_pos.astype(jnp.float32)[:, None] * freq[None, :]
    cosine = jnp.cos(angles)
    sine = jnp.sin(angles)
    first = pair_piece[:, :quarter]
    second = pair_piece[:, quarter:]
    turned = jnp.concatenate([first * cosine - second * sine, second * cosine + first * sine], axis=1)
    own_piece = jnp.where(member < key_members, turned, pair_piece).astype(jnp.bfloat16)
    shared = group_gather(jnp.concatenate([own_query, own_piece], axis=1), "blk", group_size)
    queries = shared[:, :, :HEAD_DIM].transpose(1, 0, 2)
    pieces = shared[:, :, HEAD_DIM:]
    fresh_keys = jnp.concatenate(
        [pieces[m, :, :quarter] for m in range(key_members)]
        + [pieces[m, :, quarter:] for m in range(key_members)],
        axis=1,
    )
    fresh_values = jnp.concatenate([pieces[m] for m in range(key_members, group_size)], axis=1)

    local_rows = jnp.arange(blk_count * rows_each, dtype=jnp.int32)
    stored_rows = (local_rows // rows_each) * block_rows + member * rows_each + local_rows % rows_each
    key_pos = joined_rows(span_order, kv_index, spans_here, stored_rows)
    offsets = lax.dynamic_slice_in_dim(rotate_offsets, kv_index * spans_here, spans_here, 0)
    row_shifts = jnp.take(offsets, stored_rows // SPAN)
    turned_rows = rotate_half(stored[:, :HEAD_DIM].astype(jnp.float32), row_shifts).astype(
        jnp.bfloat16
    )
    stored = jnp.concatenate([turned_rows, stored[:, HEAD_DIM:]], axis=-1)
    local_order = lax.dynamic_slice_in_dim(span_order, kv_index * spans_here, spans_here, 0)
    slot_rows = (jnp.take(local_order, own_pos // SPAN) - kv_index * spans_here) * SPAN + own_pos % SPAN
    mine = live & ((slot_rows % block_rows) // rows_each == member)
    place = jnp.where(
        mine, (slot_rows // block_rows) * rows_each + slot_rows % rows_each, blk_count * rows_each
    )
    merged = stored.at[place].set(jnp.concatenate([fresh_keys, fresh_values], axis=1), mode="drop")
    query_tenant = tenant_lookup(query_pos, tenant_of_span)
    own_part = attend_part(
        queries,
        query_pos,
        query_tenant,
        merged[:, :HEAD_DIM],
        merged[:, HEAD_DIM:],
        key_pos,
        tenant_lookup(key_pos, tenant_of_span),
    )
    prior = shifted(merged, "kv", 1)
    prior_pos = joined_rows(span_order, jnp.maximum(kv_index - 1, 0), spans_here, stored_rows)
    prior_pos = jnp.where(kv_index > 0, prior_pos, -1)
    prior_part = attend_part(
        queries,
        query_pos,
        query_tenant,
        prior[:, :HEAD_DIM],
        prior[:, HEAD_DIM:],
        prior_pos,
        tenant_lookup(prior_pos, tenant_of_span),
    )
    top = jnp.maximum(own_part[0], prior_part[0])
    scale_own = jnp.exp(own_part[0] - top)
    scale_prior = jnp.exp(prior_part[0] - top)
    totals = own_part[1] * scale_own + prior_part[1] * scale_prior
    summed = own_part[2] * scale_own[..., None] + prior_part[2] * scale_prior[..., None]
    top_hi, top_lo = split_wide(top)
    total_hi, total_lo = split_wide(totals)
    packed = jnp.concatenate(
        [summed.astype(jnp.bfloat16)] + [v[..., None] for v in (top_hi, top_lo, total_hi, total_lo)],
        axis=-1,
    )
    gathered = group_exchange(packed, "blk", group_size).astype(jnp.float32)
    part_max = gathered[:, :, HEAD_DIM] + gathered[:, :, HEAD_DIM + 1]
    part_total = gathered[:, :, HEAD_DIM + 2] + gathered[:, :, HEAD_DIM + 3]
    best = jnp.max(part_max, axis=0)
    weight = jnp.exp(part_max - best[None])
    total = jnp.sum(part_total * weight, axis=0)
    heads_sum = jnp.sum(gathered[:, :, :HEAD_DIM] * weight[..., None], axis=0)
    heads_out = (heads_sum / total[:, None]).astype(jnp.bfloat16)
    term = jnp.einsum(
        "ch,hkd->kcd",
        heads_out,
        w_out.reshape(HEAD_DIM, blk_count, own_cols),
        preferred_element_type=jnp.float32,
    )
    arrived_terms = lax.all_to_all(term.astype(jnp.bfloat16), "blk", 0, 0, tiled=True)
    summed_out = jnp.sum(arrived_terms.astype(jnp.float32), axis=0)
    return jnp.where(live[:, None], summed_out, 0.0).astype(jnp.bfloat16)


def solution(mesh):
    placed = (
        P(("kv", "blk"), None, None),
        P("kv", "blk"),
        P(),
        P(None, "blk"),
        P("blk", None),
        P("blk", None),
        P(),
        P(),
        P(),
        P(),
        P(),
    )
    return jax.shard_map(
        local, mesh=mesh, in_specs=placed, out_specs=P("kv", "blk"), check_vma=False
    )
```

```python
import math

import jax
import jax.numpy as jnp
import numpy as np
from jax import lax
from jax.sharding import PartitionSpec as P

QH = 32
KVH = 8
HEAD_DIM = 128
WINDOW = 4096
SPAN = 1024


NEG_FILL = -1e30
ROPE_BASE = 10000.0
NORM_EPS = 1e-05


def shifted(shard, axis, by):
    devices = lax.axis_size(axis)
    pairs = [(i, i + by) for i in range(devices) if 0 <= i + by < devices]
    return lax.ppermute(shard, axis, pairs)


def rotate_half(values, positions):
    half = values.shape[-1] // 2
    inverse = ROPE_BASE ** (-(jnp.arange(half, dtype=jnp.float32) * 2.0 / values.shape[-1]))
    angles = positions.astype(jnp.float32)[:, None] * inverse[None, :]
    shape = (positions.shape[0],) + (1,) * (values.ndim - 2) + (half,)
    cosine = jnp.cos(angles).reshape(shape)
    sine = jnp.sin(angles).reshape(shape)
    first = values[..., :half]
    second = values[..., half:]
    return jnp.concatenate(
        [first * cosine - second * sine, second * cosine + first * sine], axis=-1
    )


def tenant_lookup(positions, tenant_of_span):
    span_ids = positions // SPAN
    table_index = jnp.arange(tenant_of_span.shape[0], dtype=jnp.int32)
    match = span_ids[:, None] == table_index[None, :]
    return jnp.sum(jnp.where(match, tenant_of_span[None, :], 0), axis=1)


def attend_part(queries, query_pos, query_tenant, keys, values, key_pos, key_tenant):
    scale = 1.0 / math.sqrt(keys.shape[-1])
    scores = jnp.einsum("cgh,sh->gcs", queries, keys, preferred_element_type=jnp.float32) * scale
    gap = query_pos[:, None] - key_pos[None, :]
    allowed = (
        (query_tenant[:, None] == key_tenant[None, :])
        & (gap >= 0)
        & (gap < WINDOW)
        & (key_pos[None, :] >= 0)
    )
    masked = jnp.where(allowed[None], scores, NEG_FILL)
    row_max = jnp.max(masked, axis=2)
    weights = jnp.where(allowed[None], jnp.exp(masked - row_max[..., None]), 0.0)
    totals = jnp.sum(weights, axis=2)
    summed = jnp.einsum(
        "gcs,sh->gch", weights.astype(jnp.bfloat16), values, preferred_element_type=jnp.float32
    )
    return (row_max, totals, summed)


def combine_parts(first, second):
    top = jnp.maximum(first[0], second[0])
    scale_one = jnp.exp(first[0] - top)
    scale_two = jnp.exp(second[0] - top)
    totals = first[1] * scale_one + second[1] * scale_two
    summed = first[2] * scale_one[..., None] + second[2] * scale_two[..., None]
    return summed / totals[..., None]


def member_groups(devices, size):
    return [list(range(start, start + size)) for start in range(0, devices, size)]


def group_gather(piece, axis, size):
    spread = jnp.broadcast_to(piece[None], (size,) + piece.shape)
    groups = member_groups(lax.axis_size(axis), size)
    return lax.all_to_all(spread, axis, 0, 0, axis_index_groups=groups, tiled=True)


def group_exchange(parts, axis, size):
    groups = member_groups(lax.axis_size(axis), size)
    return lax.all_to_all(parts, axis, 0, 0, axis_index_groups=groups, tiled=True)


def joined_rows(span_order, shard, spans_here, stored_rows):
    local_order = lax.dynamic_slice_in_dim(span_order, shard * spans_here, spans_here, 0)
    local_order = local_order - shard * spans_here
    blocks = jnp.arange(spans_here, dtype=jnp.int32)
    inverse = jnp.sum(
        jnp.where(local_order[None, :] == blocks[:, None], blocks[None, :], 0), axis=1
    )
    slot = jnp.take(inverse, stored_rows // SPAN)
    return shard * spans_here * SPAN + slot * SPAN + stored_rows % SPAN


def local(
    cache_entries,
    recompute_input,
    norm_gain,
    w_query,
    w_keyval,
    w_out,
    rotate_offsets,
    span_order,
    tenant_of_span,
    recompute_pos,
    recompute_count,
):
    blk_count = lax.axis_size("blk")
    kv_index = lax.axis_index("kv")
    blk_index = lax.axis_index("blk")
    block_rows = cache_entries.shape[0]
    shard_len = block_rows * blk_count
    slots = recompute_input.shape[0]
    own_cols = recompute_input.shape[1]
    width = norm_gain.shape[0]
    spans_here = shard_len // SPAN
    group_size = QH // KVH
    pair_cols = w_keyval.shape[1] // blk_count
    member = blk_index % group_size
    group = blk_index // group_size

    rows_each = block_rows // group_size
    x_part = jnp.broadcast_to(recompute_input[None], (blk_count, slots, own_cols))
    quarter = pair_cols // 2
    key_members = HEAD_DIM // pair_cols
    groups_w = w_keyval.reshape(own_cols, KVH, 2 * HEAD_DIM)
    sorted_w = []
    for m in range(key_members):
        sorted_w.append(groups_w[:, :, m * quarter : (m + 1) * quarter])
        second = HEAD_DIM // 2 + m * quarter
        sorted_w.append(groups_w[:, :, second : second + quarter])
    sorted_w.append(groups_w[:, :, HEAD_DIM:])
    w_part = (
        jnp.concatenate(sorted_w, axis=2)
        .reshape(own_cols, blk_count, pair_cols)
        .transpose(1, 0, 2)
        .reshape(blk_count, own_cols * pair_cols // HEAD_DIM, HEAD_DIM)
    )
    c_part = (
        cache_entries.reshape(group_size, rows_each, KVH, 2 * HEAD_DIM)
        .transpose(2, 0, 1, 3)
        .reshape(blk_count, rows_each * 2, HEAD_DIM)
    )
    arrived = lax.all_to_all(x_part, "blk", 0, 0, tiled=True)
    wide = arrived.astype(jnp.float32)
    arrived, w_part, c_part = lax.optimization_barrier((arrived, w_part, c_part))
    w_rows = w_part.shape[1]
    moved = lax.all_to_all(jnp.concatenate([w_part, c_part], axis=1), "blk", 0, 0, tiled=True)
    kv_cols = moved[:, :w_rows].reshape(blk_count, own_cols, pair_cols)
    stored = moved[:, w_rows:].reshape(blk_count * rows_each, 2 * HEAD_DIM)

    gains = norm_gain.astype(jnp.float32).reshape(blk_count, 1, own_cols)
    scaled = (wide * gains).astype(jnp.bfloat16)
    square_acc = jnp.sum(wide * wide, axis=(0, 2))
    inv_rms = lax.rsqrt(square_acc / width + NORM_EPS)
    query_acc = jnp.einsum(
        "ksc,kcd->sd",
        scaled,
        w_query.reshape(blk_count, own_cols, HEAD_DIM),
        preferred_element_type=jnp.float32,
    ) * inv_rms[:, None]
    pair_piece = jnp.einsum(
        "ksc,kcd->sd", scaled, kv_cols, preferred_element_type=jnp.float32
    ) * inv_rms[:, None]
    own_pos = lax.dynamic_slice_in_dim(recompute_pos, kv_index * slots, slots, 0)
    own_count = lax.dynamic_index_in_dim(recompute_count, kv_index, 0, keepdims=False)
    live = jnp.arange(slots, dtype=jnp.int32) < own_count
    query_pos = kv_index * shard_len + own_pos
    own_query = rotate_half(query_acc.reshape(slots, 1, HEAD_DIM), query_pos)
    own_query = own_query.astype(jnp.bfloat16).reshape(slots, HEAD_DIM)
    inverse = ROPE_BASE ** (
        -(jnp.arange(HEAD_DIM // 2, dtype=jnp.float32) * 2.0 / HEAD_DIM)
    )
    freq = lax.dynamic_slice_in_dim(inverse, (member % key_members) * quarter, quarter, 0)
    angles = query_pos.astype(jnp.float32)[:, None] * freq[None, :]
    cosine = jnp.cos(angles)
    sine = jnp.sin(angles)
    first = pair_piece[:, :quarter]
    second = pair_piece[:, quarter:]
    turned = jnp.concatenate([first * cosine - second * sine, second * cosine + first * sine], axis=1)
    own_piece = jnp.where(member < key_members, turned, pair_piece).astype(jnp.bfloat16)
    shared = group_gather(jnp.concatenate([own_query, own_piece], axis=1), "blk", group_size)
    queries = shared[:, :, :HEAD_DIM].transpose(1, 0, 2)
    pieces = shared[:, :, HEAD_DIM:]
    fresh_keys = jnp.concatenate(
        [pieces[m, :, :quarter] for m in range(key_members)]
        + [pieces[m, :, quarter:] for m in range(key_members)],
        axis=1,
    )
    fresh_values = jnp.concatenate([pieces[m] for m in range(key_members, group_size)], axis=1)

    local_rows = jnp.arange(blk_count * rows_each, dtype=jnp.int32)
    stored_rows = (local_rows // rows_each) * block_rows + member * rows_each + local_rows % rows_each
    key_pos = joined_rows(span_order, kv_index, spans_here, stored_rows)
    offsets = lax.dynamic_slice_in_dim(rotate_offsets, kv_index * spans_here, spans_here, 0)
    row_shifts = jnp.take(offsets, stored_rows // SPAN)
    turned_rows = rotate_half(stored[:, :HEAD_DIM].astype(jnp.float32), row_shifts).astype(
        jnp.bfloat16
    )
    stored = jnp.concatenate([turned_rows, stored[:, HEAD_DIM:]], axis=-1)
    local_order = lax.dynamic_slice_in_dim(span_order, kv_index * spans_here, spans_here, 0)
    slot_rows = (jnp.take(local_order, own_pos // SPAN) - kv_index * spans_here) * SPAN + own_pos % SPAN
    mine = live & ((slot_rows % block_rows) // rows_each == member)
    place = jnp.where(
        mine, (slot_rows // block_rows) * rows_each + slot_rows % rows_each, blk_count * rows_each
    )
    merged = stored.at[place].set(jnp.concatenate([fresh_keys, fresh_values], axis=1), mode="drop")
    query_tenant = tenant_lookup(query_pos, tenant_of_span)
    own_part = attend_part(
        queries,
        query_pos,
        query_tenant,
        merged[:, :HEAD_DIM],
        merged[:, HEAD_DIM:],
        key_pos,
        tenant_lookup(key_pos, tenant_of_span),
    )
    prior = shifted(merged, "kv", 1)
    prior_pos = joined_rows(span_order, jnp.maximum(kv_index - 1, 0), spans_here, stored_rows)
    prior_pos = jnp.where(kv_index > 0, prior_pos, -1)
    prior_part = attend_part(
        queries,
        query_pos,
        query_tenant,
        prior[:, :HEAD_DIM],
        prior[:, HEAD_DIM:],
        prior_pos,
        tenant_lookup(prior_pos, tenant_of_span),
    )
    top = jnp.maximum(own_part[0], prior_part[0])
    scale_own = jnp.exp(own_part[0] - top)
    scale_prior = jnp.exp(prior_part[0] - top)
    totals = own_part[1] * scale_own + prior_part[1] * scale_prior
    summed = own_part[2] * scale_own[..., None] + prior_part[2] * scale_prior[..., None]
    packed = jnp.concatenate([summed, top[..., None], totals[..., None]], axis=-1)
    gathered = group_exchange(packed, "blk", group_size)
    part_max = gathered[:, :, HEAD_DIM]
    part_total = gathered[:, :, HEAD_DIM + 1]
    best = jnp.max(part_max, axis=0)
    weight = jnp.exp(part_max - best[None])
    total = jnp.sum(part_total * weight, axis=0)
    heads_sum = jnp.sum(gathered[:, :, :HEAD_DIM] * weight[..., None], axis=0)
    heads_out = (heads_sum / total[:, None]).astype(jnp.bfloat16)
    term = jnp.einsum(
        "ch,hkd->kcd",
        heads_out,
        w_out.reshape(HEAD_DIM, blk_count, own_cols),
        preferred_element_type=jnp.float32,
    )
    arrived_terms = lax.all_to_all(term.astype(jnp.bfloat16), "blk", 0, 0, tiled=True)
    summed_out = jnp.sum(arrived_terms.astype(jnp.float32), axis=0)
    return jnp.where(live[:, None], summed_out, 0.0).astype(jnp.bfloat16)


def solution(mesh):
    placed = (
        P(("kv", "blk"), None, None),
        P("kv", "blk"),
        P(),
        P(None, "blk"),
        P("blk", None),
        P("blk", None),
        P(),
        P(),
        P(),
        P(),
        P(),
    )
    return jax.shard_map(
        local, mesh=mesh, in_specs=placed, out_specs=P("kv", "blk"), check_vma=False
    )
```

```python
import math

import jax
import jax.numpy as jnp
import numpy as np
from jax import lax
from jax.sharding import PartitionSpec as P

QH = 32
KVH = 8
HEAD_DIM = 128
WINDOW = 4096
SPAN = 1024


NEG_FILL = -1e30
ROPE_BASE = 10000.0
NORM_EPS = 1e-05


def shifted(shard, axis, by):
    devices = lax.axis_size(axis)
    pairs = [(i, i + by) for i in range(devices) if 0 <= i + by < devices]
    return lax.ppermute(shard, axis, pairs)


def rotate_half(values, positions):
    half = values.shape[-1] // 2
    inverse = ROPE_BASE ** (-(jnp.arange(half, dtype=jnp.float32) * 2.0 / values.shape[-1]))
    angles = positions.astype(jnp.float32)[:, None] * inverse[None, :]
    shape = (positions.shape[0],) + (1,) * (values.ndim - 2) + (half,)
    cosine = jnp.cos(angles).reshape(shape)
    sine = jnp.sin(angles).reshape(shape)
    first = values[..., :half]
    second = values[..., half:]
    return jnp.concatenate(
        [first * cosine - second * sine, second * cosine + first * sine], axis=-1
    )


def tenant_lookup(positions, tenant_of_span):
    span_ids = positions // SPAN
    table_index = jnp.arange(tenant_of_span.shape[0], dtype=jnp.int32)
    match = span_ids[:, None] == table_index[None, :]
    return jnp.sum(jnp.where(match, tenant_of_span[None, :], 0), axis=1)


def attend_part(queries, query_pos, query_tenant, keys, values, key_pos, key_tenant):
    scale = 1.0 / math.sqrt(keys.shape[-1])
    scores = jnp.einsum("cgh,sh->gcs", queries, keys, preferred_element_type=jnp.float32) * scale
    gap = query_pos[:, None] - key_pos[None, :]
    allowed = (
        (query_tenant[:, None] == key_tenant[None, :])
        & (gap >= 0)
        & (gap < WINDOW)
        & (key_pos[None, :] >= 0)
    )
    masked = jnp.where(allowed[None], scores, NEG_FILL)
    row_max = jnp.max(masked, axis=2)
    weights = jnp.where(allowed[None], jnp.exp(masked - row_max[..., None]), 0.0)
    totals = jnp.sum(weights, axis=2)
    summed = jnp.einsum(
        "gcs,sh->gch", weights.astype(jnp.bfloat16), values, preferred_element_type=jnp.float32
    )
    return (row_max, totals, summed)


def combine_parts(first, second):
    top = jnp.maximum(first[0], second[0])
    scale_one = jnp.exp(first[0] - top)
    scale_two = jnp.exp(second[0] - top)
    totals = first[1] * scale_one + second[1] * scale_two
    summed = first[2] * scale_one[..., None] + second[2] * scale_two[..., None]
    return summed / totals[..., None]


def member_groups(devices, size):
    return [list(range(start, start + size)) for start in range(0, devices, size)]


def group_gather(piece, axis, size):
    spread = jnp.broadcast_to(piece[None], (size,) + piece.shape)
    groups = member_groups(lax.axis_size(axis), size)
    return lax.all_to_all(spread, axis, 0, 0, axis_index_groups=groups, tiled=True)


def group_exchange(parts, axis, size):
    groups = member_groups(lax.axis_size(axis), size)
    return lax.all_to_all(parts, axis, 0, 0, axis_index_groups=groups, tiled=True)


def joined_rows(span_order, shard, spans_here, stored_rows):
    local_order = lax.dynamic_slice_in_dim(span_order, shard * spans_here, spans_here, 0)
    local_order = local_order - shard * spans_here
    blocks = jnp.arange(spans_here, dtype=jnp.int32)
    inverse = jnp.sum(
        jnp.where(local_order[None, :] == blocks[:, None], blocks[None, :], 0), axis=1
    )
    slot = jnp.take(inverse, stored_rows // SPAN)
    return shard * spans_here * SPAN + slot * SPAN + stored_rows % SPAN


def local(
    cache_entries,
    recompute_input,
    norm_gain,
    w_query,
    w_keyval,
    w_out,
    rotate_offsets,
    span_order,
    tenant_of_span,
    recompute_pos,
    recompute_count,
):
    blk_count = lax.axis_size("blk")
    kv_index = lax.axis_index("kv")
    blk_index = lax.axis_index("blk")
    block_rows = cache_entries.shape[0]
    shard_len = block_rows * blk_count
    slots = recompute_input.shape[0]
    own_cols = recompute_input.shape[1]
    width = norm_gain.shape[0]
    spans_here = shard_len // SPAN
    group_size = QH // KVH
    pair_cols = w_keyval.shape[1] // blk_count
    member = blk_index % group_size
    group = blk_index // group_size

    rows_each = block_rows // group_size
    x_part = jnp.broadcast_to(recompute_input[None], (blk_count, slots, own_cols))
    quarter = pair_cols // 2
    key_members = HEAD_DIM // pair_cols
    groups_w = w_keyval.reshape(own_cols, KVH, 2 * HEAD_DIM)
    sorted_w = []
    for m in range(key_members):
        sorted_w.append(groups_w[:, :, m * quarter : (m + 1) * quarter])
        second = HEAD_DIM // 2 + m * quarter
        sorted_w.append(groups_w[:, :, second : second + quarter])
    sorted_w.append(groups_w[:, :, HEAD_DIM:])
    w_part = (
        jnp.concatenate(sorted_w, axis=2)
        .reshape(own_cols, blk_count, pair_cols)
        .transpose(1, 0, 2)
        .reshape(blk_count, own_cols * pair_cols // HEAD_DIM, HEAD_DIM)
    )
    c_part = (
        cache_entries.reshape(group_size, rows_each, KVH, 2 * HEAD_DIM)
        .transpose(2, 0, 1, 3)
        .reshape(blk_count, rows_each * 2, HEAD_DIM)
    )
    arrived = lax.all_to_all(jnp.concatenate([x_part, w_part], axis=1), "blk", 0, 0, tiled=True)
    wide = arrived[:, :slots].astype(jnp.float32)
    kv_cols = arrived[:, slots:].reshape(blk_count, own_cols, pair_cols)

    gains = norm_gain.astype(jnp.float32).reshape(blk_count, 1, own_cols)
    scaled = (wide * gains).astype(jnp.bfloat16)
    square_acc = jnp.sum(wide * wide, axis=(0, 2))
    inv_rms = lax.rsqrt(square_acc / width + NORM_EPS)
    query_acc = jnp.einsum(
        "ksc,kcd->sd",
        scaled,
        w_query.reshape(blk_count, own_cols, HEAD_DIM),
        preferred_element_type=jnp.float32,
    ) * inv_rms[:, None]
    pair_piece = jnp.einsum(
        "ksc,kcd->sd", scaled, kv_cols, preferred_element_type=jnp.float32
    ) * inv_rms[:, None]
    own_pos = lax.dynamic_slice_in_dim(recompute_pos, kv_index * slots, slots, 0)
    own_count = lax.dynamic_index_in_dim(recompute_count, kv_index, 0, keepdims=False)
    live = jnp.arange(slots, dtype=jnp.int32) < own_count
    query_pos = kv_index * shard_len + own_pos
    own_query = rotate_half(query_acc.reshape(slots, 1, HEAD_DIM), query_pos)
    own_query = own_query.astype(jnp.bfloat16).reshape(slots, HEAD_DIM)
    inverse = ROPE_BASE ** (
        -(jnp.arange(HEAD_DIM // 2, dtype=jnp.float32) * 2.0 / HEAD_DIM)
    )
    freq = lax.dynamic_slice_in_dim(inverse, (member % key_members) * quarter, quarter, 0)
    angles = query_pos.astype(jnp.float32)[:, None] * freq[None, :]
    cosine = jnp.cos(angles)
    sine = jnp.sin(angles)
    first = pair_piece[:, :quarter]
    second = pair_piece[:, quarter:]
    turned = jnp.concatenate([first * cosine - second * sine, second * cosine + first * sine], axis=1)
    own_piece = jnp.where(member < key_members, turned, pair_piece).astype(jnp.bfloat16)
    outgoing = jnp.concatenate([own_query, own_piece], axis=1)
    outgoing, c_part = lax.optimization_barrier((outgoing, c_part))
    stored = lax.all_to_all(c_part, "blk", 0, 0, tiled=True).reshape(
        blk_count * rows_each, 2 * HEAD_DIM
    )
    shared = group_gather(outgoing, "blk", group_size)
    queries = shared[:, :, :HEAD_DIM].transpose(1, 0, 2)
    pieces = shared[:, :, HEAD_DIM:]
    fresh_keys = jnp.concatenate(
        [pieces[m, :, :quarter] for m in range(key_members)]
        + [pieces[m, :, quarter:] for m in range(key_members)],
        axis=1,
    )
    fresh_values = jnp.concatenate([pieces[m] for m in range(key_members, group_size)], axis=1)

    local_rows = jnp.arange(blk_count * rows_each, dtype=jnp.int32)
    stored_rows = (local_rows // rows_each) * block_rows + member * rows_each + local_rows % rows_each
    key_pos = joined_rows(span_order, kv_index, spans_here, stored_rows)
    offsets = lax.dynamic_slice_in_dim(rotate_offsets, kv_index * spans_here, spans_here, 0)
    row_shifts = jnp.take(offsets, stored_rows // SPAN)
    turned_rows = rotate_half(stored[:, :HEAD_DIM].astype(jnp.float32), row_shifts).astype(
        jnp.bfloat16
    )
    stored = jnp.concatenate([turned_rows, stored[:, HEAD_DIM:]], axis=-1)
    local_order = lax.dynamic_slice_in_dim(span_order, kv_index * spans_here, spans_here, 0)
    slot_rows = (jnp.take(local_order, own_pos // SPAN) - kv_index * spans_here) * SPAN + own_pos % SPAN
    mine = live & ((slot_rows % block_rows) // rows_each == member)
    place = jnp.where(
        mine, (slot_rows // block_rows) * rows_each + slot_rows % rows_each, blk_count * rows_each
    )
    merged = stored.at[place].set(jnp.concatenate([fresh_keys, fresh_values], axis=1), mode="drop")
    query_tenant = tenant_lookup(query_pos, tenant_of_span)
    own_part = attend_part(
        queries,
        query_pos,
        query_tenant,
        merged[:, :HEAD_DIM],
        merged[:, HEAD_DIM:],
        key_pos,
        tenant_lookup(key_pos, tenant_of_span),
    )
    prior = shifted(merged, "kv", 1)
    prior_pos = joined_rows(span_order, jnp.maximum(kv_index - 1, 0), spans_here, stored_rows)
    prior_pos = jnp.where(kv_index > 0, prior_pos, -1)
    prior_part = attend_part(
        queries,
        query_pos,
        query_tenant,
        prior[:, :HEAD_DIM],
        prior[:, HEAD_DIM:],
        prior_pos,
        tenant_lookup(prior_pos, tenant_of_span),
    )
    top = jnp.maximum(own_part[0], prior_part[0])
    scale_own = jnp.exp(own_part[0] - top)
    scale_prior = jnp.exp(prior_part[0] - top)
    totals = own_part[1] * scale_own + prior_part[1] * scale_prior
    summed = own_part[2] * scale_own[..., None] + prior_part[2] * scale_prior[..., None]
    packed = jnp.concatenate([summed, top[..., None], totals[..., None]], axis=-1)
    gathered = group_exchange(packed, "blk", group_size)
    part_max = gathered[:, :, HEAD_DIM]
    part_total = gathered[:, :, HEAD_DIM + 1]
    best = jnp.max(part_max, axis=0)
    weight = jnp.exp(part_max - best[None])
    total = jnp.sum(part_total * weight, axis=0)
    heads_sum = jnp.sum(gathered[:, :, :HEAD_DIM] * weight[..., None], axis=0)
    heads_out = (heads_sum / total[:, None]).astype(jnp.bfloat16)
    term = jnp.einsum(
        "ch,hkd->kcd",
        heads_out,
        w_out.reshape(HEAD_DIM, blk_count, own_cols),
        preferred_element_type=jnp.float32,
    )
    arrived_terms = lax.all_to_all(term.astype(jnp.bfloat16), "blk", 0, 0, tiled=True)
    summed_out = jnp.sum(arrived_terms.astype(jnp.float32), axis=0)
    return jnp.where(live[:, None], summed_out, 0.0).astype(jnp.bfloat16)


def solution(mesh):
    placed = (
        P(("kv", "blk"), None, None),
        P("kv", "blk"),
        P(),
        P(None, "blk"),
        P("blk", None),
        P("blk", None),
        P(),
        P(),
        P(),
        P(),
        P(),
    )
    return jax.shard_map(
        local, mesh=mesh, in_specs=placed, out_specs=P("kv", "blk"), check_vma=False
    )
```

```python
import math

import jax
import jax.numpy as jnp
import numpy as np
from jax import lax
from jax.sharding import PartitionSpec as P

QH = 32
KVH = 8
HEAD_DIM = 128
WINDOW = 4096
SPAN = 1024


NEG_FILL = -1e30
ROPE_BASE = 10000.0
NORM_EPS = 1e-05


def shifted(shard, axis, by):
    devices = lax.axis_size(axis)
    pairs = [(i, i + by) for i in range(devices) if 0 <= i + by < devices]
    return lax.ppermute(shard, axis, pairs)


def rotate_half(values, positions):
    half = values.shape[-1] // 2
    inverse = ROPE_BASE ** (-(jnp.arange(half, dtype=jnp.float32) * 2.0 / values.shape[-1]))
    angles = positions.astype(jnp.float32)[:, None] * inverse[None, :]
    shape = (positions.shape[0],) + (1,) * (values.ndim - 2) + (half,)
    cosine = jnp.cos(angles).reshape(shape)
    sine = jnp.sin(angles).reshape(shape)
    first = values[..., :half]
    second = values[..., half:]
    return jnp.concatenate(
        [first * cosine - second * sine, second * cosine + first * sine], axis=-1
    )


def tenant_lookup(positions, tenant_of_span):
    span_ids = positions // SPAN
    table_index = jnp.arange(tenant_of_span.shape[0], dtype=jnp.int32)
    match = span_ids[:, None] == table_index[None, :]
    return jnp.sum(jnp.where(match, tenant_of_span[None, :], 0), axis=1)


def attend_part(queries, query_pos, query_tenant, keys, values, key_pos, key_tenant):
    scale = 1.0 / math.sqrt(keys.shape[-1])
    scores = jnp.einsum("cgh,sh->gcs", queries, keys, preferred_element_type=jnp.float32) * scale
    gap = query_pos[:, None] - key_pos[None, :]
    allowed = (
        (query_tenant[:, None] == key_tenant[None, :])
        & (gap >= 0)
        & (gap < WINDOW)
        & (key_pos[None, :] >= 0)
    )
    masked = jnp.where(allowed[None], scores, NEG_FILL)
    row_max = jnp.max(masked, axis=2)
    weights = jnp.where(allowed[None], jnp.exp(masked - row_max[..., None]), 0.0)
    totals = jnp.sum(weights, axis=2)
    summed = jnp.einsum(
        "gcs,sh->gch", weights.astype(jnp.bfloat16), values, preferred_element_type=jnp.float32
    )
    return (row_max, totals, summed)


def combine_parts(first, second):
    top = jnp.maximum(first[0], second[0])
    scale_one = jnp.exp(first[0] - top)
    scale_two = jnp.exp(second[0] - top)
    totals = first[1] * scale_one + second[1] * scale_two
    summed = first[2] * scale_one[..., None] + second[2] * scale_two[..., None]
    return summed / totals[..., None]


def member_groups(devices, size):
    return [list(range(start, start + size)) for start in range(0, devices, size)]


def group_gather(piece, axis, size):
    spread = jnp.broadcast_to(piece[None], (size,) + piece.shape)
    groups = member_groups(lax.axis_size(axis), size)
    return lax.all_to_all(spread, axis, 0, 0, axis_index_groups=groups, tiled=True)


def group_exchange(parts, axis, size):
    groups = member_groups(lax.axis_size(axis), size)
    return lax.all_to_all(parts, axis, 0, 0, axis_index_groups=groups, tiled=True)


def joined_rows(span_order, shard, spans_here, stored_rows):
    local_order = lax.dynamic_slice_in_dim(span_order, shard * spans_here, spans_here, 0)
    local_order = local_order - shard * spans_here
    blocks = jnp.arange(spans_here, dtype=jnp.int32)
    inverse = jnp.sum(
        jnp.where(local_order[None, :] == blocks[:, None], blocks[None, :], 0), axis=1
    )
    slot = jnp.take(inverse, stored_rows // SPAN)
    return shard * spans_here * SPAN + slot * SPAN + stored_rows % SPAN


def local(
    cache_entries,
    recompute_input,
    norm_gain,
    w_query,
    w_keyval,
    w_out,
    rotate_offsets,
    span_order,
    tenant_of_span,
    recompute_pos,
    recompute_count,
):
    blk_count = lax.axis_size("blk")
    kv_index = lax.axis_index("kv")
    blk_index = lax.axis_index("blk")
    block_rows = cache_entries.shape[0]
    shard_len = block_rows * blk_count
    slots = recompute_input.shape[0]
    own_cols = recompute_input.shape[1]
    width = norm_gain.shape[0]
    spans_here = shard_len // SPAN
    group_size = QH // KVH
    pair_cols = w_keyval.shape[1] // blk_count
    member = blk_index % group_size
    group = blk_index // group_size

    rows_each = block_rows // group_size
    x_part = jnp.broadcast_to(recompute_input[None], (blk_count, slots, own_cols))
    quarter = pair_cols // 2
    key_members = HEAD_DIM // pair_cols
    groups_w = w_keyval.reshape(own_cols, KVH, 2 * HEAD_DIM)
    sorted_w = []
    for m in range(key_members):
        sorted_w.append(groups_w[:, :, m * quarter : (m + 1) * quarter])
        second = HEAD_DIM // 2 + m * quarter
        sorted_w.append(groups_w[:, :, second : second + quarter])
    sorted_w.append(groups_w[:, :, HEAD_DIM:])
    w_part = (
        jnp.concatenate(sorted_w, axis=2)
        .reshape(own_cols, blk_count, pair_cols)
        .transpose(1, 0, 2)
        .reshape(blk_count, own_cols * pair_cols // HEAD_DIM, HEAD_DIM)
    )
    c_part = (
        cache_entries.reshape(group_size, rows_each, KVH, 2 * HEAD_DIM)
        .transpose(2, 0, 1, 3)
        .reshape(blk_count, rows_each * 2, HEAD_DIM)
    )
    w_rows = w_part.shape[1]
    arrived = lax.all_to_all(
        jnp.concatenate([x_part, w_part, c_part], axis=1), "blk", 0, 0, tiled=True
    )
    wide = arrived[:, :slots].astype(jnp.float32)
    kv_cols = arrived[:, slots : slots + w_rows].reshape(blk_count, own_cols, pair_cols)
    stored = arrived[:, slots + w_rows :].reshape(blk_count * rows_each, 2 * HEAD_DIM)

    gains = norm_gain.astype(jnp.float32).reshape(blk_count, 1, own_cols)
    scaled = (wide * gains).astype(jnp.bfloat16)
    square_acc = jnp.sum(wide * wide, axis=(0, 2))
    inv_rms = lax.rsqrt(square_acc / width + NORM_EPS)
    query_acc = jnp.einsum(
        "ksc,kcd->sd",
        scaled,
        w_query.reshape(blk_count, own_cols, HEAD_DIM),
        preferred_element_type=jnp.float32,
    ) * inv_rms[:, None]
    pair_piece = jnp.einsum(
        "ksc,kcd->sd", scaled, kv_cols, preferred_element_type=jnp.float32
    ) * inv_rms[:, None]
    own_pos = lax.dynamic_slice_in_dim(recompute_pos, kv_index * slots, slots, 0)
    own_count = lax.dynamic_index_in_dim(recompute_count, kv_index, 0, keepdims=False)
    live = jnp.arange(slots, dtype=jnp.int32) < own_count
    query_pos = kv_index * shard_len + own_pos
    own_query = rotate_half(query_acc.reshape(slots, 1, HEAD_DIM), query_pos)
    own_query = own_query.astype(jnp.bfloat16).reshape(slots, HEAD_DIM)
    inverse = ROPE_BASE ** (
        -(jnp.arange(HEAD_DIM // 2, dtype=jnp.float32) * 2.0 / HEAD_DIM)
    )
    freq = lax.dynamic_slice_in_dim(inverse, (member % key_members) * quarter, quarter, 0)
    angles = query_pos.astype(jnp.float32)[:, None] * freq[None, :]
    cosine = jnp.cos(angles)
    sine = jnp.sin(angles)
    first = pair_piece[:, :quarter]
    second = pair_piece[:, quarter:]
    turned = jnp.concatenate([first * cosine - second * sine, second * cosine + first * sine], axis=1)
    own_piece = jnp.where(member < key_members, turned, pair_piece).astype(jnp.bfloat16)
    shared = group_gather(jnp.concatenate([own_query, own_piece], axis=1), "blk", group_size)
    queries = shared[:, :, :HEAD_DIM].transpose(1, 0, 2)
    pieces = shared[:, :, HEAD_DIM:]
    fresh_keys = jnp.concatenate(
        [pieces[m, :, :quarter] for m in range(key_members)]
        + [pieces[m, :, quarter:] for m in range(key_members)],
        axis=1,
    )
    fresh_values = jnp.concatenate([pieces[m] for m in range(key_members, group_size)], axis=1)

    local_rows = jnp.arange(blk_count * rows_each, dtype=jnp.int32)
    stored_rows = (local_rows // rows_each) * block_rows + member * rows_each + local_rows % rows_each
    key_pos = joined_rows(span_order, kv_index, spans_here, stored_rows)
    offsets = lax.dynamic_slice_in_dim(rotate_offsets, kv_index * spans_here, spans_here, 0)
    row_shifts = jnp.take(offsets, stored_rows // SPAN)
    turned_rows = rotate_half(stored[:, :HEAD_DIM].astype(jnp.float32), row_shifts).astype(
        jnp.bfloat16
    )
    stored = jnp.concatenate([turned_rows, stored[:, HEAD_DIM:]], axis=-1)
    local_order = lax.dynamic_slice_in_dim(span_order, kv_index * spans_here, spans_here, 0)
    slot_rows = (jnp.take(local_order, own_pos // SPAN) - kv_index * spans_here) * SPAN + own_pos % SPAN
    mine = live & ((slot_rows % block_rows) // rows_each == member)
    place = jnp.where(
        mine, (slot_rows // block_rows) * rows_each + slot_rows % rows_each, blk_count * rows_each
    )
    merged = stored.at[place].set(jnp.concatenate([fresh_keys, fresh_values], axis=1), mode="drop")
    query_tenant = tenant_lookup(query_pos, tenant_of_span)
    own_part = attend_part(
        queries,
        query_pos,
        query_tenant,
        merged[:, :HEAD_DIM],
        merged[:, HEAD_DIM:],
        key_pos,
        tenant_lookup(key_pos, tenant_of_span),
    )
    prior = shifted(merged, "kv", 1)
    prior_pos = joined_rows(span_order, jnp.maximum(kv_index - 1, 0), spans_here, stored_rows)
    prior_pos = jnp.where(kv_index > 0, prior_pos, -1)
    prior_part = attend_part(
        queries,
        query_pos,
        query_tenant,
        prior[:, :HEAD_DIM],
        prior[:, HEAD_DIM:],
        prior_pos,
        tenant_lookup(prior_pos, tenant_of_span),
    )
    top = jnp.maximum(own_part[0], prior_part[0])
    scale_own = jnp.exp(own_part[0] - top)
    scale_prior = jnp.exp(prior_part[0] - top)
    totals = own_part[1] * scale_own + prior_part[1] * scale_prior
    summed = own_part[2] * scale_own[..., None] + prior_part[2] * scale_prior[..., None]
    packed = jnp.concatenate([summed, top[..., None], totals[..., None]], axis=-1)
    gathered = group_exchange(packed, "blk", group_size)
    part_max = gathered[:, :, HEAD_DIM]
    part_total = gathered[:, :, HEAD_DIM + 1]
    best = jnp.max(part_max, axis=0)
    weight = jnp.exp(part_max - best[None])
    total = jnp.sum(part_total * weight, axis=0)
    heads_sum = jnp.sum(gathered[:, :, :HEAD_DIM] * weight[..., None], axis=0)
    heads_out = (heads_sum / total[:, None]).astype(jnp.bfloat16)
    term = jnp.einsum(
        "ch,hkd->kcd",
        heads_out,
        w_out.reshape(HEAD_DIM, blk_count, own_cols),
        preferred_element_type=jnp.float32,
    )
    arrived_terms = lax.all_to_all(term.astype(jnp.bfloat16), "blk", 0, 0, tiled=True)
    summed_out = jnp.sum(arrived_terms.astype(jnp.float32), axis=0)
    return jnp.where(live[:, None], summed_out, 0.0).astype(jnp.bfloat16)


def solution(mesh):
    placed = (
        P(("kv", "blk"), None, None),
        P("kv", "blk"),
        P(),
        P(None, "blk"),
        P("blk", None),
        P("blk", None),
        P(),
        P(),
        P(),
        P(),
        P(),
    )
    return jax.shard_map(
        local, mesh=mesh, in_specs=placed, out_specs=P("kv", "blk"), check_vma=False
    )
```

```python
import math

import jax
import jax.numpy as jnp
import numpy as np
from jax import lax
from jax.sharding import PartitionSpec as P

QH = 32
KVH = 8
HEAD_DIM = 128
WINDOW = 4096
SPAN = 1024


NEG_FILL = -1e30
ROPE_BASE = 10000.0
NORM_EPS = 1e-05


def shifted(shard, axis, by):
    devices = lax.axis_size(axis)
    pairs = [(i, i + by) for i in range(devices) if 0 <= i + by < devices]
    return lax.ppermute(shard, axis, pairs)


def rotate_half(values, positions):
    half = values.shape[-1] // 2
    inverse = ROPE_BASE ** (-(jnp.arange(half, dtype=jnp.float32) * 2.0 / values.shape[-1]))
    angles = positions.astype(jnp.float32)[:, None] * inverse[None, :]
    shape = (positions.shape[0],) + (1,) * (values.ndim - 2) + (half,)
    cosine = jnp.cos(angles).reshape(shape)
    sine = jnp.sin(angles).reshape(shape)
    first = values[..., :half]
    second = values[..., half:]
    return jnp.concatenate(
        [first * cosine - second * sine, second * cosine + first * sine], axis=-1
    )


def tenant_lookup(positions, tenant_of_span):
    span_ids = positions // SPAN
    table_index = jnp.arange(tenant_of_span.shape[0], dtype=jnp.int32)
    match = span_ids[:, None] == table_index[None, :]
    return jnp.sum(jnp.where(match, tenant_of_span[None, :], 0), axis=1)


def attend_part(queries, query_pos, query_tenant, keys, values, key_pos, key_tenant):
    scale = 1.0 / math.sqrt(keys.shape[-1])
    scores = jnp.einsum("cgh,sh->gcs", queries, keys, preferred_element_type=jnp.float32) * scale
    gap = query_pos[:, None] - key_pos[None, :]
    allowed = (
        (query_tenant[:, None] == key_tenant[None, :])
        & (gap >= 0)
        & (gap < WINDOW)
        & (key_pos[None, :] >= 0)
    )
    masked = jnp.where(allowed[None], scores, NEG_FILL)
    row_max = jnp.max(masked, axis=2)
    weights = jnp.where(allowed[None], jnp.exp(masked - row_max[..., None]), 0.0)
    totals = jnp.sum(weights, axis=2)
    summed = jnp.einsum(
        "gcs,sh->gch", weights.astype(jnp.bfloat16), values, preferred_element_type=jnp.float32
    )
    return (row_max, totals, summed)


def combine_parts(first, second):
    top = jnp.maximum(first[0], second[0])
    scale_one = jnp.exp(first[0] - top)
    scale_two = jnp.exp(second[0] - top)
    totals = first[1] * scale_one + second[1] * scale_two
    summed = first[2] * scale_one[..., None] + second[2] * scale_two[..., None]
    return summed / totals[..., None]


def member_groups(devices, size):
    return [list(range(start, start + size)) for start in range(0, devices, size)]


def group_gather(piece, axis, size):
    spread = jnp.broadcast_to(piece[None], (size,) + piece.shape)
    groups = member_groups(lax.axis_size(axis), size)
    return lax.all_to_all(spread, axis, 0, 0, axis_index_groups=groups, tiled=True)


def group_exchange(parts, axis, size):
    groups = member_groups(lax.axis_size(axis), size)
    return lax.all_to_all(parts, axis, 0, 0, axis_index_groups=groups, tiled=True)


def joined_rows(span_order, shard, spans_here, stored_rows):
    local_order = lax.dynamic_slice_in_dim(span_order, shard * spans_here, spans_here, 0)
    local_order = local_order - shard * spans_here
    blocks = jnp.arange(spans_here, dtype=jnp.int32)
    inverse = jnp.sum(
        jnp.where(local_order[None, :] == blocks[:, None], blocks[None, :], 0), axis=1
    )
    slot = jnp.take(inverse, stored_rows // SPAN)
    return shard * spans_here * SPAN + slot * SPAN + stored_rows % SPAN


def local(
    cache_entries,
    recompute_input,
    norm_gain,
    w_query,
    w_keyval,
    w_out,
    rotate_offsets,
    span_order,
    tenant_of_span,
    recompute_pos,
    recompute_count,
):
    blk_count = lax.axis_size("blk")
    kv_index = lax.axis_index("kv")
    blk_index = lax.axis_index("blk")
    block_rows = cache_entries.shape[0]
    shard_len = block_rows * blk_count
    slots = recompute_input.shape[0]
    own_cols = recompute_input.shape[1]
    width = norm_gain.shape[0]
    spans_here = shard_len // SPAN
    group_size = QH // KVH
    pair_cols = w_keyval.shape[1] // blk_count
    member = blk_index % group_size
    group = blk_index // group_size

    rows_each = block_rows // group_size
    x_part = jnp.broadcast_to(recompute_input[None], (blk_count, slots, own_cols))
    quarter = pair_cols // 2
    key_members = HEAD_DIM // pair_cols
    groups_w = w_keyval.reshape(own_cols, KVH, 2 * HEAD_DIM)
    sorted_w = []
    for m in range(key_members):
        sorted_w.append(groups_w[:, :, m * quarter : (m + 1) * quarter])
        second = HEAD_DIM // 2 + m * quarter
        sorted_w.append(groups_w[:, :, second : second + quarter])
    sorted_w.append(groups_w[:, :, HEAD_DIM:])
    w_part = (
        jnp.concatenate(sorted_w, axis=2)
        .reshape(own_cols, blk_count, pair_cols)
        .transpose(1, 0, 2)
        .reshape(blk_count, own_cols * pair_cols // HEAD_DIM, HEAD_DIM)
    )
    c_part = (
        cache_entries.reshape(group_size, rows_each, KVH, 2 * HEAD_DIM)
        .transpose(2, 0, 1, 3)
        .reshape(blk_count, rows_each * 2, HEAD_DIM)
    )
    arrived = lax.all_to_all(x_part, "blk", 0, 0, tiled=True)
    wide = arrived.astype(jnp.float32)
    arrived, w_part, c_part = lax.optimization_barrier((arrived, w_part, c_part))
    w_rows = w_part.shape[1]
    moved = lax.all_to_all(jnp.concatenate([w_part, c_part], axis=1), "blk", 0, 0, tiled=True)
    kv_cols = moved[:, :w_rows].reshape(blk_count, own_cols, pair_cols)
    stored = moved[:, w_rows:].reshape(blk_count * rows_each, 2 * HEAD_DIM)

    gains = norm_gain.astype(jnp.float32).reshape(blk_count, 1, own_cols)
    scaled = (wide * gains).astype(jnp.bfloat16)
    square_acc = jnp.sum(wide * wide, axis=(0, 2))
    inv_rms = lax.rsqrt(square_acc / width + NORM_EPS)
    query_acc = jnp.einsum(
        "ksc,kcd->sd",
        scaled,
        w_query.reshape(blk_count, own_cols, HEAD_DIM),
        preferred_element_type=jnp.float32,
    ) * inv_rms[:, None]
    pair_piece = jnp.einsum(
        "ksc,kcd->sd", scaled, kv_cols, preferred_element_type=jnp.float32
    ) * inv_rms[:, None]
    own_pos = lax.dynamic_slice_in_dim(recompute_pos, kv_index * slots, slots, 0)
    own_count = lax.dynamic_index_in_dim(recompute_count, kv_index, 0, keepdims=False)
    live = jnp.arange(slots, dtype=jnp.int32) < own_count
    query_pos = kv_index * shard_len + own_pos
    own_query = rotate_half(query_acc.reshape(slots, 1, HEAD_DIM), query_pos)
    own_query = own_query.astype(jnp.bfloat16).reshape(slots, HEAD_DIM)
    inverse = ROPE_BASE ** (
        -(jnp.arange(HEAD_DIM // 2, dtype=jnp.float32) * 2.0 / HEAD_DIM)
    )
    freq = lax.dynamic_slice_in_dim(inverse, (member % key_members) * quarter, quarter, 0)
    angles = query_pos.astype(jnp.float32)[:, None] * freq[None, :]
    cosine = jnp.cos(angles)
    sine = jnp.sin(angles)
    first = pair_piece[:, :quarter]
    second = pair_piece[:, quarter:]
    turned = jnp.concatenate([first * cosine - second * sine, second * cosine + first * sine], axis=1)
    own_piece = jnp.where(member < key_members, turned, pair_piece).astype(jnp.bfloat16)
    shared = group_gather(jnp.concatenate([own_query, own_piece], axis=1), "blk", group_size)
    queries = shared[:, :, :HEAD_DIM].transpose(1, 0, 2)
    pieces = shared[:, :, HEAD_DIM:]
    fresh_keys = jnp.concatenate(
        [pieces[m, :, :quarter] for m in range(key_members)]
        + [pieces[m, :, quarter:] for m in range(key_members)],
        axis=1,
    )
    fresh_values = jnp.concatenate([pieces[m] for m in range(key_members, group_size)], axis=1)

    local_rows = jnp.arange(blk_count * rows_each, dtype=jnp.int32)
    stored_rows = (local_rows // rows_each) * block_rows + member * rows_each + local_rows % rows_each
    key_pos = joined_rows(span_order, kv_index, spans_here, stored_rows)
    offsets = lax.dynamic_slice_in_dim(rotate_offsets, kv_index * spans_here, spans_here, 0)
    row_shifts = jnp.take(offsets, stored_rows // SPAN)
    turned_rows = rotate_half(stored[:, :HEAD_DIM].astype(jnp.float32), row_shifts).astype(
        jnp.bfloat16
    )
    stored = jnp.concatenate([turned_rows, stored[:, HEAD_DIM:]], axis=-1)
    local_order = lax.dynamic_slice_in_dim(span_order, kv_index * spans_here, spans_here, 0)
    slot_rows = (jnp.take(local_order, own_pos // SPAN) - kv_index * spans_here) * SPAN + own_pos % SPAN
    mine = live & ((slot_rows % block_rows) // rows_each == member)
    place = jnp.where(
        mine, (slot_rows // block_rows) * rows_each + slot_rows % rows_each, blk_count * rows_each
    )
    merged = stored.at[place].set(jnp.concatenate([fresh_keys, fresh_values], axis=1), mode="drop")
    query_tenant = tenant_lookup(query_pos, tenant_of_span)
    prior = shifted(merged, "kv", 1)
    prior_pos = joined_rows(span_order, jnp.maximum(kv_index - 1, 0), spans_here, stored_rows)
    prior_pos = jnp.where(kv_index > 0, prior_pos, -1)
    both = jnp.concatenate([merged, prior], axis=0)
    both_pos = jnp.concatenate([key_pos, prior_pos], axis=0)
    top, totals, summed = attend_part(
        queries,
        query_pos,
        query_tenant,
        both[:, :HEAD_DIM],
        both[:, HEAD_DIM:],
        both_pos,
        tenant_lookup(both_pos, tenant_of_span),
    )
    packed = jnp.concatenate([summed, top[..., None], totals[..., None]], axis=-1)
    gathered = group_exchange(packed, "blk", group_size)
    part_max = gathered[:, :, HEAD_DIM]
    part_total = gathered[:, :, HEAD_DIM + 1]
    best = jnp.max(part_max, axis=0)
    weight = jnp.exp(part_max - best[None])
    total = jnp.sum(part_total * weight, axis=0)
    heads_sum = jnp.sum(gathered[:, :, :HEAD_DIM] * weight[..., None], axis=0)
    heads_out = (heads_sum / total[:, None]).astype(jnp.bfloat16)
    term = jnp.einsum(
        "ch,hkd->kcd",
        heads_out,
        w_out.reshape(HEAD_DIM, blk_count, own_cols),
        preferred_element_type=jnp.float32,
    )
    arrived_terms = lax.all_to_all(term.astype(jnp.bfloat16), "blk", 0, 0, tiled=True)
    summed_out = jnp.sum(arrived_terms.astype(jnp.float32), axis=0)
    return jnp.where(live[:, None], summed_out, 0.0).astype(jnp.bfloat16)


def solution(mesh):
    placed = (
        P(("kv", "blk"), None, None),
        P("kv", "blk"),
        P(),
        P(None, "blk"),
        P("blk", None),
        P("blk", None),
        P(),
        P(),
        P(),
        P(),
        P(),
    )
    return jax.shard_map(
        local, mesh=mesh, in_specs=placed, out_specs=P("kv", "blk"), check_vma=False
    )
```

```python
import math

import jax
import jax.numpy as jnp
import numpy as np
from jax import lax
from jax.sharding import PartitionSpec as P

QH = 32
KVH = 8
HEAD_DIM = 128
WINDOW = 4096
SPAN = 1024


NEG_FILL = -1e30
ROPE_BASE = 10000.0
NORM_EPS = 1e-05


def shifted(shard, axis, by):
    devices = lax.axis_size(axis)
    pairs = [(i, i + by) for i in range(devices) if 0 <= i + by < devices]
    return lax.ppermute(shard, axis, pairs)


def rotate_half(values, positions):
    half = values.shape[-1] // 2
    inverse = ROPE_BASE ** (-(jnp.arange(half, dtype=jnp.float32) * 2.0 / values.shape[-1]))
    angles = positions.astype(jnp.float32)[:, None] * inverse[None, :]
    shape = (positions.shape[0],) + (1,) * (values.ndim - 2) + (half,)
    cosine = jnp.cos(angles).reshape(shape)
    sine = jnp.sin(angles).reshape(shape)
    first = values[..., :half]
    second = values[..., half:]
    return jnp.concatenate(
        [first * cosine - second * sine, second * cosine + first * sine], axis=-1
    )


def tenant_lookup(positions, tenant_of_span):
    span_ids = positions // SPAN
    table_index = jnp.arange(tenant_of_span.shape[0], dtype=jnp.int32)
    match = span_ids[:, None] == table_index[None, :]
    return jnp.sum(jnp.where(match, tenant_of_span[None, :], 0), axis=1)


def attend_part(queries, query_pos, query_tenant, keys, values, key_pos, key_tenant):
    scale = 1.0 / math.sqrt(keys.shape[-1])
    scores = jnp.einsum("cgh,sh->gcs", queries, keys, preferred_element_type=jnp.float32) * scale
    gap = query_pos[:, None] - key_pos[None, :]
    allowed = (
        (query_tenant[:, None] == key_tenant[None, :])
        & (gap >= 0)
        & (gap < WINDOW)
        & (key_pos[None, :] >= 0)
    )
    masked = jnp.where(allowed[None], scores, NEG_FILL)
    row_max = jnp.max(masked, axis=2)
    weights = jnp.where(allowed[None], jnp.exp(masked - row_max[..., None]), 0.0)
    totals = jnp.sum(weights, axis=2)
    summed = jnp.einsum(
        "gcs,sh->gch", weights.astype(jnp.bfloat16), values, preferred_element_type=jnp.float32
    )
    return (row_max, totals, summed)


def combine_parts(first, second):
    top = jnp.maximum(first[0], second[0])
    scale_one = jnp.exp(first[0] - top)
    scale_two = jnp.exp(second[0] - top)
    totals = first[1] * scale_one + second[1] * scale_two
    summed = first[2] * scale_one[..., None] + second[2] * scale_two[..., None]
    return summed / totals[..., None]


def member_groups(devices, size):
    return [list(range(start, start + size)) for start in range(0, devices, size)]


def group_gather(piece, axis, size):
    spread = jnp.broadcast_to(piece[None], (size,) + piece.shape)
    groups = member_groups(lax.axis_size(axis), size)
    return lax.all_to_all(spread, axis, 0, 0, axis_index_groups=groups, tiled=True)


def group_exchange(parts, axis, size):
    groups = member_groups(lax.axis_size(axis), size)
    return lax.all_to_all(parts, axis, 0, 0, axis_index_groups=groups, tiled=True)


def joined_rows(span_order, shard, spans_here, stored_rows):
    local_order = lax.dynamic_slice_in_dim(span_order, shard * spans_here, spans_here, 0)
    local_order = local_order - shard * spans_here
    blocks = jnp.arange(spans_here, dtype=jnp.int32)
    inverse = jnp.sum(
        jnp.where(local_order[None, :] == blocks[:, None], blocks[None, :], 0), axis=1
    )
    slot = jnp.take(inverse, stored_rows // SPAN)
    return shard * spans_here * SPAN + slot * SPAN + stored_rows % SPAN


def local(
    cache_entries,
    recompute_input,
    norm_gain,
    w_query,
    w_keyval,
    w_out,
    rotate_offsets,
    span_order,
    tenant_of_span,
    recompute_pos,
    recompute_count,
):
    blk_count = lax.axis_size("blk")
    kv_index = lax.axis_index("kv")
    blk_index = lax.axis_index("blk")
    block_rows = cache_entries.shape[0]
    shard_len = block_rows * blk_count
    slots = recompute_input.shape[0]
    own_cols = recompute_input.shape[1]
    width = norm_gain.shape[0]
    spans_here = shard_len // SPAN
    group_size = QH // KVH
    pair_cols = w_keyval.shape[1] // blk_count
    member = blk_index % group_size
    group = blk_index // group_size

    rows_each = block_rows // group_size
    x_part = jnp.broadcast_to(recompute_input[None], (blk_count, slots, own_cols))
    quarter = pair_cols // 2
    key_members = HEAD_DIM // pair_cols
    groups_w = w_keyval.reshape(own_cols, KVH, 2 * HEAD_DIM)
    sorted_w = []
    for m in range(key_members):
        sorted_w.append(groups_w[:, :, m * quarter : (m + 1) * quarter])
        second = HEAD_DIM // 2 + m * quarter
        sorted_w.append(groups_w[:, :, second : second + quarter])
    sorted_w.append(groups_w[:, :, HEAD_DIM:])
    half_rows = own_cols // 2
    parity = kv_index % 2
    w_part = (
        lax.dynamic_slice_in_dim(jnp.concatenate(sorted_w, axis=2), parity * half_rows, half_rows, 0)
        .reshape(half_rows, blk_count, pair_cols)
        .transpose(1, 0, 2)
        .reshape(blk_count, half_rows * pair_cols // HEAD_DIM, HEAD_DIM)
    )
    c_part = (
        cache_entries.reshape(group_size, rows_each, KVH, 2 * HEAD_DIM)
        .transpose(2, 0, 1, 3)
        .reshape(blk_count, rows_each * 2, HEAD_DIM)
    )
    arrived = lax.all_to_all(x_part, "blk", 0, 0, tiled=True)
    wide = arrived.astype(jnp.float32)
    arrived, w_part, c_part = lax.optimization_barrier((arrived, w_part, c_part))
    w_rows = w_part.shape[1]
    moved = lax.all_to_all(jnp.concatenate([w_part, c_part], axis=1), "blk", 0, 0, tiled=True)
    mine = moved[:, :w_rows].reshape(blk_count, half_rows, pair_cols)
    kv_devices = lax.axis_size("kv")
    other = lax.ppermute(mine, "kv", [(i, i ^ 1) for i in range(kv_devices)])
    low_half = jnp.where(parity == 0, mine, other)
    high_half = jnp.where(parity == 0, other, mine)
    kv_cols = jnp.concatenate([low_half, high_half], axis=1)
    stored = moved[:, w_rows:].reshape(blk_count * rows_each, 2 * HEAD_DIM)

    gains = norm_gain.astype(jnp.float32).reshape(blk_count, 1, own_cols)
    scaled = (wide * gains).astype(jnp.bfloat16)
    square_acc = jnp.sum(wide * wide, axis=(0, 2))
    inv_rms = lax.rsqrt(square_acc / width + NORM_EPS)
    query_acc = jnp.einsum(
        "ksc,kcd->sd",
        scaled,
        w_query.reshape(blk_count, own_cols, HEAD_DIM),
        preferred_element_type=jnp.float32,
    ) * inv_rms[:, None]
    pair_piece = jnp.einsum(
        "ksc,kcd->sd", scaled, kv_cols, preferred_element_type=jnp.float32
    ) * inv_rms[:, None]
    own_pos = lax.dynamic_slice_in_dim(recompute_pos, kv_index * slots, slots, 0)
    own_count = lax.dynamic_index_in_dim(recompute_count, kv_index, 0, keepdims=False)
    live = jnp.arange(slots, dtype=jnp.int32) < own_count
    query_pos = kv_index * shard_len + own_pos
    own_query = rotate_half(query_acc.reshape(slots, 1, HEAD_DIM), query_pos)
    own_query = own_query.astype(jnp.bfloat16).reshape(slots, HEAD_DIM)
    inverse = ROPE_BASE ** (
        -(jnp.arange(HEAD_DIM // 2, dtype=jnp.float32) * 2.0 / HEAD_DIM)
    )
    freq = lax.dynamic_slice_in_dim(inverse, (member % key_members) * quarter, quarter, 0)
    angles = query_pos.astype(jnp.float32)[:, None] * freq[None, :]
    cosine = jnp.cos(angles)
    sine = jnp.sin(angles)
    first = pair_piece[:, :quarter]
    second = pair_piece[:, quarter:]
    turned = jnp.concatenate([first * cosine - second * sine, second * cosine + first * sine], axis=1)
    own_piece = jnp.where(member < key_members, turned, pair_piece).astype(jnp.bfloat16)
    shared = group_gather(jnp.concatenate([own_query, own_piece], axis=1), "blk", group_size)
    queries = shared[:, :, :HEAD_DIM].transpose(1, 0, 2)
    pieces = shared[:, :, HEAD_DIM:]
    fresh_keys = jnp.concatenate(
        [pieces[m, :, :quarter] for m in range(key_members)]
        + [pieces[m, :, quarter:] for m in range(key_members)],
        axis=1,
    )
    fresh_values = jnp.concatenate([pieces[m] for m in range(key_members, group_size)], axis=1)

    local_rows = jnp.arange(blk_count * rows_each, dtype=jnp.int32)
    stored_rows = (local_rows // rows_each) * block_rows + member * rows_each + local_rows % rows_each
    key_pos = joined_rows(span_order, kv_index, spans_here, stored_rows)
    offsets = lax.dynamic_slice_in_dim(rotate_offsets, kv_index * spans_here, spans_here, 0)
    row_shifts = jnp.take(offsets, stored_rows // SPAN)
    turned_rows = rotate_half(stored[:, :HEAD_DIM].astype(jnp.float32), row_shifts).astype(
        jnp.bfloat16
    )
    stored = jnp.concatenate([turned_rows, stored[:, HEAD_DIM:]], axis=-1)
    local_order = lax.dynamic_slice_in_dim(span_order, kv_index * spans_here, spans_here, 0)
    slot_rows = (jnp.take(local_order, own_pos // SPAN) - kv_index * spans_here) * SPAN + own_pos % SPAN
    mine = live & ((slot_rows % block_rows) // rows_each == member)
    place = jnp.where(
        mine, (slot_rows // block_rows) * rows_each + slot_rows % rows_each, blk_count * rows_each
    )
    merged = stored.at[place].set(jnp.concatenate([fresh_keys, fresh_values], axis=1), mode="drop")
    query_tenant = tenant_lookup(query_pos, tenant_of_span)
    own_part = attend_part(
        queries,
        query_pos,
        query_tenant,
        merged[:, :HEAD_DIM],
        merged[:, HEAD_DIM:],
        key_pos,
        tenant_lookup(key_pos, tenant_of_span),
    )
    prior = shifted(merged, "kv", 1)
    prior_pos = joined_rows(span_order, jnp.maximum(kv_index - 1, 0), spans_here, stored_rows)
    prior_pos = jnp.where(kv_index > 0, prior_pos, -1)
    prior_part = attend_part(
        queries,
        query_pos,
        query_tenant,
        prior[:, :HEAD_DIM],
        prior[:, HEAD_DIM:],
        prior_pos,
        tenant_lookup(prior_pos, tenant_of_span),
    )
    top = jnp.maximum(own_part[0], prior_part[0])
    scale_own = jnp.exp(own_part[0] - top)
    scale_prior = jnp.exp(prior_part[0] - top)
    totals = own_part[1] * scale_own + prior_part[1] * scale_prior
    summed = own_part[2] * scale_own[..., None] + prior_part[2] * scale_prior[..., None]
    packed = jnp.concatenate([summed, top[..., None], totals[..., None]], axis=-1)
    gathered = group_exchange(packed, "blk", group_size)
    part_max = gathered[:, :, HEAD_DIM]
    part_total = gathered[:, :, HEAD_DIM + 1]
    best = jnp.max(part_max, axis=0)
    weight = jnp.exp(part_max - best[None])
    total = jnp.sum(part_total * weight, axis=0)
    heads_sum = jnp.sum(gathered[:, :, :HEAD_DIM] * weight[..., None], axis=0)
    heads_out = (heads_sum / total[:, None]).astype(jnp.bfloat16)
    term = jnp.einsum(
        "ch,hkd->kcd",
        heads_out,
        w_out.reshape(HEAD_DIM, blk_count, own_cols),
        preferred_element_type=jnp.float32,
    )
    arrived_terms = lax.all_to_all(term.astype(jnp.bfloat16), "blk", 0, 0, tiled=True)
    summed_out = jnp.sum(arrived_terms.astype(jnp.float32), axis=0)
    return jnp.where(live[:, None], summed_out, 0.0).astype(jnp.bfloat16)


def solution(mesh):
    placed = (
        P(("kv", "blk"), None, None),
        P("kv", "blk"),
        P(),
        P(None, "blk"),
        P("blk", None),
        P("blk", None),
        P(),
        P(),
        P(),
        P(),
        P(),
    )
    return jax.shard_map(
        local, mesh=mesh, in_specs=placed, out_specs=P("kv", "blk"), check_vma=False
    )
```

```python
import math

import jax
import jax.numpy as jnp
import numpy as np
from jax import lax
from jax.sharding import PartitionSpec as P

QH = 32
KVH = 8
HEAD_DIM = 128
WINDOW = 4096
SPAN = 1024


NEG_FILL = -1e30
ROPE_BASE = 10000.0
NORM_EPS = 1e-05


def shifted(shard, axis, by):
    devices = lax.axis_size(axis)
    pairs = [(i, i + by) for i in range(devices) if 0 <= i + by < devices]
    return lax.ppermute(shard, axis, pairs)


def rotate_half(values, positions):
    half = values.shape[-1] // 2
    inverse = ROPE_BASE ** (-(jnp.arange(half, dtype=jnp.float32) * 2.0 / values.shape[-1]))
    angles = positions.astype(jnp.float32)[:, None] * inverse[None, :]
    shape = (positions.shape[0],) + (1,) * (values.ndim - 2) + (half,)
    cosine = jnp.cos(angles).reshape(shape)
    sine = jnp.sin(angles).reshape(shape)
    first = values[..., :half]
    second = values[..., half:]
    return jnp.concatenate(
        [first * cosine - second * sine, second * cosine + first * sine], axis=-1
    )


def tenant_lookup(positions, tenant_of_span):
    span_ids = positions // SPAN
    table_index = jnp.arange(tenant_of_span.shape[0], dtype=jnp.int32)
    match = span_ids[:, None] == table_index[None, :]
    return jnp.sum(jnp.where(match, tenant_of_span[None, :], 0), axis=1)


def attend_part(queries, query_pos, query_tenant, keys, values, key_pos, key_tenant):
    scale = 1.0 / math.sqrt(keys.shape[-1])
    scores = jnp.einsum("cgh,sh->gcs", queries, keys, preferred_element_type=jnp.float32) * scale
    gap = query_pos[:, None] - key_pos[None, :]
    allowed = (
        (query_tenant[:, None] == key_tenant[None, :])
        & (gap >= 0)
        & (gap < WINDOW)
        & (key_pos[None, :] >= 0)
    )
    masked = jnp.where(allowed[None], scores, NEG_FILL)
    row_max = jnp.max(masked, axis=2)
    weights = jnp.where(allowed[None], jnp.exp(masked - row_max[..., None]), 0.0)
    totals = jnp.sum(weights, axis=2)
    summed = jnp.einsum(
        "gcs,sh->gch", weights.astype(jnp.bfloat16), values, preferred_element_type=jnp.float32
    )
    return (row_max, totals, summed)


def combine_parts(first, second):
    top = jnp.maximum(first[0], second[0])
    scale_one = jnp.exp(first[0] - top)
    scale_two = jnp.exp(second[0] - top)
    totals = first[1] * scale_one + second[1] * scale_two
    summed = first[2] * scale_one[..., None] + second[2] * scale_two[..., None]
    return summed / totals[..., None]


def split_wide(values):
    high = values.astype(jnp.bfloat16)
    low = (values - high.astype(jnp.float32)).astype(jnp.bfloat16)
    return high, low


def member_groups(devices, size):
    return [list(range(start, start + size)) for start in range(0, devices, size)]


def group_gather(piece, axis, size):
    spread = jnp.broadcast_to(piece[None], (size,) + piece.shape)
    groups = member_groups(lax.axis_size(axis), size)
    return lax.all_to_all(spread, axis, 0, 0, axis_index_groups=groups, tiled=True)


def group_exchange(parts, axis, size):
    groups = member_groups(lax.axis_size(axis), size)
    return lax.all_to_all(parts, axis, 0, 0, axis_index_groups=groups, tiled=True)


def joined_rows(span_order, shard, spans_here, stored_rows):
    local_order = lax.dynamic_slice_in_dim(span_order, shard * spans_here, spans_here, 0)
    local_order = local_order - shard * spans_here
    blocks = jnp.arange(spans_here, dtype=jnp.int32)
    inverse = jnp.sum(
        jnp.where(local_order[None, :] == blocks[:, None], blocks[None, :], 0), axis=1
    )
    slot = jnp.take(inverse, stored_rows // SPAN)
    return shard * spans_here * SPAN + slot * SPAN + stored_rows % SPAN


def local(
    cache_entries,
    recompute_input,
    norm_gain,
    w_query,
    w_keyval,
    w_out,
    rotate_offsets,
    span_order,
    tenant_of_span,
    recompute_pos,
    recompute_count,
):
    blk_count = lax.axis_size("blk")
    kv_index = lax.axis_index("kv")
    blk_index = lax.axis_index("blk")
    block_rows = cache_entries.shape[0]
    shard_len = block_rows * blk_count
    slots = recompute_input.shape[0]
    own_cols = recompute_input.shape[1]
    width = norm_gain.shape[0]
    spans_here = shard_len // SPAN
    group_size = QH // KVH
    pair_cols = w_keyval.shape[1] // blk_count
    member = blk_index % group_size
    group = blk_index // group_size

    rows_each = block_rows // group_size
    x_part = jnp.broadcast_to(recompute_input[None], (blk_count, slots, own_cols))
    quarter = pair_cols // 2
    key_members = HEAD_DIM // pair_cols
    groups_w = w_keyval.reshape(own_cols, KVH, 2 * HEAD_DIM)
    sorted_w = []
    for m in range(key_members):
        sorted_w.append(groups_w[:, :, m * quarter : (m + 1) * quarter])
        second = HEAD_DIM // 2 + m * quarter
        sorted_w.append(groups_w[:, :, second : second + quarter])
    sorted_w.append(groups_w[:, :, HEAD_DIM:])
    w_part = (
        jnp.concatenate(sorted_w, axis=2)
        .reshape(own_cols, blk_count, pair_cols)
        .transpose(1, 0, 2)
        .reshape(blk_count, own_cols * pair_cols // HEAD_DIM, HEAD_DIM)
    )
    c_part = (
        cache_entries.reshape(group_size, rows_each, KVH, 2 * HEAD_DIM)
        .transpose(2, 0, 1, 3)
        .reshape(blk_count, rows_each * 2, HEAD_DIM)
    )
    arrived = lax.all_to_all(x_part, "blk", 0, 0, tiled=True)
    wide = arrived.astype(jnp.float32)
    arrived, w_part, c_part = lax.optimization_barrier((arrived, w_part, c_part))
    w_rows = w_part.shape[1]
    moved = lax.all_to_all(jnp.concatenate([w_part, c_part], axis=1), "blk", 0, 0, tiled=True)
    kv_cols = moved[:, :w_rows].reshape(blk_count, own_cols, pair_cols)
    stored = moved[:, w_rows:].reshape(blk_count * rows_each, 2 * HEAD_DIM)

    gains = norm_gain.astype(jnp.float32).reshape(blk_count, 1, own_cols)
    scaled = (wide * gains).astype(jnp.bfloat16)
    square_acc = jnp.sum(wide * wide, axis=(0, 2))
    inv_rms = lax.rsqrt(square_acc / width + NORM_EPS)
    query_acc = jnp.einsum(
        "ksc,kcd->sd",
        scaled,
        w_query.reshape(blk_count, own_cols, HEAD_DIM),
        preferred_element_type=jnp.float32,
    ) * inv_rms[:, None]
    pair_piece = jnp.einsum(
        "ksc,kcd->sd", scaled, kv_cols, preferred_element_type=jnp.float32
    ) * inv_rms[:, None]
    own_pos = lax.dynamic_slice_in_dim(recompute_pos, kv_index * slots, slots, 0)
    own_count = lax.dynamic_index_in_dim(recompute_count, kv_index, 0, keepdims=False)
    live = jnp.arange(slots, dtype=jnp.int32) < own_count
    query_pos = kv_index * shard_len + own_pos
    own_query = rotate_half(query_acc.reshape(slots, 1, HEAD_DIM), query_pos)
    own_query = own_query.astype(jnp.bfloat16).reshape(slots, HEAD_DIM)
    inverse = ROPE_BASE ** (
        -(jnp.arange(HEAD_DIM // 2, dtype=jnp.float32) * 2.0 / HEAD_DIM)
    )
    freq = lax.dynamic_slice_in_dim(inverse, (member % key_members) * quarter, quarter, 0)
    angles = query_pos.astype(jnp.float32)[:, None] * freq[None, :]
    cosine = jnp.cos(angles)
    sine = jnp.sin(angles)
    first = pair_piece[:, :quarter]
    second = pair_piece[:, quarter:]
    turned = jnp.concatenate([first * cosine - second * sine, second * cosine + first * sine], axis=1)
    own_piece = jnp.where(member < key_members, turned, pair_piece).astype(jnp.bfloat16)
    shared = group_gather(jnp.concatenate([own_query, own_piece], axis=1), "blk", group_size)
    queries = shared[:, :, :HEAD_DIM].transpose(1, 0, 2)
    pieces = shared[:, :, HEAD_DIM:]
    fresh_keys = jnp.concatenate(
        [pieces[m, :, :quarter] for m in range(key_members)]
        + [pieces[m, :, quarter:] for m in range(key_members)],
        axis=1,
    )
    fresh_values = jnp.concatenate([pieces[m] for m in range(key_members, group_size)], axis=1)

    local_rows = jnp.arange(blk_count * rows_each, dtype=jnp.int32)
    stored_rows = (local_rows // rows_each) * block_rows + member * rows_each + local_rows % rows_each
    key_pos = joined_rows(span_order, kv_index, spans_here, stored_rows)
    offsets = lax.dynamic_slice_in_dim(rotate_offsets, kv_index * spans_here, spans_here, 0)
    row_shifts = jnp.take(offsets, stored_rows // SPAN)
    turned_rows = rotate_half(stored[:, :HEAD_DIM].astype(jnp.float32), row_shifts).astype(
        jnp.bfloat16
    )
    stored = jnp.concatenate([turned_rows, stored[:, HEAD_DIM:]], axis=-1)
    local_order = lax.dynamic_slice_in_dim(span_order, kv_index * spans_here, spans_here, 0)
    slot_rows = (jnp.take(local_order, own_pos // SPAN) - kv_index * spans_here) * SPAN + own_pos % SPAN
    mine = live & ((slot_rows % block_rows) // rows_each == member)
    place = jnp.where(
        mine, (slot_rows // block_rows) * rows_each + slot_rows % rows_each, blk_count * rows_each
    )
    merged = stored.at[place].set(jnp.concatenate([fresh_keys, fresh_values], axis=1), mode="drop")
    query_tenant = tenant_lookup(query_pos, tenant_of_span)
    own_part = attend_part(
        queries,
        query_pos,
        query_tenant,
        merged[:, :HEAD_DIM],
        merged[:, HEAD_DIM:],
        key_pos,
        tenant_lookup(key_pos, tenant_of_span),
    )
    prior = shifted(merged, "kv", 1)
    prior_pos = joined_rows(span_order, jnp.maximum(kv_index - 1, 0), spans_here, stored_rows)
    prior_pos = jnp.where(kv_index > 0, prior_pos, -1)
    prior_part = attend_part(
        queries,
        query_pos,
        query_tenant,
        prior[:, :HEAD_DIM],
        prior[:, HEAD_DIM:],
        prior_pos,
        tenant_lookup(prior_pos, tenant_of_span),
    )
    top = jnp.maximum(own_part[0], prior_part[0])
    scale_own = jnp.exp(own_part[0] - top)
    scale_prior = jnp.exp(prior_part[0] - top)
    totals = own_part[1] * scale_own + prior_part[1] * scale_prior
    summed = own_part[2] * scale_own[..., None] + prior_part[2] * scale_prior[..., None]
    top_hi = top.astype(jnp.bfloat16)
    top_mid, top_lo = split_wide(top - top_hi.astype(jnp.float32))
    total_hi, total_lo = split_wide(totals)
    pieces = (top_hi, top_mid, top_lo, total_hi, total_lo)
    packed = jnp.concatenate(
        [summed.astype(jnp.bfloat16)] + [v[..., None] for v in pieces], axis=-1
    )
    gathered = group_exchange(packed, "blk", group_size).astype(jnp.float32)
    part_max = gathered[:, :, HEAD_DIM] + (gathered[:, :, HEAD_DIM + 1] + gathered[:, :, HEAD_DIM + 2])
    part_total = gathered[:, :, HEAD_DIM + 3] + gathered[:, :, HEAD_DIM + 4]
    best = jnp.max(part_max, axis=0)
    weight = jnp.exp(part_max - best[None])
    total = jnp.sum(part_total * weight, axis=0)
    heads_sum = jnp.sum(gathered[:, :, :HEAD_DIM] * weight[..., None], axis=0)
    heads_out = (heads_sum / total[:, None]).astype(jnp.bfloat16)
    term = jnp.einsum(
        "ch,hkd->kcd",
        heads_out,
        w_out.reshape(HEAD_DIM, blk_count, own_cols),
        preferred_element_type=jnp.float32,
    )
    arrived_terms = lax.all_to_all(term.astype(jnp.bfloat16), "blk", 0, 0, tiled=True)
    summed_out = jnp.sum(arrived_terms.astype(jnp.float32), axis=0)
    return jnp.where(live[:, None], summed_out, 0.0).astype(jnp.bfloat16)


def solution(mesh):
    placed = (
        P(("kv", "blk"), None, None),
        P("kv", "blk"),
        P(),
        P(None, "blk"),
        P("blk", None),
        P("blk", None),
        P(),
        P(),
        P(),
        P(),
        P(),
    )
    return jax.shard_map(
        local, mesh=mesh, in_specs=placed, out_specs=P("kv", "blk"), check_vma=False
    )
```

```python
import math

import jax
import jax.numpy as jnp
import numpy as np
from jax import lax
from jax.sharding import PartitionSpec as P

QH = 32
KVH = 8
HEAD_DIM = 128
WINDOW = 4096
SPAN = 1024


NEG_FILL = -1e30
ROPE_BASE = 10000.0
NORM_EPS = 1e-05


def shifted(shard, axis, by):
    devices = lax.axis_size(axis)
    pairs = [(i, i + by) for i in range(devices) if 0 <= i + by < devices]
    return lax.ppermute(shard, axis, pairs)


def rotate_half(values, positions):
    half = values.shape[-1] // 2
    inverse = ROPE_BASE ** (-(jnp.arange(half, dtype=jnp.float32) * 2.0 / values.shape[-1]))
    angles = positions.astype(jnp.float32)[:, None] * inverse[None, :]
    shape = (positions.shape[0],) + (1,) * (values.ndim - 2) + (half,)
    cosine = jnp.cos(angles).reshape(shape)
    sine = jnp.sin(angles).reshape(shape)
    first = values[..., :half]
    second = values[..., half:]
    return jnp.concatenate(
        [first * cosine - second * sine, second * cosine + first * sine], axis=-1
    )


def tenant_lookup(positions, tenant_of_span):
    span_ids = positions // SPAN
    table_index = jnp.arange(tenant_of_span.shape[0], dtype=jnp.int32)
    match = span_ids[:, None] == table_index[None, :]
    return jnp.sum(jnp.where(match, tenant_of_span[None, :], 0), axis=1)


def attend_part(queries, query_pos, query_tenant, keys, values, key_pos, key_tenant):
    scale = 1.0 / math.sqrt(keys.shape[-1])
    scores = jnp.einsum("cgh,sh->gcs", queries, keys, preferred_element_type=jnp.float32) * scale
    gap = query_pos[:, None] - key_pos[None, :]
    allowed = (
        (query_tenant[:, None] == key_tenant[None, :])
        & (gap >= 0)
        & (gap < WINDOW)
        & (key_pos[None, :] >= 0)
    )
    masked = jnp.where(allowed[None], scores, NEG_FILL)
    row_max = jnp.max(masked, axis=2)
    weights = jnp.where(allowed[None], jnp.exp(masked - row_max[..., None]), 0.0)
    totals = jnp.sum(weights, axis=2)
    summed = jnp.einsum(
        "gcs,sh->gch", weights.astype(jnp.bfloat16), values, preferred_element_type=jnp.float32
    )
    return (row_max, totals, summed)


def combine_parts(first, second):
    top = jnp.maximum(first[0], second[0])
    scale_one = jnp.exp(first[0] - top)
    scale_two = jnp.exp(second[0] - top)
    totals = first[1] * scale_one + second[1] * scale_two
    summed = first[2] * scale_one[..., None] + second[2] * scale_two[..., None]
    return summed / totals[..., None]


def member_groups(devices, size):
    return [list(range(start, start + size)) for start in range(0, devices, size)]


def group_gather(piece, axis, size):
    spread = jnp.broadcast_to(piece[None], (size,) + piece.shape)
    groups = member_groups(lax.axis_size(axis), size)
    return lax.all_to_all(spread, axis, 0, 0, axis_index_groups=groups, tiled=True)


def group_exchange(parts, axis, size):
    groups = member_groups(lax.axis_size(axis), size)
    return lax.all_to_all(parts, axis, 0, 0, axis_index_groups=groups, tiled=True)


def joined_rows(span_order, shard, spans_here, stored_rows):
    local_order = lax.dynamic_slice_in_dim(span_order, shard * spans_here, spans_here, 0)
    local_order = local_order - shard * spans_here
    blocks = jnp.arange(spans_here, dtype=jnp.int32)
    inverse = jnp.sum(
        jnp.where(local_order[None, :] == blocks[:, None], blocks[None, :], 0), axis=1
    )
    slot = jnp.take(inverse, stored_rows // SPAN)
    return shard * spans_here * SPAN + slot * SPAN + stored_rows % SPAN


def local(
    cache_entries,
    recompute_input,
    norm_gain,
    w_query,
    w_keyval,
    w_out,
    rotate_offsets,
    span_order,
    tenant_of_span,
    recompute_pos,
    recompute_count,
):
    blk_count = lax.axis_size("blk")
    kv_index = lax.axis_index("kv")
    blk_index = lax.axis_index("blk")
    block_rows = cache_entries.shape[0]
    shard_len = block_rows * blk_count
    slots = recompute_input.shape[0]
    own_cols = recompute_input.shape[1]
    width = norm_gain.shape[0]
    spans_here = shard_len // SPAN
    group_size = QH // KVH
    pair_cols = w_keyval.shape[1] // blk_count
    member = blk_index % group_size
    group = blk_index // group_size

    rows_each = block_rows // group_size
    x_part = jnp.broadcast_to(recompute_input[None], (blk_count, slots, own_cols))
    quarter = pair_cols // 2
    key_members = HEAD_DIM // pair_cols
    groups_w = w_keyval.reshape(own_cols, KVH, 2 * HEAD_DIM)
    sorted_w = []
    for m in range(key_members):
        sorted_w.append(groups_w[:, :, m * quarter : (m + 1) * quarter])
        second = HEAD_DIM // 2 + m * quarter
        sorted_w.append(groups_w[:, :, second : second + quarter])
    sorted_w.append(groups_w[:, :, HEAD_DIM:])
    w_part = (
        jnp.concatenate(sorted_w, axis=2)
        .reshape(own_cols, blk_count, pair_cols)
        .transpose(1, 0, 2)
        .reshape(blk_count, own_cols * pair_cols // HEAD_DIM, HEAD_DIM)
    )
    c_part = (
        cache_entries.reshape(group_size, rows_each, KVH, 2 * HEAD_DIM)
        .transpose(2, 0, 1, 3)
        .reshape(blk_count, rows_each * 2, HEAD_DIM)
    )
    arrived = lax.all_to_all(x_part, "blk", 0, 0, tiled=True)
    wide = arrived.astype(jnp.float32)
    arrived, w_part, c_part = lax.optimization_barrier((arrived, w_part, c_part))
    w_rows = w_part.shape[1]
    moved = lax.all_to_all(jnp.concatenate([w_part, c_part], axis=1), "blk", 0, 0, tiled=True)
    kv_cols = moved[:, :w_rows].reshape(blk_count, own_cols, pair_cols)
    stored = moved[:, w_rows:].reshape(blk_count * rows_each, 2 * HEAD_DIM)

    gains = norm_gain.astype(jnp.float32).reshape(blk_count, 1, own_cols)
    scaled = (wide * gains).astype(jnp.bfloat16)
    square_acc = jnp.sum(wide * wide, axis=(0, 2))
    inv_rms = lax.rsqrt(square_acc / width + NORM_EPS)
    query_acc = jnp.einsum(
        "ksc,kcd->sd",
        scaled,
        w_query.reshape(blk_count, own_cols, HEAD_DIM),
        preferred_element_type=jnp.float32,
    ) * inv_rms[:, None]
    pair_piece = jnp.einsum(
        "ksc,kcd->sd", scaled, kv_cols, preferred_element_type=jnp.float32
    ) * inv_rms[:, None]
    own_pos = lax.dynamic_slice_in_dim(recompute_pos, kv_index * slots, slots, 0)
    own_count = lax.dynamic_index_in_dim(recompute_count, kv_index, 0, keepdims=False)
    live = jnp.arange(slots, dtype=jnp.int32) < own_count
    query_pos = kv_index * shard_len + own_pos
    own_query = rotate_half(query_acc.reshape(slots, 1, HEAD_DIM), query_pos)
    own_query = own_query.astype(jnp.bfloat16).reshape(slots, HEAD_DIM)
    inverse = ROPE_BASE ** (
        -(jnp.arange(HEAD_DIM // 2, dtype=jnp.float32) * 2.0 / HEAD_DIM)
    )
    freq = lax.dynamic_slice_in_dim(inverse, (member % key_members) * quarter, quarter, 0)
    angles = query_pos.astype(jnp.float32)[:, None] * freq[None, :]
    cosine = jnp.cos(angles)
    sine = jnp.sin(angles)
    first = pair_piece[:, :quarter]
    second = pair_piece[:, quarter:]
    turned = jnp.concatenate([first * cosine - second * sine, second * cosine + first * sine], axis=1)
    own_piece = jnp.where(member < key_members, turned, pair_piece).astype(jnp.bfloat16)
    piece_rows = slots * pair_cols // HEAD_DIM
    outgoing = jnp.concatenate([own_query, own_piece.reshape(piece_rows, HEAD_DIM)], axis=0)
    shared = group_gather(outgoing, "blk", group_size)
    queries = shared[:, :slots].transpose(1, 0, 2)
    pieces = shared[:, slots:].reshape(group_size, slots, pair_cols)
    fresh_keys = jnp.concatenate(
        [pieces[m, :, :quarter] for m in range(key_members)]
        + [pieces[m, :, quarter:] for m in range(key_members)],
        axis=1,
    )
    fresh_values = jnp.concatenate([pieces[m] for m in range(key_members, group_size)], axis=1)

    local_rows = jnp.arange(blk_count * rows_each, dtype=jnp.int32)
    stored_rows = (local_rows // rows_each) * block_rows + member * rows_each + local_rows % rows_each
    key_pos = joined_rows(span_order, kv_index, spans_here, stored_rows)
    offsets = lax.dynamic_slice_in_dim(rotate_offsets, kv_index * spans_here, spans_here, 0)
    row_shifts = jnp.take(offsets, stored_rows // SPAN)
    turned_rows = rotate_half(stored[:, :HEAD_DIM].astype(jnp.float32), row_shifts).astype(
        jnp.bfloat16
    )
    stored = jnp.concatenate([turned_rows, stored[:, HEAD_DIM:]], axis=-1)
    local_order = lax.dynamic_slice_in_dim(span_order, kv_index * spans_here, spans_here, 0)
    slot_rows = (jnp.take(local_order, own_pos // SPAN) - kv_index * spans_here) * SPAN + own_pos % SPAN
    mine = live & ((slot_rows % block_rows) // rows_each == member)
    place = jnp.where(
        mine, (slot_rows // block_rows) * rows_each + slot_rows % rows_each, blk_count * rows_each
    )
    merged = stored.at[place].set(jnp.concatenate([fresh_keys, fresh_values], axis=1), mode="drop")
    query_tenant = tenant_lookup(query_pos, tenant_of_span)
    own_part = attend_part(
        queries,
        query_pos,
        query_tenant,
        merged[:, :HEAD_DIM],
        merged[:, HEAD_DIM:],
        key_pos,
        tenant_lookup(key_pos, tenant_of_span),
    )
    prior = shifted(merged, "kv", 1)
    prior_pos = joined_rows(span_order, jnp.maximum(kv_index - 1, 0), spans_here, stored_rows)
    prior_pos = jnp.where(kv_index > 0, prior_pos, -1)
    prior_part = attend_part(
        queries,
        query_pos,
        query_tenant,
        prior[:, :HEAD_DIM],
        prior[:, HEAD_DIM:],
        prior_pos,
        tenant_lookup(prior_pos, tenant_of_span),
    )
    top = jnp.maximum(own_part[0], prior_part[0])
    scale_own = jnp.exp(own_part[0] - top)
    scale_prior = jnp.exp(prior_part[0] - top)
    totals = own_part[1] * scale_own + prior_part[1] * scale_prior
    summed = own_part[2] * scale_own[..., None] + prior_part[2] * scale_prior[..., None]
    stat_rows = slots // HEAD_DIM
    packed = jnp.concatenate(
        [
            summed,
            top.reshape(group_size, stat_rows, HEAD_DIM),
            totals.reshape(group_size, stat_rows, HEAD_DIM),
        ],
        axis=1,
    )
    gathered = group_exchange(packed, "blk", group_size)
    part_max = gathered[:, slots : slots + stat_rows].reshape(group_size, slots)
    part_total = gathered[:, slots + stat_rows :].reshape(group_size, slots)
    best = jnp.max(part_max, axis=0)
    weight = jnp.exp(part_max - best[None])
    total = jnp.sum(part_total * weight, axis=0)
    heads_sum = jnp.sum(gathered[:, :slots] * weight[..., None], axis=0)
    heads_out = (heads_sum / total[:, None]).astype(jnp.bfloat16)
    term = jnp.einsum(
        "ch,hkd->kcd",
        heads_out,
        w_out.reshape(HEAD_DIM, blk_count, own_cols),
        preferred_element_type=jnp.float32,
    )
    arrived_terms = lax.all_to_all(term.astype(jnp.bfloat16), "blk", 0, 0, tiled=True)
    summed_out = jnp.sum(arrived_terms.astype(jnp.float32), axis=0)
    return jnp.where(live[:, None], summed_out, 0.0).astype(jnp.bfloat16)


def solution(mesh):
    placed = (
        P(("kv", "blk"), None, None),
        P("kv", "blk"),
        P(),
        P(None, "blk"),
        P("blk", None),
        P("blk", None),
        P(),
        P(),
        P(),
        P(),
        P(),
    )
    return jax.shard_map(
        local, mesh=mesh, in_specs=placed, out_specs=P("kv", "blk"), check_vma=False
    )
```

```python
import math

import jax
import jax.numpy as jnp
import numpy as np
from jax import lax
from jax.sharding import PartitionSpec as P

QH = 32
KVH = 8
HEAD_DIM = 128
WINDOW = 4096
SPAN = 1024


NEG_FILL = -1e30
ROPE_BASE = 10000.0
NORM_EPS = 1e-05


def shifted(shard, axis, by):
    devices = lax.axis_size(axis)
    pairs = [(i, i + by) for i in range(devices) if 0 <= i + by < devices]
    return lax.ppermute(shard, axis, pairs)


def rotate_half(values, positions):
    half = values.shape[-1] // 2
    inverse = ROPE_BASE ** (-(jnp.arange(half, dtype=jnp.float32) * 2.0 / values.shape[-1]))
    angles = positions.astype(jnp.float32)[:, None] * inverse[None, :]
    shape = (positions.shape[0],) + (1,) * (values.ndim - 2) + (half,)
    cosine = jnp.cos(angles).reshape(shape)
    sine = jnp.sin(angles).reshape(shape)
    first = values[..., :half]
    second = values[..., half:]
    return jnp.concatenate(
        [first * cosine - second * sine, second * cosine + first * sine], axis=-1
    )


def tenant_lookup(positions, tenant_of_span):
    span_ids = positions // SPAN
    table_index = jnp.arange(tenant_of_span.shape[0], dtype=jnp.int32)
    match = span_ids[:, None] == table_index[None, :]
    return jnp.sum(jnp.where(match, tenant_of_span[None, :], 0), axis=1)


def attend_part(queries, query_pos, query_tenant, keys, values, key_pos, key_tenant):
    scale = 1.0 / math.sqrt(keys.shape[-1])
    scores = jnp.einsum("cgh,sh->gcs", queries, keys, preferred_element_type=jnp.float32) * scale
    gap = query_pos[:, None] - key_pos[None, :]
    allowed = (
        (query_tenant[:, None] == key_tenant[None, :])
        & (gap >= 0)
        & (gap < WINDOW)
        & (key_pos[None, :] >= 0)
    )
    masked = jnp.where(allowed[None], scores, NEG_FILL)
    row_max = jnp.max(masked, axis=2)
    weights = jnp.where(allowed[None], jnp.exp(masked - row_max[..., None]), 0.0)
    totals = jnp.sum(weights, axis=2)
    summed = jnp.einsum(
        "gcs,sh->gch", weights.astype(jnp.bfloat16), values, preferred_element_type=jnp.float32
    )
    return (row_max, totals, summed)


def combine_parts(first, second):
    top = jnp.maximum(first[0], second[0])
    scale_one = jnp.exp(first[0] - top)
    scale_two = jnp.exp(second[0] - top)
    totals = first[1] * scale_one + second[1] * scale_two
    summed = first[2] * scale_one[..., None] + second[2] * scale_two[..., None]
    return summed / totals[..., None]


def member_groups(devices, size):
    return [list(range(start, start + size)) for start in range(0, devices, size)]


def group_gather(piece, axis, size):
    spread = jnp.broadcast_to(piece[None], (size,) + piece.shape)
    groups = member_groups(lax.axis_size(axis), size)
    return lax.all_to_all(spread, axis, 0, 0, axis_index_groups=groups, tiled=True)


def group_exchange(parts, axis, size):
    groups = member_groups(lax.axis_size(axis), size)
    return lax.all_to_all(parts, axis, 0, 0, axis_index_groups=groups, tiled=True)


def joined_rows(span_order, shard, spans_here, stored_rows):
    local_order = lax.dynamic_slice_in_dim(span_order, shard * spans_here, spans_here, 0)
    local_order = local_order - shard * spans_here
    blocks = jnp.arange(spans_here, dtype=jnp.int32)
    inverse = jnp.sum(
        jnp.where(local_order[None, :] == blocks[:, None], blocks[None, :], 0), axis=1
    )
    slot = jnp.take(inverse, stored_rows // SPAN)
    return shard * spans_here * SPAN + slot * SPAN + stored_rows % SPAN


def local(
    cache_entries,
    recompute_input,
    norm_gain,
    w_query,
    w_keyval,
    w_out,
    rotate_offsets,
    span_order,
    tenant_of_span,
    recompute_pos,
    recompute_count,
):
    blk_count = lax.axis_size("blk")
    kv_index = lax.axis_index("kv")
    blk_index = lax.axis_index("blk")
    block_rows = cache_entries.shape[0]
    shard_len = block_rows * blk_count
    slots = recompute_input.shape[0]
    own_cols = recompute_input.shape[1]
    width = norm_gain.shape[0]
    spans_here = shard_len // SPAN
    group_size = QH // KVH
    pair_cols = w_keyval.shape[1] // blk_count
    member = blk_index % group_size
    group = blk_index // group_size

    rows_each = block_rows // group_size
    x_part = jnp.broadcast_to(recompute_input[None], (blk_count, slots, own_cols))
    quarter = pair_cols // 2
    key_members = HEAD_DIM // pair_cols
    groups_w = w_keyval.reshape(own_cols, KVH, 2 * HEAD_DIM)
    sorted_w = []
    for m in range(key_members):
        sorted_w.append(groups_w[:, :, m * quarter : (m + 1) * quarter])
        second = HEAD_DIM // 2 + m * quarter
        sorted_w.append(groups_w[:, :, second : second + quarter])
    sorted_w.append(groups_w[:, :, HEAD_DIM:])
    w_part = (
        jnp.concatenate(sorted_w, axis=2)
        .reshape(own_cols, blk_count, pair_cols)
        .transpose(1, 0, 2)
        .reshape(blk_count, own_cols * pair_cols // HEAD_DIM, HEAD_DIM)
    )
    c_part = (
        cache_entries.reshape(group_size, rows_each, KVH, 2 * HEAD_DIM)
        .transpose(2, 0, 1, 3)
        .reshape(blk_count, rows_each * 2, HEAD_DIM)
    )
    arrived = lax.all_to_all(x_part, "blk", 0, 0, tiled=True)
    wide = arrived.astype(jnp.float32)
    arrived, w_part, c_part = lax.optimization_barrier((arrived, w_part, c_part))
    w_rows = w_part.shape[1]
    moved = lax.all_to_all(jnp.concatenate([w_part, c_part], axis=1), "blk", 0, 0, tiled=True)
    kv_cols = moved[:, :w_rows].reshape(blk_count, own_cols, pair_cols)
    stored = moved[:, w_rows:].reshape(blk_count * rows_each, 2 * HEAD_DIM)

    gains = norm_gain.astype(jnp.float32).reshape(blk_count, 1, own_cols)
    scaled = (wide * gains).astype(jnp.bfloat16)
    square_acc = jnp.sum(wide * wide, axis=(0, 2))
    inv_rms = lax.rsqrt(square_acc / width + NORM_EPS)
    query_acc = jnp.einsum(
        "ksc,kcd->sd",
        scaled,
        w_query.reshape(blk_count, own_cols, HEAD_DIM),
        preferred_element_type=jnp.float32,
    ) * inv_rms[:, None]
    pair_piece = jnp.einsum(
        "ksc,kcd->sd", scaled, kv_cols, preferred_element_type=jnp.float32
    ) * inv_rms[:, None]
    own_pos = lax.dynamic_slice_in_dim(recompute_pos, kv_index * slots, slots, 0)
    own_count = lax.dynamic_index_in_dim(recompute_count, kv_index, 0, keepdims=False)
    live = jnp.arange(slots, dtype=jnp.int32) < own_count
    query_pos = kv_index * shard_len + own_pos
    own_query = rotate_half(query_acc.reshape(slots, 1, HEAD_DIM), query_pos)
    own_query = own_query.astype(jnp.bfloat16).reshape(slots, HEAD_DIM)
    inverse = ROPE_BASE ** (
        -(jnp.arange(HEAD_DIM // 2, dtype=jnp.float32) * 2.0 / HEAD_DIM)
    )
    freq = lax.dynamic_slice_in_dim(inverse, (member % key_members) * quarter, quarter, 0)
    angles = query_pos.astype(jnp.float32)[:, None] * freq[None, :]
    cosine = jnp.cos(angles)
    sine = jnp.sin(angles)
    first = pair_piece[:, :quarter]
    second = pair_piece[:, quarter:]
    turned = jnp.concatenate([first * cosine - second * sine, second * cosine + first * sine], axis=1)
    own_piece = jnp.where(member < key_members, turned, pair_piece).astype(jnp.bfloat16)
    shared = group_gather(jnp.concatenate([own_query, own_piece], axis=1), "blk", group_size)
    queries = shared[:, :, :HEAD_DIM].transpose(1, 0, 2)
    pieces = shared[:, :, HEAD_DIM:]
    fresh_keys = jnp.concatenate(
        [pieces[m, :, :quarter] for m in range(key_members)]
        + [pieces[m, :, quarter:] for m in range(key_members)],
        axis=1,
    )
    fresh_values = jnp.concatenate([pieces[m] for m in range(key_members, group_size)], axis=1)

    local_rows = jnp.arange(blk_count * rows_each, dtype=jnp.int32)
    stored_rows = (local_rows // rows_each) * block_rows + member * rows_each + local_rows % rows_each
    key_pos = joined_rows(span_order, kv_index, spans_here, stored_rows)
    offsets = lax.dynamic_slice_in_dim(rotate_offsets, kv_index * spans_here, spans_here, 0)
    row_shifts = jnp.take(offsets, stored_rows // SPAN)
    turned_rows = rotate_half(stored[:, :HEAD_DIM].astype(jnp.float32), row_shifts).astype(
        jnp.bfloat16
    )
    stored = jnp.concatenate([turned_rows, stored[:, HEAD_DIM:]], axis=-1)
    local_order = lax.dynamic_slice_in_dim(span_order, kv_index * spans_here, spans_here, 0)
    slot_rows = (jnp.take(local_order, own_pos // SPAN) - kv_index * spans_here) * SPAN + own_pos % SPAN
    mine = live & ((slot_rows % block_rows) // rows_each == member)
    place = jnp.where(
        mine, (slot_rows // block_rows) * rows_each + slot_rows % rows_each, blk_count * rows_each
    )
    merged = stored.at[place].set(jnp.concatenate([fresh_keys, fresh_values], axis=1), mode="drop")
    query_tenant = tenant_lookup(query_pos, tenant_of_span)
    own_part = attend_part(
        queries,
        query_pos,
        query_tenant,
        merged[:, :HEAD_DIM],
        merged[:, HEAD_DIM:],
        key_pos,
        tenant_lookup(key_pos, tenant_of_span),
    )
    prior = shifted(merged, "kv", 1)
    prior_pos = joined_rows(span_order, jnp.maximum(kv_index - 1, 0), spans_here, stored_rows)
    prior_pos = jnp.where(kv_index > 0, prior_pos, -1)
    prior_part = attend_part(
        queries,
        query_pos,
        query_tenant,
        prior[:, :HEAD_DIM],
        prior[:, HEAD_DIM:],
        prior_pos,
        tenant_lookup(prior_pos, tenant_of_span),
    )
    top = jnp.maximum(own_part[0], prior_part[0])
    scale_own = jnp.exp(own_part[0] - top)
    scale_prior = jnp.exp(prior_part[0] - top)
    totals = own_part[1] * scale_own + prior_part[1] * scale_prior
    summed = own_part[2] * scale_own[..., None] + prior_part[2] * scale_prior[..., None]
    stat_rows = slots // HEAD_DIM
    packed = jnp.concatenate(
        [
            summed,
            top.reshape(group_size, stat_rows, HEAD_DIM),
            totals.reshape(group_size, stat_rows, HEAD_DIM),
        ],
        axis=1,
    )
    gathered = group_exchange(packed, "blk", group_size)
    part_max = gathered[:, slots : slots + stat_rows].reshape(group_size, slots)
    part_total = gathered[:, slots + stat_rows :].reshape(group_size, slots)
    best = jnp.max(part_max, axis=0)
    weight = jnp.exp(part_max - best[None])
    total = jnp.sum(part_total * weight, axis=0)
    heads_sum = jnp.sum(gathered[:, :slots] * weight[..., None], axis=0)
    heads_out = (heads_sum / total[:, None]).astype(jnp.bfloat16)
    term = jnp.einsum(
        "ch,hkd->kcd",
        heads_out,
        w_out.reshape(HEAD_DIM, blk_count, own_cols),
        preferred_element_type=jnp.float32,
    )
    arrived_terms = lax.all_to_all(term.astype(jnp.bfloat16), "blk", 0, 0, tiled=True)
    summed_out = jnp.sum(arrived_terms.astype(jnp.float32), axis=0)
    return jnp.where(live[:, None], summed_out, 0.0).astype(jnp.bfloat16)


def solution(mesh):
    placed = (
        P(("kv", "blk"), None, None),
        P("kv", "blk"),
        P(),
        P(None, "blk"),
        P("blk", None),
        P("blk", None),
        P(),
        P(),
        P(),
        P(),
        P(),
    )
    return jax.shard_map(
        local, mesh=mesh, in_specs=placed, out_specs=P("kv", "blk"), check_vma=False
    )
```
